32 devices in a mesh: day: 4 (over z), dom: 8 (over y, x, core).
Axes of the slice: x: 2, y: 2, z: 4, core: 2. Of those that a mesh axis runs over, the one named last changes fastest.
Arguments:
- node_states: bfloat16 [16, 2048, 256], P('day', 'dom'), may hold values from -12 to 12
- edge_source: int32 [16, 8192], P('day', 'dom'), may hold values from 0 to 383
- edge_target: int32 [16, 8192], P('day', 'dom'), may hold values from 0 to 255
- halo_rows: int32 [16, 1024], P('day', 'dom'), may hold values from 0 to 255
- halo_count: int32 [16, 8], P('day', 'dom'), may hold values from 1 to 128, 640 in all within a row
- w_message: bfloat16 [256, 256], replicated, may hold values from -0.375 to 0.375
- w_query: bfloat16 [256, 256], replicated, may hold values from -1 to 1, as said below
- w_key: bfloat16 [256, 256], replicated, may hold values from -1 to 1, as said below
- w_value: bfloat16 [256, 256], replicated, may hold values from -0.375 to 0.375
- cotangent: bfloat16 [16, 8, 4, 64, 256], P(None, 'dom', 'day'), may hold values from -6 to 6
Outputs:
- state_grad: float32 [16, 2048, 256], P('day', 'dom')
- grad_message: float32 [256, 256], replicated
- grad_query: float32 [256, 256], replicated
- grad_key: float32 [256, 256], replicated
- grad_value: float32 [256, 256], replicated
The draws below stay inside these ranges and needn't reach their ends.
Inputs may be any that keep to these rules, and one draw needn't show every extreme that they name: `edge_source`: indices of the extended rows: below 256 a partition's own account, from 256 on a received halo slot. `halo_rows`: rows of the sending partition's own block; repeats allowed. `halo_count`: on every day some partition has all 128 slots live. `w_query`: entries of order 256 ** -0.5. `w_key`: entries of order 256 ** -0.5.
All inputs are finite; a program needn't handle non-finite values. No bound on the sum of `halo_count` on one device may be relied on, other than what follows from the above.
Results may differ from the reference program's by a relative error of at most 0.004.
The reference program's roundings to bfloat16 on the way count: a program that leaves them out, or rounds other values in their place, can miss the bound.
Values may be sent and summed in bfloat16 or wider, within the bound.
No kernel may reach another device: no remote copies, remote signals or barrier semaphores. Data moves between devices by JAX's collectives and lax.ppermute only.
A program may use at most 64 MiB of HBM per device.

```python
import math
import jax
import jax.numpy as jnp
import numpy as np
from jax import lax

H = 256
HEADS = 4
HALO = 128
NODE_DEV = 256
DAYS = 16
GROUPS = 8
QUARTERS = 4
NQ = 64
NODES = 2048
EDGE_DEV = 1024


def draw_node_states(key, part):
    first = jax.random.fold_in(key, 101)
    result = jnp.clip(jax.random.normal(first, (DAYS, NODES, H), jnp.float32), -6.0, 6.0)
    return result.astype(jnp.bfloat16)


def weight_pair(key):
    scale_value = H ** (-0.5)
    first = jnp.clip(jax.random.normal(jax.random.fold_in(key, 201), (H, H), jnp.float32), -4.0, 4.0) * scale_value
    second = jnp.clip(jax.random.normal(jax.random.fold_in(key, 202), (H, H), jnp.float32), -4.0, 4.0) * scale_value
    return (first, second)


def draw_w_query(key, part):
    return weight_pair(key)[0].astype(jnp.bfloat16)


def draw_w_key(key, part):
    return weight_pair(key)[1].astype(jnp.bfloat16)


def with_ends(values, stream_key, low, largest):
    shape = values.shape
    index_at = [jax.random.randint(jax.random.fold_in(stream_key, axis), (), 0, shape[axis]) for axis in range(len(shape))]
    values = values.at[tuple(index_at)].set(low)
    longest = shape.index(max(shape))
    index_at[longest] = (index_at[longest] + 1) % shape[longest]
    return values.at[tuple(index_at)].set(largest)


def level_of(rng, extent, shards, least, largest):
    factor_of, own = 1.0, jax.random.fold_in(rng, 6)
    for axis_at, blocks in shards:
        steps = jnp.exp(jax.random.uniform(jax.random.fold_in(own, axis_at), (blocks,), jnp.float32, least / len(shards), largest / len(shards)))
        factor_of = factor_of * jnp.repeat(steps, extent[axis_at] // blocks).reshape([-1 if axis == axis_at else 1 for axis in range(len(extent))])
    return factor_of


def profile(amount, total, bound, lean):
    loads = [(1 << 20) // math.isqrt(rank ** lean) + 1 for rank in range(2, amount + 1)]
    rest, holding = total - bound - (amount - 1), [1] * (amount - 1)
    while rest > 0:
        free = [i for i in range(amount - 1) if holding[i] < bound]
        whole, remaining = sum([loads[i] for i in free]), rest
        for i in free:
            addition = min(bound - holding[i], max(1, remaining * loads[i] // whole), rest)
            holding[i] = holding[i] + addition
            rest = rest - addition
    return np.array([bound] + holding)


def ragged(own_key, amount, total, limit, slope):
    if amount == 2:
        one = jax.random.randint(own_key, (), max(1, total - limit), min(limit, total - 1) + 1)
        return jnp.stack([one, total - one])
    lengths = jnp.asarray(profile(amount, total, limit, slope), jnp.int32)
    twos = (amount - 1) // 2
    giver, receiver = lengths[1:1 + 2 * twos:2], lengths[2:2 + 2 * twos:2]
    slack = jnp.minimum(giver - 1, limit - receiver)
    moved = jax.random.randint(jax.random.fold_in(own_key, 1), (twos,), 0, 1 << 20) % (slack + 1)
    lengths = lengths.at[1:1 + 2 * twos:2].set(giver - moved).at[2:2 + 2 * twos:2].set(receiver + moved)
    return lengths[jax.random.permutation(jax.random.fold_in(own_key, 2), amount)]


def bell_draw(own_key, extent, spread, most, cuts=(), kind=jnp.bfloat16):
    level = level_of(own_key, extent, cuts, -0.22, 0.18) if cuts else 1.0
    array = jax.random.normal(own_key, extent, jnp.float32) * spread * level
    return jnp.minimum(jnp.maximum(array, -most), most).astype(kind)


def setup_inputs(seed: int = 0) -> dict:
    seeds = jax.random.split(jax.random.key(seed), 11)
    return {
        "node_states": draw_node_states(jax.random.fold_in(seeds[10], 71), 0),
        "edge_source": with_ends(jax.random.randint(seeds[1], (DAYS, GROUPS * EDGE_DEV), 0, NODE_DEV + HALO), jax.random.fold_in(seeds[1], 1), 0, (NODE_DEV + HALO) - 1).astype(jnp.int32),
        "edge_target": with_ends(jax.random.randint(seeds[2], (DAYS, GROUPS * EDGE_DEV), 0, NODE_DEV), jax.random.fold_in(seeds[2], 1), 0, NODE_DEV - 1).astype(jnp.int32),
        "halo_rows": with_ends(jax.random.randint(seeds[3], (DAYS, GROUPS * HALO), 0, NODE_DEV), jax.random.fold_in(seeds[3], 1), 0, NODE_DEV - 1).astype(jnp.int32),
        "halo_count": jax.vmap(lambda own: ragged(own, GROUPS, GROUPS * HALO * 5 // 8, HALO, 2))(jax.random.split(seeds[4], DAYS)).reshape((DAYS, GROUPS)).astype(jnp.int32),
        "w_message": bell_draw(seeds[5], (H, H), H ** -0.5, 0.375),
        "w_query": draw_w_query(jax.random.fold_in(seeds[10], 71), 0),
        "w_key": draw_w_key(jax.random.fold_in(seeds[10], 71), 0),
        "w_value": bell_draw(seeds[8], (H, H), H ** -0.5, 0.375),
        "cotangent": bell_draw(seeds[9], (DAYS, GROUPS, QUARTERS, NQ, H), 1.0, 6.0, ((1, 8), (2, 4))),
    }


def gnn_forward(states, received, sources, targets, w_message):
    count_rows = states.shape[0]
    extended = jnp.concatenate([states, received], axis=0)
    neighbours = jax.ops.segment_sum(jnp.take(extended, sources, axis=0).astype(jnp.float32), targets, num_segments=count_rows)
    counted = jax.ops.segment_sum(jnp.ones(targets.shape, jnp.float32), targets, num_segments=count_rows)
    inverse = 1.0 / (counted + 1.0)
    aggregate = ((states.astype(jnp.float32) + neighbours) * inverse[:, None]).astype(jnp.bfloat16)
    preact = jnp.dot(aggregate, w_message, preferred_element_type=jnp.float32)
    hidden = (states.astype(jnp.float32) + jax.nn.silu(preact)).astype(jnp.bfloat16)
    return (aggregate, preact, inverse, hidden)

def gnn_backward(upstream, aggregate, preact, inverse, sources, targets, w_message, halo_slots):
    count_rows = aggregate.shape[0]
    up_float = upstream.astype(jnp.float32)
    sigmoid_val = jax.nn.sigmoid(preact)
    pre_grad = (up_float * sigmoid_val * (1.0 + preact * (1.0 - sigmoid_val))).astype(jnp.bfloat16)
    message_part = lax.dot_general(aggregate, pre_grad, (((0,), (0,)), ((), ())), preferred_element_type=jnp.float32)
    agg_grad = lax.dot_general(pre_grad, w_message, (((1,), (1,)), ((), ())), preferred_element_type=jnp.float32)
    term_grad = agg_grad * inverse[:, None]
    ext_grad = jax.ops.segment_sum(jnp.take(term_grad, targets, axis=0), sources, num_segments=count_rows + halo_slots)
    local_grad = up_float + term_grad + ext_grad[:count_rows]
    halo_grad = ext_grad[count_rows:].astype(jnp.bfloat16)
    return (message_part, local_grad, halo_grad)

def attend(states, upstream, w_query, w_key, w_value):
    steps_all, nodes_here, width = states.shape
    head_dim = width // HEADS
    scale_factor = head_dim ** (-0.5)
    flat = states.reshape(steps_all * nodes_here, width)

    def project(weight):
        return jnp.dot(flat, weight, preferred_element_type=jnp.float32).astype(jnp.bfloat16)

    def splitter(matrix):
        return matrix.reshape(steps_all, nodes_here, HEADS, head_dim).astype(jnp.float32)
    queries = project(w_query)
    key_rows = project(w_key)
    value_rows = project(w_value)
    query_f = splitter(queries)
    key_f = splitter(key_rows)
    value_f = splitter(value_rows)
    scores = jnp.einsum('tnhd,snhd->nhts', query_f, key_f) * scale_factor
    causal = jnp.arange(steps_all)[:, None] >= jnp.arange(steps_all)[None, :]
    scores = jnp.where(causal, scores, -jnp.inf)
    highest = lax.optimization_barrier(jnp.max(scores, axis=-1, keepdims=True))
    exponent = jnp.exp(scores - highest)
    probs = exponent / lax.optimization_barrier(jnp.sum(exponent, axis=-1, keepdims=True))
    probs_low = probs.astype(jnp.bfloat16).astype(jnp.float32)
    up_heads = splitter(upstream)
    value_grad = jnp.einsum('nhts,tnhd->snhd', probs_low, up_heads).astype(jnp.bfloat16)
    prob_grad = jnp.einsum('tnhd,snhd->nhts', up_heads, value_f)
    score_grad = (probs * (prob_grad - lax.optimization_barrier(jnp.sum(prob_grad * probs, axis=-1, keepdims=True))) * scale_factor).astype(jnp.bfloat16)
    score_f = score_grad.astype(jnp.float32)
    query_grad = jnp.einsum('nhts,snhd->tnhd', score_f, key_f).astype(jnp.bfloat16)
    key_grad = jnp.einsum('nhts,tnhd->snhd', score_f, query_f).astype(jnp.bfloat16)
    query_flat = query_grad.reshape(steps_all * nodes_here, width)
    key_flat = key_grad.reshape(steps_all * nodes_here, width)
    value_flat = value_grad.reshape(steps_all * nodes_here, width)

    def weight_grad(grad_rows):
        return lax.dot_general(flat, grad_rows, (((0,), (0,)), ((), ())), preferred_element_type=jnp.float32)

    def input_grad(grad_rows, weight):
        return lax.dot_general(grad_rows, weight, (((1,), (1,)), ((), ())), preferred_element_type=jnp.float32)
    back = upstream.reshape(steps_all * nodes_here, width).astype(jnp.float32)
    back = back + input_grad(query_flat, w_query) + input_grad(key_flat, w_key) + input_grad(value_flat, w_value)
    back = back.astype(jnp.bfloat16).reshape(steps_all, nodes_here, width)
    return ((weight_grad(query_flat), weight_grad(key_flat), weight_grad(value_flat)), back)

def reference(node_states, edge_source, edge_target, halo_rows, halo_count, w_message, w_query, w_key, w_value, cotangent):
    days_all, nodes_all, width = node_states.shape
    parts = GROUPS
    blocks = node_states.reshape(days_all, parts, NODE_DEV, width)
    picks = halo_rows.reshape(days_all, parts, HALO)
    live = jnp.arange(HALO)[None, None, :] < halo_count[:, :, None]
    picked = jnp.take_along_axis(blocks, picks[:, :, :, None], axis=2)
    sent = jnp.where(live[:, :, :, None], picked, jnp.zeros_like(picked))
    received = jnp.roll(sent, 1, axis=1)
    flat_count = days_all * parts
    block_flat = blocks.reshape(flat_count, NODE_DEV, width)
    recv_flat = received.reshape(flat_count, HALO, width)
    source_flat = edge_source.reshape(flat_count, -1)
    target_flat = edge_target.reshape(flat_count, -1)

    def forward_one(items):
        return gnn_forward(items[0], items[1], items[2], items[3], w_message)[3]
    hidden = lax.map(forward_one, (block_flat, recv_flat, source_flat, target_flat))
    hidden_parts = jnp.moveaxis(hidden.reshape(days_all, parts, NODE_DEV, width), 1, 0)
    cot_parts = jnp.moveaxis(cotangent.reshape(days_all, parts, NODE_DEV, width), 1, 0)

    def attend_one(items):
        return attend(items[0], items[1], w_query, w_key, w_value)
    attn_grads, back = lax.map(attend_one, (hidden_parts, cot_parts))
    grad_query = lax.optimization_barrier(jnp.sum(attn_grads[0], axis=0))
    grad_key = lax.optimization_barrier(jnp.sum(attn_grads[1], axis=0))
    grad_value = lax.optimization_barrier(jnp.sum(attn_grads[2], axis=0))
    back_flat = jnp.moveaxis(back, 0, 1).reshape(flat_count, NODE_DEV, width)

    def backward_one(carry, items):
        aggregate, preact, inverse, hidden_one = gnn_forward(items[0], items[1], items[2], items[3], w_message)
        message_part, local_grad, halo_grad = gnn_backward(items[4], aggregate, preact, inverse, items[2], items[3], w_message, HALO)
        return (carry + message_part, (local_grad, halo_grad))
    grad_message, outputs = lax.scan(backward_one, jnp.zeros((width, width), jnp.float32), (block_flat, recv_flat, source_flat, target_flat, back_flat))
    local_grad, halo_grad = outputs
    returned = jnp.roll(halo_grad.reshape(days_all, parts, HALO, width), -1, axis=1)
    returned = jnp.where(live[:, :, :, None], returned.astype(jnp.float32), jnp.zeros(returned.shape, jnp.float32))

    def scatter_back(rows_grad, indices):
        return jax.ops.segment_sum(rows_grad, indices, num_segments=NODE_DEV)
    scattered = jax.vmap(scatter_back)(returned.reshape(flat_count, HALO, width), picks.reshape(flat_count, HALO))
    state_grad = (local_grad + scattered).reshape(days_all, nodes_all, width)
    return (state_grad, grad_message, grad_query, grad_key, grad_value)
```

```python
import jax
import jax.numpy as jnp
from jax import lax
from jax.sharding import PartitionSpec as P

HEADS = 4


def from_behind(value, axis, steps):
    count = lax.axis_size(axis)
    pairs = [(source, (source + steps) % count) for source in range(count)]
    return lax.ppermute(value, axis, pairs)


def _power_of_two(count):
    return count > 0 and count & (count - 1) == 0


def tree_sum(values, axes):
    sizes = [lax.axis_size(axis) for axis in axes]
    flat = jnp.concatenate([value.reshape(-1) for value in values])
    total = 1
    for size in sizes:
        total *= size
    if not all(_power_of_two(size) for size in sizes) or flat.shape[0] % total:
        return lax.psum(tuple(values), axes)
    steps = [(axis, bit) for axis, size in zip(axes, sizes) for bit in [1 << k for k in range(size.bit_length() - 1)]]
    for axis, bit in steps:
        side = (lax.axis_index(axis) // bit) % 2
        halves = flat.reshape(2, -1)
        keep = jnp.where(side == 0, halves[0], halves[1])
        send = jnp.where(side == 0, halves[1], halves[0])
        pairs = [(source, source ^ bit) for source in range(lax.axis_size(axis))]
        flat = keep + lax.ppermute(send, axis, pairs)
    for axis, bit in reversed(steps):
        side = (lax.axis_index(axis) // bit) % 2
        pairs = [(source, source ^ bit) for source in range(lax.axis_size(axis))]
        other = lax.ppermute(flat, axis, pairs)
        flat = jnp.where(side == 0, jnp.concatenate([flat, other]), jnp.concatenate([other, flat]))
    results, start = [], 0
    for value in values:
        results.append(flat[start : start + value.size].reshape(value.shape))
        start += value.size
    return tuple(results)


def adjacency(sources, targets, count_rows, total_rows):
    target_hot = (targets[:, None] == jnp.arange(count_rows, dtype=jnp.int32)[None, :]).astype(
        jnp.bfloat16
    )
    source_hot = (sources[:, None] == jnp.arange(total_rows, dtype=jnp.int32)[None, :]).astype(
        jnp.bfloat16
    )
    counts = lax.dot_general(
        target_hot, source_hot, (((0,), (0,)), ((), ())), preferred_element_type=jnp.float32
    )
    return counts.astype(jnp.bfloat16)


def gnn_forward(states, received, adjacent, w_message):
    extended = jnp.concatenate([states, received], axis=0)
    neighbours = jnp.dot(adjacent, extended, preferred_element_type=jnp.float32)
    counted = jnp.sum(adjacent.astype(jnp.float32), axis=1)
    inverse = 1.0 / (counted + 1.0)
    aggregate = ((states.astype(jnp.float32) + neighbours) * inverse[:, None]).astype(jnp.bfloat16)
    preact = jnp.dot(aggregate, w_message, preferred_element_type=jnp.float32)
    hidden = (states.astype(jnp.float32) + jax.nn.silu(preact)).astype(jnp.bfloat16)
    return (aggregate, preact, inverse, hidden)


def gnn_backward(upstream, aggregate, preact, inverse, adjacent, w_message):
    count_rows = aggregate.shape[0]
    up_float = upstream.astype(jnp.float32)
    sigmoid_val = jax.nn.sigmoid(preact)
    pre_grad = (up_float * sigmoid_val * (1.0 + preact * (1.0 - sigmoid_val))).astype(jnp.bfloat16)
    message_part = lax.dot_general(
        aggregate, pre_grad, (((0,), (0,)), ((), ())), preferred_element_type=jnp.float32
    )
    agg_grad = lax.dot_general(
        pre_grad, w_message, (((1,), (1,)), ((), ())), preferred_element_type=jnp.float32
    )
    term_grad = agg_grad * inverse[:, None]
    ext_grad = lax.dot_general(
        adjacent.astype(jnp.float32),
        term_grad,
        (((0,), (0,)), ((), ())),
        precision=lax.Precision.HIGHEST,
        preferred_element_type=jnp.float32,
    )
    local_grad = up_float + term_grad + ext_grad[:count_rows]
    halo_grad = ext_grad[count_rows:].astype(jnp.bfloat16)
    return (message_part, local_grad, halo_grad)


def attend(states, upstream, w_query, w_key, w_value):
    steps_all, nodes_here, width = states.shape
    head_dim = width // HEADS
    scale_factor = head_dim ** (-0.5)
    flat = states.reshape(steps_all * nodes_here, width)

    def project(weight):
        return jnp.dot(flat, weight, preferred_element_type=jnp.float32).astype(jnp.bfloat16)

    def splitter(matrix):
        return matrix.reshape(steps_all, nodes_here, HEADS, head_dim).astype(jnp.float32)

    queries = project(w_query)
    key_rows = project(w_key)
    value_rows = project(w_value)
    query_f = splitter(queries)
    key_f = splitter(key_rows)
    value_f = splitter(value_rows)
    scores = jnp.einsum("tnhd,snhd->nhts", query_f, key_f) * scale_factor
    causal = jnp.arange(steps_all)[:, None] >= jnp.arange(steps_all)[None, :]
    scores = jnp.where(causal, scores, -jnp.inf)
    highest = jnp.max(scores, axis=-1, keepdims=True)
    exponent = jnp.exp(scores - highest)
    probs = exponent / jnp.sum(exponent, axis=-1, keepdims=True)
    probs_low = probs.astype(jnp.bfloat16).astype(jnp.float32)
    up_heads = splitter(upstream)
    value_grad = jnp.einsum("nhts,tnhd->snhd", probs_low, up_heads).astype(jnp.bfloat16)
    prob_grad = jnp.einsum("tnhd,snhd->nhts", up_heads, value_f)
    score_grad = (
        probs * (prob_grad - jnp.sum(prob_grad * probs, axis=-1, keepdims=True)) * scale_factor
    ).astype(jnp.bfloat16)
    score_f = score_grad.astype(jnp.float32)
    query_grad = jnp.einsum("nhts,snhd->tnhd", score_f, key_f).astype(jnp.bfloat16)
    key_grad = jnp.einsum("nhts,tnhd->snhd", score_f, query_f).astype(jnp.bfloat16)
    query_flat = query_grad.reshape(steps_all * nodes_here, width)
    key_flat = key_grad.reshape(steps_all * nodes_here, width)
    value_flat = value_grad.reshape(steps_all * nodes_here, width)

    def weight_grad(grad_rows):
        return lax.dot_general(
            flat, grad_rows, (((0,), (0,)), ((), ())), preferred_element_type=jnp.float32
        )

    def input_grad(grad_rows, weight):
        return lax.dot_general(
            grad_rows, weight, (((1,), (1,)), ((), ())), preferred_element_type=jnp.float32
        )

    back = upstream.reshape(steps_all * nodes_here, width).astype(jnp.float32)
    back = (
        back
        + input_grad(query_flat, w_query)
        + input_grad(key_flat, w_key)
        + input_grad(value_flat, w_value)
    )
    back = back.astype(jnp.bfloat16).reshape(steps_all, nodes_here, width)
    return ((weight_grad(query_flat), weight_grad(key_flat), weight_grad(value_flat)), back)


def local(
    node_states,
    edge_source,
    edge_target,
    halo_rows,
    halo_count,
    w_message,
    w_query,
    w_key,
    w_value,
    cotangent,
):
    days_local, node_local, width = node_states.shape
    halo_slots = halo_rows.shape[1]
    live = jnp.arange(halo_slots)[None, :] < halo_count
    picked = jnp.take_along_axis(node_states, halo_rows[:, :, None], axis=1)
    sent = jnp.where(live[:, :, None], picked, jnp.zeros_like(picked))
    received = from_behind(sent, "dom", 1)

    def forward_one(items):
        adjacent = adjacency(items[2], items[3], node_local, node_local + halo_slots)
        aggregate, preact, inverse, hidden = gnn_forward(items[0], items[1], adjacent, w_message)
        return (aggregate, preact, inverse, hidden, adjacent)

    aggregate, preact, inverse, hidden, adjacent = lax.map(
        forward_one, (node_states, received, edge_source, edge_target)
    )
    node_major = lax.all_to_all(hidden, "day", split_axis=1, concat_axis=0, tiled=True)
    upstream = cotangent.reshape(cotangent.shape[0], -1, width)
    attn_grads, back = attend(node_major, upstream, w_query, w_key, w_value)
    back_days = lax.all_to_all(back, "day", split_axis=0, concat_axis=1, tiled=True)

    def backward_one(items):
        return gnn_backward(items[0], items[1], items[2], items[3], items[4], w_message)

    message_parts, local_grad, halo_grad = lax.map(
        backward_one, (back_days, aggregate, preact, inverse, adjacent)
    )
    grad_message = jnp.sum(message_parts, axis=0)
    returned = from_behind(halo_grad, "dom", -1)
    slot_hot = jnp.logical_and(
        halo_rows[:, :, None] == jnp.arange(node_local, dtype=jnp.int32)[None, None, :],
        live[:, :, None],
    ).astype(jnp.bfloat16)
    scattered = jnp.einsum("dsn,dsh->dnh", slot_hot, returned, preferred_element_type=jnp.float32)
    state_grad = local_grad + scattered
    grad_message, grad_query, grad_key, grad_value = tree_sum(
        (grad_message, attn_grads[0], attn_grads[1], attn_grads[2]), ("dom", "day")
    )
    return (state_grad, grad_message, grad_query, grad_key, grad_value)


def solution(mesh):
    return jax.shard_map(
        local,
        mesh=mesh,
        in_specs=(
            P("day", "dom", None),
            P("day", "dom"),
            P("day", "dom"),
            P("day", "dom"),
            P("day", "dom"),
            P(),
            P(),
            P(),
            P(),
            P(None, "dom", "day", None, None),
        ),
        out_specs=(P("day", "dom", None), P(), P(), P(), P()),
        check_vma=False,
    )
```

```python
import jax
import jax.numpy as jnp
from jax import lax
from jax.sharding import PartitionSpec as P

HEADS = 4


def from_behind(value, axis, steps):
    count = lax.axis_size(axis)
    pairs = [(source, (source + steps) % count) for source in range(count)]
    return lax.ppermute(value, axis, pairs)


def _power_of_two(count):
    return count > 0 and count & (count - 1) == 0


def tree_sum(values, axes):
    sizes = [lax.axis_size(axis) for axis in axes]
    flat = jnp.concatenate([value.reshape(-1) for value in values])
    total = 1
    for size in sizes:
        total *= size
    if not all(_power_of_two(size) for size in sizes) or flat.shape[0] % total:
        return lax.psum(tuple(values), axes)
    steps = [(axis, bit) for axis, size in zip(axes, sizes) for bit in [1 << k for k in range(size.bit_length() - 1)]]
    for axis, bit in steps:
        side = (lax.axis_index(axis) // bit) % 2
        halves = flat.reshape(2, -1)
        keep = jnp.where(side == 0, halves[0], halves[1])
        send = jnp.where(side == 0, halves[1], halves[0])
        pairs = [(source, source ^ bit) for source in range(lax.axis_size(axis))]
        flat = keep + lax.ppermute(send, axis, pairs)
    for axis, bit in reversed(steps):
        side = (lax.axis_index(axis) // bit) % 2
        pairs = [(source, source ^ bit) for source in range(lax.axis_size(axis))]
        other = lax.ppermute(flat, axis, pairs)
        flat = jnp.where(side == 0, jnp.concatenate([flat, other]), jnp.concatenate([other, flat]))
    results, start = [], 0
    for value in values:
        results.append(flat[start : start + value.size].reshape(value.shape))
        start += value.size
    return tuple(results)


def adjacency(sources, targets, count_rows, total_rows):
    target_hot = (targets[:, None] == jnp.arange(count_rows, dtype=jnp.int32)[None, :]).astype(
        jnp.bfloat16
    )
    source_hot = (sources[:, None] == jnp.arange(total_rows, dtype=jnp.int32)[None, :]).astype(
        jnp.bfloat16
    )
    counts = lax.dot_general(
        target_hot, source_hot, (((0,), (0,)), ((), ())), preferred_element_type=jnp.float32
    )
    return counts.astype(jnp.bfloat16)


def gnn_forward(states, received, adjacent, w_message):
    extended = jnp.concatenate([states, received], axis=0)
    neighbours = jnp.dot(adjacent, extended, preferred_element_type=jnp.float32)
    counted = jnp.sum(adjacent.astype(jnp.float32), axis=1)
    inverse = 1.0 / (counted + 1.0)
    aggregate = ((states.astype(jnp.float32) + neighbours) * inverse[:, None]).astype(jnp.bfloat16)
    preact = jnp.dot(aggregate, w_message, preferred_element_type=jnp.float32)
    hidden = (states.astype(jnp.float32) + jax.nn.silu(preact)).astype(jnp.bfloat16)
    return (aggregate, preact, inverse, hidden)


def gnn_backward(upstream, aggregate, preact, inverse, adjacent, w_message):
    count_rows = aggregate.shape[0]
    up_float = upstream.astype(jnp.float32)
    sigmoid_val = jax.nn.sigmoid(preact)
    pre_grad = (up_float * sigmoid_val * (1.0 + preact * (1.0 - sigmoid_val))).astype(jnp.bfloat16)
    message_part = lax.dot_general(
        aggregate, pre_grad, (((0,), (0,)), ((), ())), preferred_element_type=jnp.float32
    )
    agg_grad = lax.dot_general(
        pre_grad, w_message, (((1,), (1,)), ((), ())), preferred_element_type=jnp.float32
    )
    term_grad = agg_grad * inverse[:, None]
    ext_grad = lax.dot_general(
        adjacent.astype(jnp.float32),
        term_grad,
        (((0,), (0,)), ((), ())),
        precision=lax.Precision.HIGHEST,
        preferred_element_type=jnp.float32,
    )
    local_grad = up_float + term_grad + ext_grad[:count_rows]
    halo_grad = ext_grad[count_rows:].astype(jnp.bfloat16)
    return (message_part, local_grad, halo_grad)


def attend(states, upstream, w_query, w_key, w_value):
    steps_all, nodes_here, width = states.shape
    head_dim = width // HEADS
    scale_factor = head_dim ** (-0.5)
    flat = states.reshape(steps_all * nodes_here, width)

    def project(weight):
        return jnp.dot(flat, weight, preferred_element_type=jnp.float32).astype(jnp.bfloat16)

    def splitter(matrix):
        return matrix.reshape(steps_all, nodes_here, HEADS, head_dim).astype(jnp.float32)

    queries = project(w_query)
    key_rows = project(w_key)
    value_rows = project(w_value)
    query_f = splitter(queries)
    key_f = splitter(key_rows)
    value_f = splitter(value_rows)
    scores = jnp.einsum("tnhd,snhd->nhts", query_f, key_f) * scale_factor
    causal = jnp.arange(steps_all)[:, None] >= jnp.arange(steps_all)[None, :]
    scores = jnp.where(causal, scores, -jnp.inf)
    highest = jnp.max(scores, axis=-1, keepdims=True)
    exponent = jnp.exp(scores - highest)
    probs = exponent / jnp.sum(exponent, axis=-1, keepdims=True)
    probs_low = probs.astype(jnp.bfloat16).astype(jnp.float32)
    up_heads = splitter(upstream)
    value_grad = jnp.einsum("nhts,tnhd->snhd", probs_low, up_heads).astype(jnp.bfloat16)
    prob_grad = jnp.einsum("tnhd,snhd->nhts", up_heads, value_f)
    score_grad = (
        probs * (prob_grad - jnp.sum(prob_grad * probs, axis=-1, keepdims=True)) * scale_factor
    ).astype(jnp.bfloat16)
    score_f = score_grad.astype(jnp.float32)
    query_grad = jnp.einsum("nhts,snhd->tnhd", score_f, key_f).astype(jnp.bfloat16)
    key_grad = jnp.einsum("nhts,tnhd->snhd", score_f, query_f).astype(jnp.bfloat16)
    query_flat = query_grad.reshape(steps_all * nodes_here, width)
    key_flat = key_grad.reshape(steps_all * nodes_here, width)
    value_flat = value_grad.reshape(steps_all * nodes_here, width)

    def weight_grad(grad_rows):
        return lax.dot_general(
            flat, grad_rows, (((0,), (0,)), ((), ())), preferred_element_type=jnp.float32
        )

    def input_grad(grad_rows, weight):
        return lax.dot_general(
            grad_rows, weight, (((1,), (1,)), ((), ())), preferred_element_type=jnp.float32
        )

    back = upstream.reshape(steps_all * nodes_here, width).astype(jnp.float32)
    back = (
        back
        + input_grad(query_flat, w_query)
        + input_grad(key_flat, w_key)
        + input_grad(value_flat, w_value)
    )
    back = back.astype(jnp.bfloat16).reshape(steps_all, nodes_here, width)
    return ((weight_grad(query_flat), weight_grad(key_flat), weight_grad(value_flat)), back)


def local(
    node_states,
    edge_source,
    edge_target,
    halo_rows,
    halo_count,
    w_message,
    w_query,
    w_key,
    w_value,
    cotangent,
):
    days_local, node_local, width = node_states.shape
    halo_slots = halo_rows.shape[1]
    live = jnp.arange(halo_slots)[None, :] < halo_count
    rows = jnp.arange(node_local, dtype=jnp.int32)
    slot_hot = jnp.logical_and(
        halo_rows[:, :, None] == rows[None, None, :], live[:, :, None]
    ).astype(jnp.bfloat16)
    sent = jnp.einsum(
        "dsn,dnh->dsh", slot_hot, node_states, preferred_element_type=jnp.float32
    ).astype(jnp.bfloat16)
    received = from_behind(sent, "dom", 1)

    target_hot = (edge_target[:, :, None] == rows[None, None, :]).astype(jnp.bfloat16)
    local_hot = (edge_source[:, :, None] == rows[None, None, :]).astype(jnp.bfloat16)
    halo_ids = node_local + jnp.arange(halo_slots, dtype=jnp.int32)
    halo_hot = (edge_source[:, :, None] == halo_ids[None, None, :]).astype(jnp.bfloat16)
    adjacent_local = jnp.einsum(
        "der,des->drs", target_hot, local_hot, preferred_element_type=jnp.float32
    ).astype(jnp.bfloat16)
    adjacent_halo = jnp.einsum(
        "der,des->drs", target_hot, halo_hot, preferred_element_type=jnp.float32
    ).astype(jnp.bfloat16)
    counted = jnp.sum(target_hot.astype(jnp.float32), axis=1)
    inverse = 1.0 / (counted + 1.0)

    states_f = node_states.astype(jnp.float32)
    neighbours = jnp.einsum(
        "drs,dsh->drh", adjacent_local, node_states, preferred_element_type=jnp.float32
    ) + jnp.einsum("drs,dsh->drh", adjacent_halo, received, preferred_element_type=jnp.float32)
    aggregate = ((states_f + neighbours) * inverse[:, :, None]).astype(jnp.bfloat16)
    preact = jnp.einsum("drh,hk->drk", aggregate, w_message, preferred_element_type=jnp.float32)
    hidden = (states_f + jax.nn.silu(preact)).astype(jnp.bfloat16)

    node_major = lax.all_to_all(hidden, "day", split_axis=1, concat_axis=0, tiled=True)
    upstream = cotangent.reshape(cotangent.shape[0], -1, width)
    attn_grads, back = attend(node_major, upstream, w_query, w_key, w_value)
    back_days = lax.all_to_all(back, "day", split_axis=0, concat_axis=1, tiled=True)

    sigmoid_val = jax.nn.sigmoid(preact)
    pre_grad = (
        back_days.astype(jnp.float32) * sigmoid_val * (1.0 + preact * (1.0 - sigmoid_val))
    ).astype(jnp.bfloat16)
    grad_message = lax.dot_general(
        aggregate.reshape(-1, width),
        pre_grad.reshape(-1, width),
        (((0,), (0,)), ((), ())),
        preferred_element_type=jnp.float32,
    )
    grad_message, grad_query, grad_key, grad_value = tree_sum(
        (grad_message, attn_grads[0], attn_grads[1], attn_grads[2]), ("dom", "day")
    )
    agg_grad = jnp.einsum("drk,hk->drh", pre_grad, w_message, preferred_element_type=jnp.float32)
    term_grad = agg_grad * inverse[:, :, None]
    halo_grad = jnp.einsum(
        "drs,drh->dsh",
        adjacent_halo.astype(jnp.float32),
        term_grad,
        precision=lax.Precision.HIGHEST,
        preferred_element_type=jnp.float32,
    ).astype(jnp.bfloat16)
    returned = from_behind(halo_grad, "dom", -1)
    own_grad = jnp.einsum(
        "drs,drh->dsh",
        adjacent_local.astype(jnp.float32),
        term_grad,
        precision=lax.Precision.HIGHEST,
        preferred_element_type=jnp.float32,
    )
    scattered = jnp.einsum("dsn,dsh->dnh", slot_hot, returned, preferred_element_type=jnp.float32)
    state_grad = back_days.astype(jnp.float32) + term_grad + own_grad + scattered
    return (state_grad, grad_message, grad_query, grad_key, grad_value)


def solution(mesh):
    return jax.shard_map(
        local,
        mesh=mesh,
        in_specs=(
            P("day", "dom", None),
            P("day", "dom"),
            P("day", "dom"),
            P("day", "dom"),
            P("day", "dom"),
            P(),
            P(),
            P(),
            P(),
            P(None, "dom", "day", None, None),
        ),
        out_specs=(P("day", "dom", None), P(), P(), P(), P()),
        check_vma=False,
    )
```

```python
import jax
import jax.numpy as jnp
from jax import lax
from jax.sharding import PartitionSpec as P

HEADS = 4


def from_behind(value, axis, steps):
    count = lax.axis_size(axis)
    pairs = [(source, (source + steps) % count) for source in range(count)]
    return lax.ppermute(value, axis, pairs)


def _power_of_two(count):
    return count > 0 and count & (count - 1) == 0


def tree_sum(values, axes):
    sizes = [lax.axis_size(axis) for axis in axes]
    flat = jnp.concatenate([value.reshape(-1) for value in values])
    total = 1
    for size in sizes:
        total *= size
    if not all(_power_of_two(size) for size in sizes) or flat.shape[0] % total:
        return lax.psum(tuple(values), axes)
    steps = [(axis, bit) for axis, size in zip(axes, sizes) for bit in [1 << k for k in range(size.bit_length() - 1)]]
    for axis, bit in steps:
        side = (lax.axis_index(axis) // bit) % 2
        halves = flat.reshape(2, -1)
        keep = jnp.where(side == 0, halves[0], halves[1])
        send = jnp.where(side == 0, halves[1], halves[0])
        pairs = [(source, source ^ bit) for source in range(lax.axis_size(axis))]
        flat = keep + lax.ppermute(send, axis, pairs)
    for axis, bit in reversed(steps):
        side = (lax.axis_index(axis) // bit) % 2
        pairs = [(source, source ^ bit) for source in range(lax.axis_size(axis))]
        other = lax.ppermute(flat, axis, pairs)
        flat = jnp.where(side == 0, jnp.concatenate([flat, other]), jnp.concatenate([other, flat]))
    results, start = [], 0
    for value in values:
        results.append(flat[start : start + value.size].reshape(value.shape))
        start += value.size
    return tuple(results)


def adjacency(sources, targets, count_rows, total_rows):
    target_hot = (targets[:, None] == jnp.arange(count_rows, dtype=jnp.int32)[None, :]).astype(
        jnp.bfloat16
    )
    source_hot = (sources[:, None] == jnp.arange(total_rows, dtype=jnp.int32)[None, :]).astype(
        jnp.bfloat16
    )
    counts = lax.dot_general(
        target_hot, source_hot, (((0,), (0,)), ((), ())), preferred_element_type=jnp.float32
    )
    return counts.astype(jnp.bfloat16)


def gnn_forward(states, received, adjacent, w_message):
    extended = jnp.concatenate([states, received], axis=0)
    neighbours = jnp.dot(adjacent, extended, preferred_element_type=jnp.float32)
    counted = jnp.sum(adjacent.astype(jnp.float32), axis=1)
    inverse = 1.0 / (counted + 1.0)
    aggregate = ((states.astype(jnp.float32) + neighbours) * inverse[:, None]).astype(jnp.bfloat16)
    preact = jnp.dot(aggregate, w_message, preferred_element_type=jnp.float32)
    hidden = (states.astype(jnp.float32) + jax.nn.silu(preact)).astype(jnp.bfloat16)
    return (aggregate, preact, inverse, hidden)


def gnn_backward(upstream, aggregate, preact, inverse, adjacent, w_message):
    count_rows = aggregate.shape[0]
    up_float = upstream.astype(jnp.float32)
    sigmoid_val = jax.nn.sigmoid(preact)
    pre_grad = (up_float * sigmoid_val * (1.0 + preact * (1.0 - sigmoid_val))).astype(jnp.bfloat16)
    message_part = lax.dot_general(
        aggregate, pre_grad, (((0,), (0,)), ((), ())), preferred_element_type=jnp.float32
    )
    agg_grad = lax.dot_general(
        pre_grad, w_message, (((1,), (1,)), ((), ())), preferred_element_type=jnp.float32
    )
    term_grad = agg_grad * inverse[:, None]
    ext_grad = lax.dot_general(
        adjacent.astype(jnp.float32),
        term_grad,
        (((0,), (0,)), ((), ())),
        precision=lax.Precision.HIGHEST,
        preferred_element_type=jnp.float32,
    )
    local_grad = up_float + term_grad + ext_grad[:count_rows]
    halo_grad = ext_grad[count_rows:].astype(jnp.bfloat16)
    return (message_part, local_grad, halo_grad)


def attend(states, upstream, w_query, w_key, w_value):
    steps_all, nodes_here, width = states.shape
    head_dim = width // HEADS
    scale_factor = head_dim ** (-0.5)
    flat = states.reshape(steps_all * nodes_here, width)

    def project(weight):
        return jnp.dot(flat, weight, preferred_element_type=jnp.float32).astype(jnp.bfloat16)

    def splitter(matrix):
        return matrix.reshape(steps_all, nodes_here, HEADS, head_dim).astype(jnp.float32)

    queries = project(w_query)
    key_rows = project(w_key)
    value_rows = project(w_value)
    query_f = splitter(queries)
    key_f = splitter(key_rows)
    value_f = splitter(value_rows)
    scores = jnp.einsum("tnhd,snhd->nhts", query_f, key_f) * scale_factor
    causal = jnp.arange(steps_all)[:, None] >= jnp.arange(steps_all)[None, :]
    scores = jnp.where(causal, scores, -jnp.inf)
    highest = jnp.max(scores, axis=-1, keepdims=True)
    exponent = jnp.exp(scores - highest)
    probs = exponent / jnp.sum(exponent, axis=-1, keepdims=True)
    probs_low = probs.astype(jnp.bfloat16).astype(jnp.float32)
    up_heads = splitter(upstream)
    value_grad = jnp.einsum("nhts,tnhd->snhd", probs_low, up_heads).astype(jnp.bfloat16)
    prob_grad = jnp.einsum("tnhd,snhd->nhts", up_heads, value_f)
    score_grad = (
        probs * (prob_grad - jnp.sum(prob_grad * probs, axis=-1, keepdims=True)) * scale_factor
    ).astype(jnp.bfloat16)
    score_f = score_grad.astype(jnp.float32)
    query_grad = jnp.einsum("nhts,snhd->tnhd", score_f, key_f).astype(jnp.bfloat16)
    key_grad = jnp.einsum("nhts,tnhd->snhd", score_f, query_f).astype(jnp.bfloat16)
    query_flat = query_grad.reshape(steps_all * nodes_here, width)
    key_flat = key_grad.reshape(steps_all * nodes_here, width)
    value_flat = value_grad.reshape(steps_all * nodes_here, width)

    def weight_grad(grad_rows):
        return lax.dot_general(
            flat, grad_rows, (((0,), (0,)), ((), ())), preferred_element_type=jnp.float32
        )

    def input_grad(grad_rows, weight):
        return lax.dot_general(
            grad_rows, weight, (((1,), (1,)), ((), ())), preferred_element_type=jnp.float32
        )

    back = upstream.reshape(steps_all * nodes_here, width).astype(jnp.float32)
    back = (
        back
        + input_grad(query_flat, w_query)
        + input_grad(key_flat, w_key)
        + input_grad(value_flat, w_value)
    )
    back = back.astype(jnp.bfloat16).reshape(steps_all, nodes_here, width)
    return ((weight_grad(query_flat), weight_grad(key_flat), weight_grad(value_flat)), back)


def attend_blocked(states, upstream, w_query, w_key, w_value):
    steps_all, nodes_here, width = states.shape
    head_dim = width // HEADS
    scale_factor = head_dim ** (-0.5)
    per_group = max(1, 128 // steps_all)
    if nodes_here % per_group:
        per_group = 1
    groups = nodes_here // per_group
    block = per_group * steps_all
    flat = jnp.swapaxes(states, 0, 1).reshape(nodes_here * steps_all, width)
    up_flat = jnp.swapaxes(upstream, 0, 1).reshape(nodes_here * steps_all, width)

    def project(weight):
        return jnp.dot(flat, weight, preferred_element_type=jnp.float32).astype(jnp.bfloat16)

    def blocks(matrix):
        return matrix.reshape(groups, block, HEADS, head_dim)

    queries = blocks(project(w_query))
    key_rows = blocks(project(w_key))
    value_rows = blocks(project(w_value))
    up_heads = blocks(up_flat)
    position = jnp.arange(block)
    same = (position[:, None] // steps_all) == (position[None, :] // steps_all)
    causal = jnp.logical_and(same, (position[:, None] % steps_all) >= (position[None, :] % steps_all))

    def contract(spec, left, right):
        return jnp.einsum(spec, left, right, preferred_element_type=jnp.float32)

    scores = contract("gihd,gjhd->ghij", queries, key_rows) * scale_factor
    scores = jnp.where(causal, scores, -jnp.inf)
    highest = jnp.max(scores, axis=-1, keepdims=True)
    exponent = jnp.exp(scores - highest)
    probs = exponent / jnp.sum(exponent, axis=-1, keepdims=True)
    probs_low = probs.astype(jnp.bfloat16)
    value_grad = contract("ghij,gihd->gjhd", probs_low, up_heads).astype(jnp.bfloat16)
    prob_grad = contract("gihd,gjhd->ghij", up_heads, value_rows)
    score_grad = (
        probs * (prob_grad - jnp.sum(prob_grad * probs, axis=-1, keepdims=True)) * scale_factor
    ).astype(jnp.bfloat16)
    query_grad = contract("ghij,gjhd->gihd", score_grad, key_rows).astype(jnp.bfloat16)
    key_grad = contract("ghij,gihd->gjhd", score_grad, queries).astype(jnp.bfloat16)
    query_flat = query_grad.reshape(-1, width)
    key_flat = key_grad.reshape(-1, width)
    value_flat = value_grad.reshape(-1, width)

    def weight_grad(grad_rows):
        return lax.dot_general(
            flat, grad_rows, (((0,), (0,)), ((), ())), preferred_element_type=jnp.float32
        )

    def input_grad(grad_rows, weight):
        return lax.dot_general(
            grad_rows, weight, (((1,), (1,)), ((), ())), preferred_element_type=jnp.float32
        )

    back = (
        up_flat.astype(jnp.float32)
        + input_grad(query_flat, w_query)
        + input_grad(key_flat, w_key)
        + input_grad(value_flat, w_value)
    )
    back = jnp.swapaxes(back.astype(jnp.bfloat16).reshape(nodes_here, steps_all, width), 0, 1)
    return ((weight_grad(query_flat), weight_grad(key_flat), weight_grad(value_flat)), back)


def local(
    node_states,
    edge_source,
    edge_target,
    halo_rows,
    halo_count,
    w_message,
    w_query,
    w_key,
    w_value,
    cotangent,
):
    days_local, node_local, width = node_states.shape
    halo_slots = halo_rows.shape[1]
    live = jnp.arange(halo_slots)[None, :] < halo_count
    rows = jnp.arange(node_local, dtype=jnp.int32)
    slot_hot = jnp.logical_and(
        halo_rows[:, :, None] == rows[None, None, :], live[:, :, None]
    ).astype(jnp.bfloat16)
    sent = jnp.einsum(
        "dsn,dnh->dsh", slot_hot, node_states, preferred_element_type=jnp.float32
    ).astype(jnp.bfloat16)
    received = from_behind(sent, "dom", 1)

    target_hot = (edge_target[:, :, None] == rows[None, None, :]).astype(jnp.bfloat16)
    local_hot = (edge_source[:, :, None] == rows[None, None, :]).astype(jnp.bfloat16)
    halo_ids = node_local + jnp.arange(halo_slots, dtype=jnp.int32)
    halo_hot = (edge_source[:, :, None] == halo_ids[None, None, :]).astype(jnp.bfloat16)
    adjacent_local = jnp.einsum(
        "der,des->drs", target_hot, local_hot, preferred_element_type=jnp.float32
    ).astype(jnp.bfloat16)
    adjacent_halo = jnp.einsum(
        "der,des->drs", target_hot, halo_hot, preferred_element_type=jnp.float32
    ).astype(jnp.bfloat16)
    counted = jnp.sum(target_hot.astype(jnp.float32), axis=1)
    inverse = 1.0 / (counted + 1.0)

    states_f = node_states.astype(jnp.float32)
    neighbours = jnp.einsum(
        "drs,dsh->drh", adjacent_local, node_states, preferred_element_type=jnp.float32
    ) + jnp.einsum("drs,dsh->drh", adjacent_halo, received, preferred_element_type=jnp.float32)
    aggregate = ((states_f + neighbours) * inverse[:, :, None]).astype(jnp.bfloat16)
    preact = jnp.einsum("drh,hk->drk", aggregate, w_message, preferred_element_type=jnp.float32)
    hidden = (states_f + jax.nn.silu(preact)).astype(jnp.bfloat16)

    node_major = lax.all_to_all(hidden, "day", split_axis=1, concat_axis=0, tiled=True)
    upstream = cotangent.reshape(cotangent.shape[0], -1, width)
    attn_grads, back = attend_blocked(node_major, upstream, w_query, w_key, w_value)
    back_days = lax.all_to_all(back, "day", split_axis=0, concat_axis=1, tiled=True)

    sigmoid_val = jax.nn.sigmoid(preact)
    pre_grad = (
        back_days.astype(jnp.float32) * sigmoid_val * (1.0 + preact * (1.0 - sigmoid_val))
    ).astype(jnp.bfloat16)
    grad_message = lax.dot_general(
        aggregate.reshape(-1, width),
        pre_grad.reshape(-1, width),
        (((0,), (0,)), ((), ())),
        preferred_element_type=jnp.float32,
    )
    grad_message, grad_query, grad_key, grad_value = tree_sum(
        (grad_message, attn_grads[0], attn_grads[1], attn_grads[2]), ("dom", "day")
    )
    agg_grad = jnp.einsum("drk,hk->drh", pre_grad, w_message, preferred_element_type=jnp.float32)
    term_grad = agg_grad * inverse[:, :, None]
    halo_grad = jnp.einsum(
        "drs,drh->dsh",
        adjacent_halo.astype(jnp.float32),
        term_grad,
        precision=lax.Precision.HIGHEST,
        preferred_element_type=jnp.float32,
    ).astype(jnp.bfloat16)
    returned = from_behind(halo_grad, "dom", -1)
    own_grad = jnp.einsum(
        "drs,drh->dsh",
        adjacent_local.astype(jnp.float32),
        term_grad,
        precision=lax.Precision.HIGHEST,
        preferred_element_type=jnp.float32,
    )
    scattered = jnp.einsum("dsn,dsh->dnh", slot_hot, returned, preferred_element_type=jnp.float32)
    state_grad = back_days.astype(jnp.float32) + term_grad + own_grad + scattered
    return (state_grad, grad_message, grad_query, grad_key, grad_value)


def solution(mesh):
    return jax.shard_map(
        local,
        mesh=mesh,
        in_specs=(
            P("day", "dom", None),
            P("day", "dom"),
            P("day", "dom"),
            P("day", "dom"),
            P("day", "dom"),
            P(),
            P(),
            P(),
            P(),
            P(None, "dom", "day", None, None),
        ),
        out_specs=(P("day", "dom", None), P(), P(), P(), P()),
        check_vma=False,
    )
```

```python
import jax
import jax.numpy as jnp
from jax import lax
from jax.sharding import PartitionSpec as P

HEADS = 4


def from_behind(value, axis, steps):
    count = lax.axis_size(axis)
    pairs = [(source, (source + steps) % count) for source in range(count)]
    return lax.ppermute(value, axis, pairs)


def _power_of_two(count):
    return count > 0 and count & (count - 1) == 0


def _group_pairs(axis, stride, group, shift):
    pairs = []
    for source in range(lax.axis_size(axis)):
        digit = (source // stride) % group
        pairs.append((source, source + ((digit + shift) % group - digit) * stride))
    return pairs


def _scatter_step(flat, axis, stride, group):
    digit = (lax.axis_index(axis) // stride) % group
    chunks = flat.reshape(group, -1)
    total = lax.dynamic_index_in_dim(chunks, digit, 0, keepdims=False)
    for shift in range(1, group):
        send = lax.dynamic_index_in_dim(chunks, (digit + shift) % group, 0, keepdims=False)
        total = total + lax.ppermute(send, axis, _group_pairs(axis, stride, group, shift))
    return total


def _gather_step(flat, axis, stride, group):
    digit = (lax.axis_index(axis) // stride) % group
    got = [flat] + [
        lax.ppermute(flat, axis, _group_pairs(axis, stride, group, shift)) for shift in range(1, group)
    ]
    stacked = jnp.stack(got)
    order = (digit - jnp.arange(group)) % group
    return jnp.take(stacked, order, axis=0).reshape(-1)


def _factors(size):
    if size <= 4:
        return [size]
    return [2] + _factors(size // 2)


def tree_sum(values, axes):
    sizes = [lax.axis_size(axis) for axis in axes]
    flat = jnp.concatenate([value.reshape(-1) for value in values])
    total = 1
    for size in sizes:
        total *= size
    if not all(_power_of_two(size) for size in sizes) or flat.shape[0] % total:
        return lax.psum(tuple(values), axes)
    steps = []
    for axis, size in zip(axes, sizes):
        stride = 1
        for group in _factors(size):
            if group > 1:
                steps.append((axis, stride, group))
            stride *= group
    for axis, stride, group in steps:
        flat = _scatter_step(flat, axis, stride, group)
    for axis, stride, group in reversed(steps):
        flat = _gather_step(flat, axis, stride, group)
    results, start = [], 0
    for value in values:
        results.append(flat[start : start + value.size].reshape(value.shape))
        start += value.size
    return tuple(results)


def exchange(value, axis, split_axis, concat_axis):
    count = lax.axis_size(axis)
    mine = lax.axis_index(axis)
    pieces = jnp.stack(jnp.split(value, count, axis=split_axis))
    got = []
    for shift in range(count):
        send = lax.dynamic_index_in_dim(pieces, (mine + shift) % count, 0, keepdims=False)
        if shift:
            send = lax.ppermute(send, axis, [(i, (i + shift) % count) for i in range(count)])
        got.append(send)
    stacked = jnp.take(jnp.stack(got), (mine - jnp.arange(count)) % count, axis=0)
    return jnp.concatenate([stacked[k] for k in range(count)], axis=concat_axis)


def adjacency(sources, targets, count_rows, total_rows):
    target_hot = (targets[:, None] == jnp.arange(count_rows, dtype=jnp.int32)[None, :]).astype(
        jnp.bfloat16
    )
    source_hot = (sources[:, None] == jnp.arange(total_rows, dtype=jnp.int32)[None, :]).astype(
        jnp.bfloat16
    )
    counts = lax.dot_general(
        target_hot, source_hot, (((0,), (0,)), ((), ())), preferred_element_type=jnp.float32
    )
    return counts.astype(jnp.bfloat16)


def gnn_forward(states, received, adjacent, w_message):
    extended = jnp.concatenate([states, received], axis=0)
    neighbours = jnp.dot(adjacent, extended, preferred_element_type=jnp.float32)
    counted = jnp.sum(adjacent.astype(jnp.float32), axis=1)
    inverse = 1.0 / (counted + 1.0)
    aggregate = ((states.astype(jnp.float32) + neighbours) * inverse[:, None]).astype(jnp.bfloat16)
    preact = jnp.dot(aggregate, w_message, preferred_element_type=jnp.float32)
    hidden = (states.astype(jnp.float32) + jax.nn.silu(preact)).astype(jnp.bfloat16)
    return (aggregate, preact, inverse, hidden)


def gnn_backward(upstream, aggregate, preact, inverse, adjacent, w_message):
    count_rows = aggregate.shape[0]
    up_float = upstream.astype(jnp.float32)
    sigmoid_val = jax.nn.sigmoid(preact)
    pre_grad = (up_float * sigmoid_val * (1.0 + preact * (1.0 - sigmoid_val))).astype(jnp.bfloat16)
    message_part = lax.dot_general(
        aggregate, pre_grad, (((0,), (0,)), ((), ())), preferred_element_type=jnp.float32
    )
    agg_grad = lax.dot_general(
        pre_grad, w_message, (((1,), (1,)), ((), ())), preferred_element_type=jnp.float32
    )
    term_grad = agg_grad * inverse[:, None]
    ext_grad = lax.dot_general(
        adjacent.astype(jnp.float32),
        term_grad,
        (((0,), (0,)), ((), ())),
        precision=lax.Precision.HIGHEST,
        preferred_element_type=jnp.float32,
    )
    local_grad = up_float + term_grad + ext_grad[:count_rows]
    halo_grad = ext_grad[count_rows:].astype(jnp.bfloat16)
    return (message_part, local_grad, halo_grad)


def attend(states, upstream, w_query, w_key, w_value):
    steps_all, nodes_here, width = states.shape
    head_dim = width // HEADS
    scale_factor = head_dim ** (-0.5)
    flat = states.reshape(steps_all * nodes_here, width)

    def project(weight):
        return jnp.dot(flat, weight, preferred_element_type=jnp.float32).astype(jnp.bfloat16)

    def splitter(matrix):
        return matrix.reshape(steps_all, nodes_here, HEADS, head_dim).astype(jnp.float32)

    queries = project(w_query)
    key_rows = project(w_key)
    value_rows = project(w_value)
    query_f = splitter(queries)
    key_f = splitter(key_rows)
    value_f = splitter(value_rows)
    scores = jnp.einsum("tnhd,snhd->nhts", query_f, key_f) * scale_factor
    causal = jnp.arange(steps_all)[:, None] >= jnp.arange(steps_all)[None, :]
    scores = jnp.where(causal, scores, -jnp.inf)
    highest = jnp.max(scores, axis=-1, keepdims=True)
    exponent = jnp.exp(scores - highest)
    probs = exponent / jnp.sum(exponent, axis=-1, keepdims=True)
    probs_low = probs.astype(jnp.bfloat16).astype(jnp.float32)
    up_heads = splitter(upstream)
    value_grad = jnp.einsum("nhts,tnhd->snhd", probs_low, up_heads).astype(jnp.bfloat16)
    prob_grad = jnp.einsum("tnhd,snhd->nhts", up_heads, value_f)
    score_grad = (
        probs * (prob_grad - jnp.sum(prob_grad * probs, axis=-1, keepdims=True)) * scale_factor
    ).astype(jnp.bfloat16)
    score_f = score_grad.astype(jnp.float32)
    query_grad = jnp.einsum("nhts,snhd->tnhd", score_f, key_f).astype(jnp.bfloat16)
    key_grad = jnp.einsum("nhts,tnhd->snhd", score_f, query_f).astype(jnp.bfloat16)
    query_flat = query_grad.reshape(steps_all * nodes_here, width)
    key_flat = key_grad.reshape(steps_all * nodes_here, width)
    value_flat = value_grad.reshape(steps_all * nodes_here, width)

    def weight_grad(grad_rows):
        return lax.dot_general(
            flat, grad_rows, (((0,), (0,)), ((), ())), preferred_element_type=jnp.float32
        )

    def input_grad(grad_rows, weight):
        return lax.dot_general(
            grad_rows, weight, (((1,), (1,)), ((), ())), preferred_element_type=jnp.float32
        )

    back = upstream.reshape(steps_all * nodes_here, width).astype(jnp.float32)
    back = (
        back
        + input_grad(query_flat, w_query)
        + input_grad(key_flat, w_key)
        + input_grad(value_flat, w_value)
    )
    back = back.astype(jnp.bfloat16).reshape(steps_all, nodes_here, width)
    return ((weight_grad(query_flat), weight_grad(key_flat), weight_grad(value_flat)), back)


def attend_blocked(states, upstream, w_query, w_key, w_value):
    steps_all, nodes_here, width = states.shape
    head_dim = width // HEADS
    scale_factor = head_dim ** (-0.5)
    per_group = max(1, 128 // steps_all)
    if nodes_here % per_group:
        per_group = 1
    groups = nodes_here // per_group
    block = per_group * steps_all
    flat = jnp.swapaxes(states, 0, 1).reshape(nodes_here * steps_all, width)
    up_flat = jnp.swapaxes(upstream, 0, 1).reshape(nodes_here * steps_all, width)

    def project(weight):
        return jnp.dot(flat, weight, preferred_element_type=jnp.float32).astype(jnp.bfloat16)

    def blocks(matrix):
        return matrix.reshape(groups, block, HEADS, head_dim)

    queries = blocks(project(w_query))
    key_rows = blocks(project(w_key))
    value_rows = blocks(project(w_value))
    up_heads = blocks(up_flat)
    position = jnp.arange(block)
    same = (position[:, None] // steps_all) == (position[None, :] // steps_all)
    causal = jnp.logical_and(same, (position[:, None] % steps_all) >= (position[None, :] % steps_all))

    def contract(spec, left, right):
        return jnp.einsum(spec, left, right, preferred_element_type=jnp.float32)

    scores = contract("gihd,gjhd->ghij", queries, key_rows) * scale_factor
    scores = jnp.where(causal, scores, -jnp.inf)
    highest = jnp.max(scores, axis=-1, keepdims=True)
    exponent = jnp.exp(scores - highest)
    probs = exponent / jnp.sum(exponent, axis=-1, keepdims=True)
    probs_low = probs.astype(jnp.bfloat16)
    value_grad = contract("ghij,gihd->gjhd", probs_low, up_heads).astype(jnp.bfloat16)
    prob_grad = contract("gihd,gjhd->ghij", up_heads, value_rows)
    score_grad = (
        probs * (prob_grad - jnp.sum(prob_grad * probs, axis=-1, keepdims=True)) * scale_factor
    ).astype(jnp.bfloat16)
    query_grad = contract("ghij,gjhd->gihd", score_grad, key_rows).astype(jnp.bfloat16)
    key_grad = contract("ghij,gihd->gjhd", score_grad, queries).astype(jnp.bfloat16)
    query_flat = query_grad.reshape(-1, width)
    key_flat = key_grad.reshape(-1, width)
    value_flat = value_grad.reshape(-1, width)

    def weight_grad(grad_rows):
        return lax.dot_general(
            flat, grad_rows, (((0,), (0,)), ((), ())), preferred_element_type=jnp.float32
        )

    def input_grad(grad_rows, weight):
        return lax.dot_general(
            grad_rows, weight, (((1,), (1,)), ((), ())), preferred_element_type=jnp.float32
        )

    back = (
        up_flat.astype(jnp.float32)
        + input_grad(query_flat, w_query)
        + input_grad(key_flat, w_key)
        + input_grad(value_flat, w_value)
    )
    back = jnp.swapaxes(back.astype(jnp.bfloat16).reshape(nodes_here, steps_all, width), 0, 1)
    return ((weight_grad(query_flat), weight_grad(key_flat), weight_grad(value_flat)), back)


def local(
    node_states,
    edge_source,
    edge_target,
    halo_rows,
    halo_count,
    w_message,
    w_query,
    w_key,
    w_value,
    cotangent,
):
    days_local, node_local, width = node_states.shape
    halo_slots = halo_rows.shape[1]
    live = jnp.arange(halo_slots)[None, :] < halo_count
    rows = jnp.arange(node_local, dtype=jnp.int32)
    slot_hot = jnp.logical_and(
        halo_rows[:, :, None] == rows[None, None, :], live[:, :, None]
    ).astype(jnp.bfloat16)
    sent = jnp.einsum(
        "dsn,dnh->dsh", slot_hot, node_states, preferred_element_type=jnp.float32
    ).astype(jnp.bfloat16)
    received = from_behind(sent, "dom", 1)

    target_hot = (edge_target[:, :, None] == rows[None, None, :]).astype(jnp.bfloat16)
    local_hot = (edge_source[:, :, None] == rows[None, None, :]).astype(jnp.bfloat16)
    halo_ids = node_local + jnp.arange(halo_slots, dtype=jnp.int32)
    halo_hot = (edge_source[:, :, None] == halo_ids[None, None, :]).astype(jnp.bfloat16)
    adjacent_local = jnp.einsum(
        "der,des->drs", target_hot, local_hot, preferred_element_type=jnp.float32
    ).astype(jnp.bfloat16)
    adjacent_halo = jnp.einsum(
        "der,des->drs", target_hot, halo_hot, preferred_element_type=jnp.float32
    ).astype(jnp.bfloat16)
    counted = jnp.sum(target_hot.astype(jnp.float32), axis=1)
    inverse = 1.0 / (counted + 1.0)

    states_f = node_states.astype(jnp.float32)
    neighbours = jnp.einsum(
        "drs,dsh->drh", adjacent_local, node_states, preferred_element_type=jnp.float32
    ) + jnp.einsum("drs,dsh->drh", adjacent_halo, received, preferred_element_type=jnp.float32)
    aggregate = ((states_f + neighbours) * inverse[:, :, None]).astype(jnp.bfloat16)
    preact = jnp.einsum("drh,hk->drk", aggregate, w_message, preferred_element_type=jnp.float32)
    hidden = (states_f + jax.nn.silu(preact)).astype(jnp.bfloat16)

    node_major = exchange(hidden, "day", 1, 0)
    upstream = cotangent.reshape(cotangent.shape[0], -1, width)
    attn_grads, back = attend_blocked(node_major, upstream, w_query, w_key, w_value)
    back_days = exchange(back, "day", 0, 1)

    sigmoid_val = jax.nn.sigmoid(preact)
    pre_grad = (
        back_days.astype(jnp.float32) * sigmoid_val * (1.0 + preact * (1.0 - sigmoid_val))
    ).astype(jnp.bfloat16)
    grad_message = lax.dot_general(
        aggregate.reshape(-1, width),
        pre_grad.reshape(-1, width),
        (((0,), (0,)), ((), ())),
        preferred_element_type=jnp.float32,
    )
    grad_message, grad_query, grad_key, grad_value = tree_sum(
        (grad_message, attn_grads[0], attn_grads[1], attn_grads[2]), ("dom", "day")
    )
    agg_grad = jnp.einsum("drk,hk->drh", pre_grad, w_message, preferred_element_type=jnp.float32)
    term_grad = agg_grad * inverse[:, :, None]
    halo_grad = jnp.einsum(
        "drs,drh->dsh",
        adjacent_halo.astype(jnp.float32),
        term_grad,
        precision=lax.Precision.HIGHEST,
        preferred_element_type=jnp.float32,
    ).astype(jnp.bfloat16)
    returned = from_behind(halo_grad, "dom", -1)
    own_grad = jnp.einsum(
        "drs,drh->dsh",
        adjacent_local.astype(jnp.float32),
        term_grad,
        precision=lax.Precision.HIGHEST,
        preferred_element_type=jnp.float32,
    )
    scattered = jnp.einsum("dsn,dsh->dnh", slot_hot, returned, preferred_element_type=jnp.float32)
    state_grad = back_days.astype(jnp.float32) + term_grad + own_grad + scattered
    return (state_grad, grad_message, grad_query, grad_key, grad_value)


def solution(mesh):
    return jax.shard_map(
        local,
        mesh=mesh,
        in_specs=(
            P("day", "dom", None),
            P("day", "dom"),
            P("day", "dom"),
            P("day", "dom"),
            P("day", "dom"),
            P(),
            P(),
            P(),
            P(),
            P(None, "dom", "day", None, None),
        ),
        out_specs=(P("day", "dom", None), P(), P(), P(), P()),
        check_vma=False,
    )
```

```python
import jax
import jax.numpy as jnp
from jax import lax
from jax.sharding import PartitionSpec as P

HEADS = 4


def from_behind(value, axis, steps):
    count = lax.axis_size(axis)
    pairs = [(source, (source + steps) % count) for source in range(count)]
    return lax.ppermute(value, axis, pairs)


def _power_of_two(count):
    return count > 0 and count & (count - 1) == 0


def _group_pairs(axis, stride, group, shift):
    pairs = []
    for source in range(lax.axis_size(axis)):
        digit = (source // stride) % group
        pairs.append((source, source + ((digit + shift) % group - digit) * stride))
    return pairs


def _scatter_step(flat, axis, stride, group):
    digit = (lax.axis_index(axis) // stride) % group
    chunks = flat.reshape(group, -1)
    total = lax.dynamic_index_in_dim(chunks, digit, 0, keepdims=False)
    for shift in range(1, group):
        send = lax.dynamic_index_in_dim(chunks, (digit + shift) % group, 0, keepdims=False)
        total = total + lax.ppermute(send, axis, _group_pairs(axis, stride, group, shift))
    return total


def _gather_step(flat, axis, stride, group):
    digit = (lax.axis_index(axis) // stride) % group
    got = [flat] + [
        lax.ppermute(flat, axis, _group_pairs(axis, stride, group, shift)) for shift in range(1, group)
    ]
    stacked = jnp.stack(got)
    order = (digit - jnp.arange(group)) % group
    return jnp.take(stacked, order, axis=0).reshape(-1)


def _factors(size):
    if size <= 4:
        return [size]
    return [2] + _factors(size // 2)


def tree_sum(values, axes):
    sizes = [lax.axis_size(axis) for axis in axes]
    flat = jnp.concatenate([value.reshape(-1) for value in values])
    total = 1
    for size in sizes:
        total *= size
    if not all(_power_of_two(size) for size in sizes) or flat.shape[0] % total:
        return lax.psum(tuple(values), axes)
    steps = []
    for axis, size in zip(axes, sizes):
        stride = 1
        for group in _factors(size):
            if group > 1:
                steps.append((axis, stride, group))
            stride *= group
    for axis, stride, group in steps:
        flat = _scatter_step(flat, axis, stride, group)
    for axis, stride, group in reversed(steps):
        flat = _gather_step(flat, axis, stride, group)
    results, start = [], 0
    for value in values:
        results.append(flat[start : start + value.size].reshape(value.shape))
        start += value.size
    return tuple(results)


def exchange(value, axis, split_axis, concat_axis):
    count = lax.axis_size(axis)
    mine = lax.axis_index(axis)
    pieces = jnp.stack(jnp.split(value, count, axis=split_axis))
    got = []
    for shift in range(count):
        send = lax.dynamic_index_in_dim(pieces, (mine + shift) % count, 0, keepdims=False)
        if shift:
            send = lax.ppermute(send, axis, [(i, (i + shift) % count) for i in range(count)])
        got.append(send)
    stacked = jnp.take(jnp.stack(got), (mine - jnp.arange(count)) % count, axis=0)
    return jnp.concatenate([stacked[k] for k in range(count)], axis=concat_axis)


def adjacency(sources, targets, count_rows, total_rows):
    target_hot = (targets[:, None] == jnp.arange(count_rows, dtype=jnp.int32)[None, :]).astype(
        jnp.bfloat16
    )
    source_hot = (sources[:, None] == jnp.arange(total_rows, dtype=jnp.int32)[None, :]).astype(
        jnp.bfloat16
    )
    counts = lax.dot_general(
        target_hot, source_hot, (((0,), (0,)), ((), ())), preferred_element_type=jnp.float32
    )
    return counts.astype(jnp.bfloat16)


def gnn_forward(states, received, adjacent, w_message):
    extended = jnp.concatenate([states, received], axis=0)
    neighbours = jnp.dot(adjacent, extended, preferred_element_type=jnp.float32)
    counted = jnp.sum(adjacent.astype(jnp.float32), axis=1)
    inverse = 1.0 / (counted + 1.0)
    aggregate = ((states.astype(jnp.float32) + neighbours) * inverse[:, None]).astype(jnp.bfloat16)
    preact = jnp.dot(aggregate, w_message, preferred_element_type=jnp.float32)
    hidden = (states.astype(jnp.float32) + jax.nn.silu(preact)).astype(jnp.bfloat16)
    return (aggregate, preact, inverse, hidden)


def gnn_backward(upstream, aggregate, preact, inverse, adjacent, w_message):
    count_rows = aggregate.shape[0]
    up_float = upstream.astype(jnp.float32)
    sigmoid_val = jax.nn.sigmoid(preact)
    pre_grad = (up_float * sigmoid_val * (1.0 + preact * (1.0 - sigmoid_val))).astype(jnp.bfloat16)
    message_part = lax.dot_general(
        aggregate, pre_grad, (((0,), (0,)), ((), ())), preferred_element_type=jnp.float32
    )
    agg_grad = lax.dot_general(
        pre_grad, w_message, (((1,), (1,)), ((), ())), preferred_element_type=jnp.float32
    )
    term_grad = agg_grad * inverse[:, None]
    ext_grad = lax.dot_general(
        adjacent.astype(jnp.float32),
        term_grad,
        (((0,), (0,)), ((), ())),
        precision=lax.Precision.HIGHEST,
        preferred_element_type=jnp.float32,
    )
    local_grad = up_float + term_grad + ext_grad[:count_rows]
    halo_grad = ext_grad[count_rows:].astype(jnp.bfloat16)
    return (message_part, local_grad, halo_grad)


def attend(states, upstream, w_query, w_key, w_value):
    steps_all, nodes_here, width = states.shape
    head_dim = width // HEADS
    scale_factor = head_dim ** (-0.5)
    flat = states.reshape(steps_all * nodes_here, width)

    def project(weight):
        return jnp.dot(flat, weight, preferred_element_type=jnp.float32).astype(jnp.bfloat16)

    def splitter(matrix):
        return matrix.reshape(steps_all, nodes_here, HEADS, head_dim).astype(jnp.float32)

    queries = project(w_query)
    key_rows = project(w_key)
    value_rows = project(w_value)
    query_f = splitter(queries)
    key_f = splitter(key_rows)
    value_f = splitter(value_rows)
    scores = jnp.einsum("tnhd,snhd->nhts", query_f, key_f) * scale_factor
    causal = jnp.arange(steps_all)[:, None] >= jnp.arange(steps_all)[None, :]
    scores = jnp.where(causal, scores, -jnp.inf)
    highest = jnp.max(scores, axis=-1, keepdims=True)
    exponent = jnp.exp(scores - highest)
    probs = exponent / jnp.sum(exponent, axis=-1, keepdims=True)
    probs_low = probs.astype(jnp.bfloat16).astype(jnp.float32)
    up_heads = splitter(upstream)
    value_grad = jnp.einsum("nhts,tnhd->snhd", probs_low, up_heads).astype(jnp.bfloat16)
    prob_grad = jnp.einsum("tnhd,snhd->nhts", up_heads, value_f)
    score_grad = (
        probs * (prob_grad - jnp.sum(prob_grad * probs, axis=-1, keepdims=True)) * scale_factor
    ).astype(jnp.bfloat16)
    score_f = score_grad.astype(jnp.float32)
    query_grad = jnp.einsum("nhts,snhd->tnhd", score_f, key_f).astype(jnp.bfloat16)
    key_grad = jnp.einsum("nhts,tnhd->snhd", score_f, query_f).astype(jnp.bfloat16)
    query_flat = query_grad.reshape(steps_all * nodes_here, width)
    key_flat = key_grad.reshape(steps_all * nodes_here, width)
    value_flat = value_grad.reshape(steps_all * nodes_here, width)

    def weight_grad(grad_rows):
        return lax.dot_general(
            flat, grad_rows, (((0,), (0,)), ((), ())), preferred_element_type=jnp.float32
        )

    def input_grad(grad_rows, weight):
        return lax.dot_general(
            grad_rows, weight, (((1,), (1,)), ((), ())), preferred_element_type=jnp.float32
        )

    back = upstream.reshape(steps_all * nodes_here, width).astype(jnp.float32)
    back = (
        back
        + input_grad(query_flat, w_query)
        + input_grad(key_flat, w_key)
        + input_grad(value_flat, w_value)
    )
    back = back.astype(jnp.bfloat16).reshape(steps_all, nodes_here, width)
    return ((weight_grad(query_flat), weight_grad(key_flat), weight_grad(value_flat)), back)


def attend_blocked(states, upstream, w_query, w_key, w_value):
    steps_all, nodes_here, width = states.shape
    head_dim = width // HEADS
    scale_factor = head_dim ** (-0.5)
    per_group = max(1, 128 // steps_all)
    if nodes_here % per_group:
        per_group = 1
    groups = nodes_here // per_group
    block = per_group * steps_all
    flat = jnp.swapaxes(states, 0, 1).reshape(nodes_here * steps_all, width)
    up_flat = jnp.swapaxes(upstream, 0, 1).reshape(nodes_here * steps_all, width)

    def project(weight):
        return jnp.dot(flat, weight, preferred_element_type=jnp.float32).astype(jnp.bfloat16)

    def blocks(matrix):
        return matrix.reshape(groups, block, HEADS, head_dim)

    queries = blocks(project(w_query))
    key_rows = blocks(project(w_key))
    value_rows = blocks(project(w_value))
    up_heads = blocks(up_flat)
    position = jnp.arange(block)
    same = (position[:, None] // steps_all) == (position[None, :] // steps_all)
    causal = jnp.logical_and(same, (position[:, None] % steps_all) >= (position[None, :] % steps_all))

    def contract(spec, left, right):
        return jnp.einsum(spec, left, right, preferred_element_type=jnp.float32)

    scores = contract("gihd,gjhd->ghij", queries, key_rows) * scale_factor
    scores = jnp.where(causal, scores, -jnp.inf)
    highest = jnp.max(scores, axis=-1, keepdims=True)
    exponent = jnp.exp(scores - highest)
    probs = exponent / jnp.sum(exponent, axis=-1, keepdims=True)
    probs_low = probs.astype(jnp.bfloat16)
    value_grad = contract("ghij,gihd->gjhd", probs_low, up_heads).astype(jnp.bfloat16)
    prob_grad = contract("gihd,gjhd->ghij", up_heads, value_rows)
    score_grad = (
        probs * (prob_grad - jnp.sum(prob_grad * probs, axis=-1, keepdims=True)) * scale_factor
    ).astype(jnp.bfloat16)
    query_grad = contract("ghij,gjhd->gihd", score_grad, key_rows).astype(jnp.bfloat16)
    key_grad = contract("ghij,gihd->gjhd", score_grad, queries).astype(jnp.bfloat16)
    query_flat = query_grad.reshape(-1, width)
    key_flat = key_grad.reshape(-1, width)
    value_flat = value_grad.reshape(-1, width)

    def weight_grad(grad_rows):
        return lax.dot_general(
            flat, grad_rows, (((0,), (0,)), ((), ())), preferred_element_type=jnp.float32
        )

    def input_grad(grad_rows, weight):
        return lax.dot_general(
            grad_rows, weight, (((1,), (1,)), ((), ())), preferred_element_type=jnp.float32
        )

    back = (
        up_flat.astype(jnp.float32)
        + input_grad(query_flat, w_query)
        + input_grad(key_flat, w_key)
        + input_grad(value_flat, w_value)
    )
    back = jnp.swapaxes(back.astype(jnp.bfloat16).reshape(nodes_here, steps_all, width), 0, 1)
    return ((weight_grad(query_flat), weight_grad(key_flat), weight_grad(value_flat)), back)


def local(
    node_states,
    edge_source,
    edge_target,
    halo_rows,
    halo_count,
    w_message,
    w_query,
    w_key,
    w_value,
    cotangent,
):
    days_local, node_local, width = node_states.shape
    halo_slots = halo_rows.shape[1]
    live = jnp.arange(halo_slots)[None, :] < halo_count
    rows = jnp.arange(node_local, dtype=jnp.int32)
    slot_hot = jnp.logical_and(
        halo_rows[:, :, None] == rows[None, None, :], live[:, :, None]
    ).astype(jnp.bfloat16)
    sent = jnp.einsum(
        "dsn,dnh->dsh", slot_hot, node_states, preferred_element_type=jnp.float32
    ).astype(jnp.bfloat16)
    received = from_behind(sent, "dom", 1)

    target_hot = (edge_target[:, :, None] == rows[None, None, :]).astype(jnp.bfloat16)
    local_hot = (edge_source[:, :, None] == rows[None, None, :]).astype(jnp.bfloat16)
    halo_ids = node_local + jnp.arange(halo_slots, dtype=jnp.int32)
    halo_hot = (edge_source[:, :, None] == halo_ids[None, None, :]).astype(jnp.bfloat16)
    adjacent_local = jnp.einsum(
        "der,des->drs", target_hot, local_hot, preferred_element_type=jnp.float32
    ).astype(jnp.bfloat16)
    adjacent_halo = jnp.einsum(
        "der,des->drs", target_hot, halo_hot, preferred_element_type=jnp.float32
    ).astype(jnp.bfloat16)
    counted = jnp.sum(target_hot.astype(jnp.float32), axis=1)
    inverse = 1.0 / (counted + 1.0)

    states_f = node_states.astype(jnp.float32)
    neighbours = jnp.einsum(
        "drs,dsh->drh", adjacent_local, node_states, preferred_element_type=jnp.float32
    ) + jnp.einsum("drs,dsh->drh", adjacent_halo, received, preferred_element_type=jnp.float32)
    aggregate = ((states_f + neighbours) * inverse[:, :, None]).astype(jnp.bfloat16)
    preact = jnp.einsum("drh,hk->drk", aggregate, w_message, preferred_element_type=jnp.float32)
    hidden = (states_f + jax.nn.silu(preact)).astype(jnp.bfloat16)

    node_major = exchange(hidden, "day", 1, 0)
    upstream = cotangent.reshape(cotangent.shape[0], -1, width)
    attn_grads, back = attend_blocked(node_major, upstream, w_query, w_key, w_value)
    grad_query, grad_key, grad_value = tree_sum(attn_grads, ("dom", "day"))
    back_days = exchange(back, "day", 0, 1)

    sigmoid_val = jax.nn.sigmoid(preact)
    pre_grad = (
        back_days.astype(jnp.float32) * sigmoid_val * (1.0 + preact * (1.0 - sigmoid_val))
    ).astype(jnp.bfloat16)
    grad_message = lax.dot_general(
        aggregate.reshape(-1, width),
        pre_grad.reshape(-1, width),
        (((0,), (0,)), ((), ())),
        preferred_element_type=jnp.float32,
    )
    (grad_message,) = tree_sum((grad_message,), ("dom", "day"))
    agg_grad = jnp.einsum("drk,hk->drh", pre_grad, w_message, preferred_element_type=jnp.float32)
    term_grad = agg_grad * inverse[:, :, None]
    halo_grad = jnp.einsum(
        "drs,drh->dsh",
        adjacent_halo.astype(jnp.float32),
        term_grad,
        precision=lax.Precision.HIGHEST,
        preferred_element_type=jnp.float32,
    ).astype(jnp.bfloat16)
    returned = from_behind(halo_grad, "dom", -1)
    own_grad = jnp.einsum(
        "drs,drh->dsh",
        adjacent_local.astype(jnp.float32),
        term_grad,
        precision=lax.Precision.HIGHEST,
        preferred_element_type=jnp.float32,
    )
    scattered = jnp.einsum("dsn,dsh->dnh", slot_hot, returned, preferred_element_type=jnp.float32)
    state_grad = back_days.astype(jnp.float32) + term_grad + own_grad + scattered
    return (state_grad, grad_message, grad_query, grad_key, grad_value)


def solution(mesh):
    return jax.shard_map(
        local,
        mesh=mesh,
        in_specs=(
            P("day", "dom", None),
            P("day", "dom"),
            P("day", "dom"),
            P("day", "dom"),
            P("day", "dom"),
            P(),
            P(),
            P(),
            P(),
            P(None, "dom", "day", None, None),
        ),
        out_specs=(P("day", "dom", None), P(), P(), P(), P()),
        check_vma=False,
    )
```

```python
import jax
import jax.numpy as jnp
from jax import lax
from jax.sharding import PartitionSpec as P

HEADS = 4


def from_behind(value, axis, steps):
    count = lax.axis_size(axis)
    pairs = [(source, (source + steps) % count) for source in range(count)]
    return lax.ppermute(value, axis, pairs)


def _power_of_two(count):
    return count > 0 and count & (count - 1) == 0


def _group_pairs(axis, stride, group, shift):
    pairs = []
    for source in range(lax.axis_size(axis)):
        digit = (source // stride) % group
        pairs.append((source, source + ((digit + shift) % group - digit) * stride))
    return pairs


def _scatter_step(flat, axis, stride, group):
    digit = (lax.axis_index(axis) // stride) % group
    chunks = flat.reshape(group, -1)
    total = lax.dynamic_index_in_dim(chunks, digit, 0, keepdims=False)
    for shift in range(1, group):
        send = lax.dynamic_index_in_dim(chunks, (digit + shift) % group, 0, keepdims=False)
        total = total + lax.ppermute(send, axis, _group_pairs(axis, stride, group, shift))
    return total


def _by_source(got, digit):
    group = len(got)
    turned = jnp.stack([got[0]] + got[:0:-1] + [got[0]] + got[:0:-1])
    return lax.dynamic_slice_in_dim(turned, group - digit, group, axis=0)


def _gather_step(flat, axis, stride, group):
    digit = (lax.axis_index(axis) // stride) % group
    got = [flat] + [
        lax.ppermute(flat, axis, _group_pairs(axis, stride, group, shift)) for shift in range(1, group)
    ]
    return _by_source(got, digit).reshape(-1)


def _reduce_step(flat, axis, stride, group):
    digit = (lax.axis_index(axis) // stride) % group
    got = [flat] + [
        lax.ppermute(flat, axis, _group_pairs(axis, stride, group, shift)) for shift in range(1, group)
    ]
    ordered = _by_source(got, digit)
    total = ordered[0]
    for source in range(1, group):
        total = total + ordered[source]
    return total


def _factors(size):
    if size <= 4:
        return [size]
    return [2] + _factors(size // 2)


def tree_sum(values, axes):
    sizes = [lax.axis_size(axis) for axis in axes]
    flat = jnp.concatenate([value.reshape(-1) for value in values])
    total = 1
    for size in sizes:
        total *= size
    if not all(_power_of_two(size) for size in sizes) or flat.shape[0] % total:
        return lax.psum(tuple(values), axes)
    steps = []
    for axis, size in zip(axes, sizes):
        stride = 1
        for group in _factors(size):
            if group > 1:
                steps.append((axis, stride, group))
            stride *= group
    for axis, stride, group in steps[:-1]:
        flat = _scatter_step(flat, axis, stride, group)
    flat = _reduce_step(flat, *steps[-1])
    for axis, stride, group in reversed(steps[:-1]):
        flat = _gather_step(flat, axis, stride, group)
    results, start = [], 0
    for value in values:
        results.append(flat[start : start + value.size].reshape(value.shape))
        start += value.size
    return tuple(results)


def exchange(value, axis, split_axis, concat_axis):
    count = lax.axis_size(axis)
    mine = lax.axis_index(axis)
    pieces = jnp.stack(jnp.split(value, count, axis=split_axis))
    got = []
    for shift in range(count):
        send = lax.dynamic_index_in_dim(pieces, (mine + shift) % count, 0, keepdims=False)
        if shift:
            send = lax.ppermute(send, axis, [(i, (i + shift) % count) for i in range(count)])
        got.append(send)
    stacked = _by_source(got, mine)
    return jnp.concatenate([stacked[k] for k in range(count)], axis=concat_axis)


def adjacency(sources, targets, count_rows, total_rows):
    target_hot = (targets[:, None] == jnp.arange(count_rows, dtype=jnp.int32)[None, :]).astype(
        jnp.bfloat16
    )
    source_hot = (sources[:, None] == jnp.arange(total_rows, dtype=jnp.int32)[None, :]).astype(
        jnp.bfloat16
    )
    counts = lax.dot_general(
        target_hot, source_hot, (((0,), (0,)), ((), ())), preferred_element_type=jnp.float32
    )
    return counts.astype(jnp.bfloat16)


def gnn_forward(states, received, adjacent, w_message):
    extended = jnp.concatenate([states, received], axis=0)
    neighbours = jnp.dot(adjacent, extended, preferred_element_type=jnp.float32)
    counted = jnp.sum(adjacent.astype(jnp.float32), axis=1)
    inverse = 1.0 / (counted + 1.0)
    aggregate = ((states.astype(jnp.float32) + neighbours) * inverse[:, None]).astype(jnp.bfloat16)
    preact = jnp.dot(aggregate, w_message, preferred_element_type=jnp.float32)
    hidden = (states.astype(jnp.float32) + jax.nn.silu(preact)).astype(jnp.bfloat16)
    return (aggregate, preact, inverse, hidden)


def gnn_backward(upstream, aggregate, preact, inverse, adjacent, w_message):
    count_rows = aggregate.shape[0]
    up_float = upstream.astype(jnp.float32)
    sigmoid_val = jax.nn.sigmoid(preact)
    pre_grad = (up_float * sigmoid_val * (1.0 + preact * (1.0 - sigmoid_val))).astype(jnp.bfloat16)
    message_part = lax.dot_general(
        aggregate, pre_grad, (((0,), (0,)), ((), ())), preferred_element_type=jnp.float32
    )
    agg_grad = lax.dot_general(
        pre_grad, w_message, (((1,), (1,)), ((), ())), preferred_element_type=jnp.float32
    )
    term_grad = agg_grad * inverse[:, None]
    ext_grad = lax.dot_general(
        adjacent.astype(jnp.float32),
        term_grad,
        (((0,), (0,)), ((), ())),
        precision=lax.Precision.HIGHEST,
        preferred_element_type=jnp.float32,
    )
    local_grad = up_float + term_grad + ext_grad[:count_rows]
    halo_grad = ext_grad[count_rows:].astype(jnp.bfloat16)
    return (message_part, local_grad, halo_grad)


def attend(states, upstream, w_query, w_key, w_value):
    steps_all, nodes_here, width = states.shape
    head_dim = width // HEADS
    scale_factor = head_dim ** (-0.5)
    flat = states.reshape(steps_all * nodes_here, width)

    def project(weight):
        return jnp.dot(flat, weight, preferred_element_type=jnp.float32).astype(jnp.bfloat16)

    def splitter(matrix):
        return matrix.reshape(steps_all, nodes_here, HEADS, head_dim).astype(jnp.float32)

    queries = project(w_query)
    key_rows = project(w_key)
    value_rows = project(w_value)
    query_f = splitter(queries)
    key_f = splitter(key_rows)
    value_f = splitter(value_rows)
    scores = jnp.einsum("tnhd,snhd->nhts", query_f, key_f) * scale_factor
    causal = jnp.arange(steps_all)[:, None] >= jnp.arange(steps_all)[None, :]
    scores = jnp.where(causal, scores, -jnp.inf)
    highest = jnp.max(scores, axis=-1, keepdims=True)
    exponent = jnp.exp(scores - highest)
    probs = exponent / jnp.sum(exponent, axis=-1, keepdims=True)
    probs_low = probs.astype(jnp.bfloat16).astype(jnp.float32)
    up_heads = splitter(upstream)
    value_grad = jnp.einsum("nhts,tnhd->snhd", probs_low, up_heads).astype(jnp.bfloat16)
    prob_grad = jnp.einsum("tnhd,snhd->nhts", up_heads, value_f)
    score_grad = (
        probs * (prob_grad - jnp.sum(prob_grad * probs, axis=-1, keepdims=True)) * scale_factor
    ).astype(jnp.bfloat16)
    score_f = score_grad.astype(jnp.float32)
    query_grad = jnp.einsum("nhts,snhd->tnhd", score_f, key_f).astype(jnp.bfloat16)
    key_grad = jnp.einsum("nhts,tnhd->snhd", score_f, query_f).astype(jnp.bfloat16)
    query_flat = query_grad.reshape(steps_all * nodes_here, width)
    key_flat = key_grad.reshape(steps_all * nodes_here, width)
    value_flat = value_grad.reshape(steps_all * nodes_here, width)

    def weight_grad(grad_rows):
        return lax.dot_general(
            flat, grad_rows, (((0,), (0,)), ((), ())), preferred_element_type=jnp.float32
        )

    def input_grad(grad_rows, weight):
        return lax.dot_general(
            grad_rows, weight, (((1,), (1,)), ((), ())), preferred_element_type=jnp.float32
        )

    back = upstream.reshape(steps_all * nodes_here, width).astype(jnp.float32)
    back = (
        back
        + input_grad(query_flat, w_query)
        + input_grad(key_flat, w_key)
        + input_grad(value_flat, w_value)
    )
    back = back.astype(jnp.bfloat16).reshape(steps_all, nodes_here, width)
    return ((weight_grad(query_flat), weight_grad(key_flat), weight_grad(value_flat)), back)


def attend_blocked(states, upstream, w_query, w_key, w_value):
    steps_all, nodes_here, width = states.shape
    head_dim = width // HEADS
    scale_factor = head_dim ** (-0.5)
    per_group = max(1, 128 // steps_all)
    if nodes_here % per_group:
        per_group = 1
    groups = nodes_here // per_group
    block = per_group * steps_all
    flat = jnp.swapaxes(states, 0, 1).reshape(nodes_here * steps_all, width)
    up_flat = jnp.swapaxes(upstream, 0, 1).reshape(nodes_here * steps_all, width)

    def project(weight):
        return jnp.dot(flat, weight, preferred_element_type=jnp.float32).astype(jnp.bfloat16)

    def blocks(matrix):
        return matrix.reshape(groups, block, HEADS, head_dim)

    queries = blocks(project(w_query))
    key_rows = blocks(project(w_key))
    value_rows = blocks(project(w_value))
    up_heads = blocks(up_flat)
    position = jnp.arange(block)
    same = (position[:, None] // steps_all) == (position[None, :] // steps_all)
    causal = jnp.logical_and(same, (position[:, None] % steps_all) >= (position[None, :] % steps_all))

    def contract(spec, left, right):
        return jnp.einsum(spec, left, right, preferred_element_type=jnp.float32)

    scores = contract("gihd,gjhd->ghij", queries, key_rows) * scale_factor
    scores = jnp.where(causal, scores, -jnp.inf)
    highest = jnp.max(scores, axis=-1, keepdims=True)
    exponent = jnp.exp(scores - highest)
    probs = exponent / jnp.sum(exponent, axis=-1, keepdims=True)
    probs_low = probs.astype(jnp.bfloat16)
    value_grad = contract("ghij,gihd->gjhd", probs_low, up_heads).astype(jnp.bfloat16)
    prob_grad = contract("gihd,gjhd->ghij", up_heads, value_rows)
    score_grad = (
        probs * (prob_grad - jnp.sum(prob_grad * probs, axis=-1, keepdims=True)) * scale_factor
    ).astype(jnp.bfloat16)
    score_grad = lax.optimization_barrier(score_grad)
    query_grad = contract("ghij,gjhd->gihd", score_grad, key_rows).astype(jnp.bfloat16)
    key_grad = contract("ghij,gihd->gjhd", score_grad, queries).astype(jnp.bfloat16)
    query_flat = query_grad.reshape(-1, width)
    key_flat = key_grad.reshape(-1, width)
    value_flat = value_grad.reshape(-1, width)

    def weight_grad(grad_rows):
        return lax.dot_general(
            flat, grad_rows, (((0,), (0,)), ((), ())), preferred_element_type=jnp.float32
        )

    def input_grad(grad_rows, weight):
        return lax.dot_general(
            grad_rows, weight, (((1,), (1,)), ((), ())), preferred_element_type=jnp.float32
        )

    back = (
        up_flat.astype(jnp.float32)
        + input_grad(query_flat, w_query)
        + input_grad(key_flat, w_key)
        + input_grad(value_flat, w_value)
    )
    back = jnp.swapaxes(back.astype(jnp.bfloat16).reshape(nodes_here, steps_all, width), 0, 1)
    return ((weight_grad(query_flat), weight_grad(key_flat), weight_grad(value_flat)), back)


def local(
    node_states,
    edge_source,
    edge_target,
    halo_rows,
    halo_count,
    w_message,
    w_query,
    w_key,
    w_value,
    cotangent,
):
    days_local, node_local, width = node_states.shape
    halo_slots = halo_rows.shape[1]
    live = jnp.arange(halo_slots)[None, :] < halo_count
    rows = jnp.arange(node_local, dtype=jnp.int32)
    slot_hot = jnp.logical_and(
        halo_rows[:, :, None] == rows[None, None, :], live[:, :, None]
    ).astype(jnp.bfloat16)
    sent = jnp.einsum(
        "dsn,dnh->dsh", slot_hot, node_states, preferred_element_type=jnp.float32
    ).astype(jnp.bfloat16)
    received = from_behind(sent, "dom", 1)

    target_hot = (edge_target[:, :, None] == rows[None, None, :]).astype(jnp.bfloat16)
    local_hot = (edge_source[:, :, None] == rows[None, None, :]).astype(jnp.bfloat16)
    halo_ids = node_local + jnp.arange(halo_slots, dtype=jnp.int32)
    halo_hot = (edge_source[:, :, None] == halo_ids[None, None, :]).astype(jnp.bfloat16)
    adjacent_local = jnp.einsum(
        "der,des->drs", target_hot, local_hot, preferred_element_type=jnp.float32
    ).astype(jnp.bfloat16)
    adjacent_halo = jnp.einsum(
        "der,des->drs", target_hot, halo_hot, preferred_element_type=jnp.float32
    ).astype(jnp.bfloat16)
    counted = jnp.sum(target_hot.astype(jnp.float32), axis=1)
    inverse = 1.0 / (counted + 1.0)

    states_f = node_states.astype(jnp.float32)
    neighbours = jnp.einsum(
        "drs,dsh->drh", adjacent_local, node_states, preferred_element_type=jnp.float32
    ) + jnp.einsum("drs,dsh->drh", adjacent_halo, received, preferred_element_type=jnp.float32)
    aggregate = ((states_f + neighbours) * inverse[:, :, None]).astype(jnp.bfloat16)
    preact = jnp.einsum("drh,hk->drk", aggregate, w_message, preferred_element_type=jnp.float32)
    hidden = (states_f + jax.nn.silu(preact)).astype(jnp.bfloat16)

    node_major = exchange(hidden, "day", 1, 0)
    upstream = cotangent.reshape(cotangent.shape[0], -1, width)
    attn_grads, back = attend_blocked(node_major, upstream, w_query, w_key, w_value)
    back_days = exchange(back, "day", 0, 1)

    sigmoid_val = jax.nn.sigmoid(preact)
    pre_grad = (
        back_days.astype(jnp.float32) * sigmoid_val * (1.0 + preact * (1.0 - sigmoid_val))
    ).astype(jnp.bfloat16)
    grad_message = lax.dot_general(
        aggregate.reshape(-1, width),
        pre_grad.reshape(-1, width),
        (((0,), (0,)), ((), ())),
        preferred_element_type=jnp.float32,
    )
    grad_message, grad_query, grad_key, grad_value = tree_sum(
        (grad_message, attn_grads[0], attn_grads[1], attn_grads[2]), ("dom", "day")
    )
    agg_grad = jnp.einsum("drk,hk->drh", pre_grad, w_message, preferred_element_type=jnp.float32)
    term_grad = agg_grad * inverse[:, :, None]
    halo_grad = jnp.einsum(
        "drs,drh->dsh",
        adjacent_halo.astype(jnp.float32),
        term_grad,
        precision=lax.Precision.HIGHEST,
        preferred_element_type=jnp.float32,
    ).astype(jnp.bfloat16)
    returned = from_behind(halo_grad, "dom", -1)
    own_grad = jnp.einsum(
        "drs,drh->dsh",
        adjacent_local.astype(jnp.float32),
        term_grad,
        precision=lax.Precision.HIGHEST,
        preferred_element_type=jnp.float32,
    )
    scattered = jnp.einsum("dsn,dsh->dnh", slot_hot, returned, preferred_element_type=jnp.float32)
    state_grad = back_days.astype(jnp.float32) + term_grad + own_grad + scattered
    return (state_grad, grad_message, grad_query, grad_key, grad_value)


def solution(mesh):
    return jax.shard_map(
        local,
        mesh=mesh,
        in_specs=(
            P("day", "dom", None),
            P("day", "dom"),
            P("day", "dom"),
            P("day", "dom"),
            P("day", "dom"),
            P(),
            P(),
            P(),
            P(),
            P(None, "dom", "day", None, None),
        ),
        out_specs=(P("day", "dom", None), P(), P(), P(), P()),
        check_vma=False,
    )
```

```python
import jax
import jax.numpy as jnp
from jax import lax
from jax.sharding import PartitionSpec as P

HEADS = 4


def from_behind(value, axis, steps):
    count = lax.axis_size(axis)
    pairs = [(source, (source + steps) % count) for source in range(count)]
    return lax.ppermute(value, axis, pairs)


def _power_of_two(count):
    return count > 0 and count & (count - 1) == 0


def _group_pairs(axis, stride, group, shift):
    pairs = []
    for source in range(lax.axis_size(axis)):
        digit = (source // stride) % group
        pairs.append((source, source + ((digit + shift) % group - digit) * stride))
    return pairs


def _scatter_step(flat, axis, stride, group):
    digit = (lax.axis_index(axis) // stride) % group
    chunks = flat.reshape(group, -1)
    total = lax.dynamic_index_in_dim(chunks, digit, 0, keepdims=False)
    for shift in range(1, group):
        send = lax.dynamic_index_in_dim(chunks, (digit + shift) % group, 0, keepdims=False)
        total = total + lax.ppermute(send, axis, _group_pairs(axis, stride, group, shift))
    return total


def _gather_step(flat, axis, stride, group):
    digit = (lax.axis_index(axis) // stride) % group
    got = [flat] + [
        lax.ppermute(flat, axis, _group_pairs(axis, stride, group, shift)) for shift in range(1, group)
    ]
    stacked = jnp.stack(got)
    order = (digit - jnp.arange(group)) % group
    return jnp.take(stacked, order, axis=0).reshape(-1)


def _factors(size):
    if size <= 4:
        return [size]
    return [2] + _factors(size // 2)


def tree_sum(values, axes):
    sizes = [lax.axis_size(axis) for axis in axes]
    flat = jnp.concatenate([value.reshape(-1) for value in values])
    total = 1
    for size in sizes:
        total *= size
    if not all(_power_of_two(size) for size in sizes) or flat.shape[0] % total:
        return lax.psum(tuple(values), axes)
    steps = []
    for axis, size in zip(axes, sizes):
        stride = 1
        for group in _factors(size):
            if group > 1:
                steps.append((axis, stride, group))
            stride *= group
    for axis, stride, group in steps:
        flat = _scatter_step(flat, axis, stride, group)
    for axis, stride, group in reversed(steps):
        flat = _gather_step(flat, axis, stride, group)
    results, start = [], 0
    for value in values:
        results.append(flat[start : start + value.size].reshape(value.shape))
        start += value.size
    return tuple(results)


def exchange(value, axis, split_axis, concat_axis):
    count = lax.axis_size(axis)
    mine = lax.axis_index(axis)
    pieces = jnp.stack(jnp.split(value, count, axis=split_axis))
    got = []
    for shift in range(count):
        send = lax.dynamic_index_in_dim(pieces, (mine + shift) % count, 0, keepdims=False)
        if shift:
            send = lax.ppermute(send, axis, [(i, (i + shift) % count) for i in range(count)])
        got.append(send)
    stacked = jnp.take(jnp.stack(got), (mine - jnp.arange(count)) % count, axis=0)
    return jnp.concatenate([stacked[k] for k in range(count)], axis=concat_axis)


def adjacency(sources, targets, count_rows, total_rows):
    target_hot = (targets[:, None] == jnp.arange(count_rows, dtype=jnp.int32)[None, :]).astype(
        jnp.bfloat16
    )
    source_hot = (sources[:, None] == jnp.arange(total_rows, dtype=jnp.int32)[None, :]).astype(
        jnp.bfloat16
    )
    counts = lax.dot_general(
        target_hot, source_hot, (((0,), (0,)), ((), ())), preferred_element_type=jnp.float32
    )
    return counts.astype(jnp.bfloat16)


def gnn_forward(states, received, adjacent, w_message):
    extended = jnp.concatenate([states, received], axis=0)
    neighbours = jnp.dot(adjacent, extended, preferred_element_type=jnp.float32)
    counted = jnp.sum(adjacent.astype(jnp.float32), axis=1)
    inverse = 1.0 / (counted + 1.0)
    aggregate = ((states.astype(jnp.float32) + neighbours) * inverse[:, None]).astype(jnp.bfloat16)
    preact = jnp.dot(aggregate, w_message, preferred_element_type=jnp.float32)
    hidden = (states.astype(jnp.float32) + jax.nn.silu(preact)).astype(jnp.bfloat16)
    return (aggregate, preact, inverse, hidden)


def gnn_backward(upstream, aggregate, preact, inverse, adjacent, w_message):
    count_rows = aggregate.shape[0]
    up_float = upstream.astype(jnp.float32)
    sigmoid_val = jax.nn.sigmoid(preact)
    pre_grad = (up_float * sigmoid_val * (1.0 + preact * (1.0 - sigmoid_val))).astype(jnp.bfloat16)
    message_part = lax.dot_general(
        aggregate, pre_grad, (((0,), (0,)), ((), ())), preferred_element_type=jnp.float32
    )
    agg_grad = lax.dot_general(
        pre_grad, w_message, (((1,), (1,)), ((), ())), preferred_element_type=jnp.float32
    )
    term_grad = agg_grad * inverse[:, None]
    ext_grad = lax.dot_general(
        adjacent.astype(jnp.float32),
        term_grad,
        (((0,), (0,)), ((), ())),
        precision=lax.Precision.HIGHEST,
        preferred_element_type=jnp.float32,
    )
    local_grad = up_float + term_grad + ext_grad[:count_rows]
    halo_grad = ext_grad[count_rows:].astype(jnp.bfloat16)
    return (message_part, local_grad, halo_grad)


def attend(states, upstream, w_query, w_key, w_value):
    steps_all, nodes_here, width = states.shape
    head_dim = width // HEADS
    scale_factor = head_dim ** (-0.5)
    flat = states.reshape(steps_all * nodes_here, width)

    def project(weight):
        return jnp.dot(flat, weight, preferred_element_type=jnp.float32).astype(jnp.bfloat16)

    def splitter(matrix):
        return matrix.reshape(steps_all, nodes_here, HEADS, head_dim).astype(jnp.float32)

    queries = project(w_query)
    key_rows = project(w_key)
    value_rows = project(w_value)
    query_f = splitter(queries)
    key_f = splitter(key_rows)
    value_f = splitter(value_rows)
    scores = jnp.einsum("tnhd,snhd->nhts", query_f, key_f) * scale_factor
    causal = jnp.arange(steps_all)[:, None] >= jnp.arange(steps_all)[None, :]
    scores = jnp.where(causal, scores, -jnp.inf)
    highest = jnp.max(scores, axis=-1, keepdims=True)
    exponent = jnp.exp(scores - highest)
    probs = exponent / jnp.sum(exponent, axis=-1, keepdims=True)
    probs_low = probs.astype(jnp.bfloat16).astype(jnp.float32)
    up_heads = splitter(upstream)
    value_grad = jnp.einsum("nhts,tnhd->snhd", probs_low, up_heads).astype(jnp.bfloat16)
    prob_grad = jnp.einsum("tnhd,snhd->nhts", up_heads, value_f)
    score_grad = (
        probs * (prob_grad - jnp.sum(prob_grad * probs, axis=-1, keepdims=True)) * scale_factor
    ).astype(jnp.bfloat16)
    score_f = score_grad.astype(jnp.float32)
    query_grad = jnp.einsum("nhts,snhd->tnhd", score_f, key_f).astype(jnp.bfloat16)
    key_grad = jnp.einsum("nhts,tnhd->snhd", score_f, query_f).astype(jnp.bfloat16)
    query_flat = query_grad.reshape(steps_all * nodes_here, width)
    key_flat = key_grad.reshape(steps_all * nodes_here, width)
    value_flat = value_grad.reshape(steps_all * nodes_here, width)

    def weight_grad(grad_rows):
        return lax.dot_general(
            flat, grad_rows, (((0,), (0,)), ((), ())), preferred_element_type=jnp.float32
        )

    def input_grad(grad_rows, weight):
        return lax.dot_general(
            grad_rows, weight, (((1,), (1,)), ((), ())), preferred_element_type=jnp.float32
        )

    back = upstream.reshape(steps_all * nodes_here, width).astype(jnp.float32)
    back = (
        back
        + input_grad(query_flat, w_query)
        + input_grad(key_flat, w_key)
        + input_grad(value_flat, w_value)
    )
    back = back.astype(jnp.bfloat16).reshape(steps_all, nodes_here, width)
    return ((weight_grad(query_flat), weight_grad(key_flat), weight_grad(value_flat)), back)


def attend_blocked(states, upstream, w_query, w_key, w_value):
    steps_all, nodes_here, width = states.shape
    head_dim = width // HEADS
    scale_factor = head_dim ** (-0.5)
    per_group = max(1, 128 // steps_all)
    if nodes_here % per_group:
        per_group = 1
    groups = nodes_here // per_group
    block = per_group * steps_all
    flat = jnp.swapaxes(states, 0, 1).reshape(nodes_here * steps_all, width)
    up_flat = jnp.swapaxes(upstream, 0, 1).reshape(nodes_here * steps_all, width)

    def project(weight):
        return jnp.dot(flat, weight, preferred_element_type=jnp.float32).astype(jnp.bfloat16)

    def blocks(matrix):
        return matrix.reshape(groups, block, HEADS, head_dim)

    queries = blocks(project(w_query))
    key_rows = blocks(project(w_key))
    value_rows = blocks(project(w_value))
    up_heads = blocks(up_flat)
    position = jnp.arange(block)
    same = (position[:, None] // steps_all) == (position[None, :] // steps_all)
    causal = jnp.logical_and(same, (position[:, None] % steps_all) >= (position[None, :] % steps_all))

    def contract(spec, left, right):
        return jnp.einsum(spec, left, right, preferred_element_type=jnp.float32)

    scores = contract("gihd,gjhd->ghij", queries, key_rows) * scale_factor
    scores = jnp.where(causal, scores, -jnp.inf)
    highest = jnp.max(scores, axis=-1, keepdims=True)
    exponent = jnp.exp(scores - highest)
    probs = exponent / jnp.sum(exponent, axis=-1, keepdims=True)
    probs_low = probs.astype(jnp.bfloat16)
    value_grad = contract("ghij,gihd->gjhd", probs_low, up_heads).astype(jnp.bfloat16)
    prob_grad = contract("gihd,gjhd->ghij", up_heads, value_rows)
    score_grad = (
        probs * (prob_grad - jnp.sum(prob_grad * probs, axis=-1, keepdims=True)) * scale_factor
    ).astype(jnp.bfloat16)
    score_grad = lax.optimization_barrier(score_grad)
    query_grad = contract("ghij,gjhd->gihd", score_grad, key_rows).astype(jnp.bfloat16)
    key_grad = contract("ghij,gihd->gjhd", score_grad, queries).astype(jnp.bfloat16)
    query_flat = query_grad.reshape(-1, width)
    key_flat = key_grad.reshape(-1, width)
    value_flat = value_grad.reshape(-1, width)

    def weight_grad(grad_rows):
        return lax.dot_general(
            flat, grad_rows, (((0,), (0,)), ((), ())), preferred_element_type=jnp.float32
        )

    def input_grad(grad_rows, weight):
        return lax.dot_general(
            grad_rows, weight, (((1,), (1,)), ((), ())), preferred_element_type=jnp.float32
        )

    back = (
        up_flat.astype(jnp.float32)
        + input_grad(query_flat, w_query)
        + input_grad(key_flat, w_key)
        + input_grad(value_flat, w_value)
    )
    back = jnp.swapaxes(back.astype(jnp.bfloat16).reshape(nodes_here, steps_all, width), 0, 1)
    return ((weight_grad(query_flat), weight_grad(key_flat), weight_grad(value_flat)), back)


def local(
    node_states,
    edge_source,
    edge_target,
    halo_rows,
    halo_count,
    w_message,
    w_query,
    w_key,
    w_value,
    cotangent,
):
    days_local, node_local, width = node_states.shape
    halo_slots = halo_rows.shape[1]
    live = jnp.arange(halo_slots)[None, :] < halo_count
    rows = jnp.arange(node_local, dtype=jnp.int32)
    slot_hot = jnp.logical_and(
        halo_rows[:, :, None] == rows[None, None, :], live[:, :, None]
    ).astype(jnp.bfloat16)
    sent = jnp.einsum(
        "dsn,dnh->dsh", slot_hot, node_states, preferred_element_type=jnp.float32
    ).astype(jnp.bfloat16)
    received = from_behind(sent, "dom", 1)

    target_hot = (edge_target[:, :, None] == rows[None, None, :]).astype(jnp.bfloat16)
    local_hot = (edge_source[:, :, None] == rows[None, None, :]).astype(jnp.bfloat16)
    halo_ids = node_local + jnp.arange(halo_slots, dtype=jnp.int32)
    halo_hot = (edge_source[:, :, None] == halo_ids[None, None, :]).astype(jnp.bfloat16)
    adjacent_local = jnp.einsum(
        "der,des->drs", target_hot, local_hot, preferred_element_type=jnp.float32
    ).astype(jnp.bfloat16)
    adjacent_halo = jnp.einsum(
        "der,des->drs", target_hot, halo_hot, preferred_element_type=jnp.float32
    ).astype(jnp.bfloat16)
    counted = jnp.sum(target_hot.astype(jnp.float32), axis=1)
    inverse = 1.0 / (counted + 1.0)

    states_f = node_states.astype(jnp.float32)
    neighbours = jnp.einsum(
        "drs,dsh->drh", adjacent_local, node_states, preferred_element_type=jnp.float32
    ) + jnp.einsum("drs,dsh->drh", adjacent_halo, received, preferred_element_type=jnp.float32)
    aggregate = ((states_f + neighbours) * inverse[:, :, None]).astype(jnp.bfloat16)
    preact = jnp.einsum("drh,hk->drk", aggregate, w_message, preferred_element_type=jnp.float32)
    hidden = (states_f + jax.nn.silu(preact)).astype(jnp.bfloat16)

    node_major = exchange(hidden, "day", 1, 0)
    upstream = cotangent.reshape(cotangent.shape[0], -1, width)
    attn_grads, back = attend_blocked(node_major, upstream, w_query, w_key, w_value)
    back_days = exchange(back, "day", 0, 1)

    sigmoid_val = jax.nn.sigmoid(preact)
    pre_grad = (
        back_days.astype(jnp.float32) * sigmoid_val * (1.0 + preact * (1.0 - sigmoid_val))
    ).astype(jnp.bfloat16)
    grad_message = lax.dot_general(
        aggregate.reshape(-1, width),
        pre_grad.reshape(-1, width),
        (((0,), (0,)), ((), ())),
        preferred_element_type=jnp.float32,
    )
    grad_message, grad_query, grad_key, grad_value = tree_sum(
        (grad_message, attn_grads[0], attn_grads[1], attn_grads[2]), ("dom", "day")
    )
    agg_grad = jnp.einsum("drk,hk->drh", pre_grad, w_message, preferred_element_type=jnp.float32)
    term_grad = agg_grad * inverse[:, :, None]
    halo_grad = jnp.einsum(
        "drs,drh->dsh",
        adjacent_halo.astype(jnp.float32),
        term_grad,
        precision=lax.Precision.HIGHEST,
        preferred_element_type=jnp.float32,
    ).astype(jnp.bfloat16)
    returned = from_behind(halo_grad, "dom", -1)
    own_grad = jnp.einsum(
        "drs,drh->dsh",
        adjacent_local.astype(jnp.float32),
        term_grad,
        precision=lax.Precision.HIGHEST,
        preferred_element_type=jnp.float32,
    )
    scattered = jnp.einsum("dsn,dsh->dnh", slot_hot, returned, preferred_element_type=jnp.float32)
    state_grad = back_days.astype(jnp.float32) + term_grad + own_grad + scattered
    return (state_grad, grad_message, grad_query, grad_key, grad_value)


def solution(mesh):
    return jax.shard_map(
        local,
        mesh=mesh,
        in_specs=(
            P("day", "dom", None),
            P("day", "dom"),
            P("day", "dom"),
            P("day", "dom"),
            P("day", "dom"),
            P(),
            P(),
            P(),
            P(),
            P(None, "dom", "day", None, None),
        ),
        out_specs=(P("day", "dom", None), P(), P(), P(), P()),
        check_vma=False,
    )
```

```python
import jax
import jax.numpy as jnp
from jax import lax
from jax.sharding import PartitionSpec as P

HEADS = 4


def from_behind(value, axis, steps):
    count = lax.axis_size(axis)
    pairs = [(source, (source + steps) % count) for source in range(count)]
    return lax.ppermute(value, axis, pairs)


def _power_of_two(count):
    return count > 0 and count & (count - 1) == 0


def _group_pairs(axis, stride, group, shift):
    pairs = []
    for source in range(lax.axis_size(axis)):
        digit = (source // stride) % group
        pairs.append((source, source + ((digit + shift) % group - digit) * stride))
    return pairs


def _scatter_step(flat, axis, stride, group):
    digit = (lax.axis_index(axis) // stride) % group
    chunks = flat.reshape(group, -1)
    total = lax.dynamic_index_in_dim(chunks, digit, 0, keepdims=False)
    for shift in range(1, group):
        send = lax.dynamic_index_in_dim(chunks, (digit + shift) % group, 0, keepdims=False)
        total = total + lax.ppermute(send, axis, _group_pairs(axis, stride, group, shift))
    return total


def _gather_step(flat, axis, stride, group):
    digit = (lax.axis_index(axis) // stride) % group
    got = [flat] + [
        lax.ppermute(flat, axis, _group_pairs(axis, stride, group, shift)) for shift in range(1, group)
    ]
    stacked = jnp.stack(got)
    order = (digit - jnp.arange(group)) % group
    return jnp.take(stacked, order, axis=0).reshape(-1)


def _factors(size):
    if size <= 4:
        return [size]
    return [2] + _factors(size // 2)


def tree_sum(values, axes, companion=None):
    sizes = [lax.axis_size(axis) for axis in axes]
    flat = jnp.concatenate([value.reshape(-1) for value in values])
    total = 1
    for size in sizes:
        total *= size
    if not all(_power_of_two(size) for size in sizes) or flat.shape[0] % total:
        return lax.psum(tuple(values), axes), companion
    steps = []
    for axis, size in zip(axes, sizes):
        stride = 1
        for group in _factors(size):
            if group > 1:
                steps.append((axis, stride, group))
            stride *= group
    for axis, stride, group in steps:
        flat = _scatter_step(flat, axis, stride, group)
    flat, companion = lax.optimization_barrier((flat, companion))
    for axis, stride, group in reversed(steps):
        flat = _gather_step(flat, axis, stride, group)
    results, start = [], 0
    for value in values:
        results.append(flat[start : start + value.size].reshape(value.shape))
        start += value.size
    return tuple(results), companion


def exchange(value, axis, split_axis, concat_axis):
    count = lax.axis_size(axis)
    mine = lax.axis_index(axis)
    pieces = jnp.stack(jnp.split(value, count, axis=split_axis))
    got = []
    for shift in range(count):
        send = lax.dynamic_index_in_dim(pieces, (mine + shift) % count, 0, keepdims=False)
        if shift:
            send = lax.ppermute(send, axis, [(i, (i + shift) % count) for i in range(count)])
        got.append(send)
    stacked = jnp.take(jnp.stack(got), (mine - jnp.arange(count)) % count, axis=0)
    return jnp.concatenate([stacked[k] for k in range(count)], axis=concat_axis)


def adjacency(sources, targets, count_rows, total_rows):
    target_hot = (targets[:, None] == jnp.arange(count_rows, dtype=jnp.int32)[None, :]).astype(
        jnp.bfloat16
    )
    source_hot = (sources[:, None] == jnp.arange(total_rows, dtype=jnp.int32)[None, :]).astype(
        jnp.bfloat16
    )
    counts = lax.dot_general(
        target_hot, source_hot, (((0,), (0,)), ((), ())), preferred_element_type=jnp.float32
    )
    return counts.astype(jnp.bfloat16)


def gnn_forward(states, received, adjacent, w_message):
    extended = jnp.concatenate([states, received], axis=0)
    neighbours = jnp.dot(adjacent, extended, preferred_element_type=jnp.float32)
    counted = jnp.sum(adjacent.astype(jnp.float32), axis=1)
    inverse = 1.0 / (counted + 1.0)
    aggregate = ((states.astype(jnp.float32) + neighbours) * inverse[:, None]).astype(jnp.bfloat16)
    preact = jnp.dot(aggregate, w_message, preferred_element_type=jnp.float32)
    hidden = (states.astype(jnp.float32) + jax.nn.silu(preact)).astype(jnp.bfloat16)
    return (aggregate, preact, inverse, hidden)


def gnn_backward(upstream, aggregate, preact, inverse, adjacent, w_message):
    count_rows = aggregate.shape[0]
    up_float = upstream.astype(jnp.float32)
    sigmoid_val = jax.nn.sigmoid(preact)
    pre_grad = (up_float * sigmoid_val * (1.0 + preact * (1.0 - sigmoid_val))).astype(jnp.bfloat16)
    message_part = lax.dot_general(
        aggregate, pre_grad, (((0,), (0,)), ((), ())), preferred_element_type=jnp.float32
    )
    agg_grad = lax.dot_general(
        pre_grad, w_message, (((1,), (1,)), ((), ())), preferred_element_type=jnp.float32
    )
    term_grad = agg_grad * inverse[:, None]
    ext_grad = lax.dot_general(
        adjacent.astype(jnp.float32),
        term_grad,
        (((0,), (0,)), ((), ())),
        precision=lax.Precision.HIGHEST,
        preferred_element_type=jnp.float32,
    )
    local_grad = up_float + term_grad + ext_grad[:count_rows]
    halo_grad = ext_grad[count_rows:].astype(jnp.bfloat16)
    return (message_part, local_grad, halo_grad)


def attend(states, upstream, w_query, w_key, w_value):
    steps_all, nodes_here, width = states.shape
    head_dim = width // HEADS
    scale_factor = head_dim ** (-0.5)
    flat = states.reshape(steps_all * nodes_here, width)

    def project(weight):
        return jnp.dot(flat, weight, preferred_element_type=jnp.float32).astype(jnp.bfloat16)

    def splitter(matrix):
        return matrix.reshape(steps_all, nodes_here, HEADS, head_dim).astype(jnp.float32)

    queries = project(w_query)
    key_rows = project(w_key)
    value_rows = project(w_value)
    query_f = splitter(queries)
    key_f = splitter(key_rows)
    value_f = splitter(value_rows)
    scores = jnp.einsum("tnhd,snhd->nhts", query_f, key_f) * scale_factor
    causal = jnp.arange(steps_all)[:, None] >= jnp.arange(steps_all)[None, :]
    scores = jnp.where(causal, scores, -jnp.inf)
    highest = jnp.max(scores, axis=-1, keepdims=True)
    exponent = jnp.exp(scores - highest)
    probs = exponent / jnp.sum(exponent, axis=-1, keepdims=True)
    probs_low = probs.astype(jnp.bfloat16).astype(jnp.float32)
    up_heads = splitter(upstream)
    value_grad = jnp.einsum("nhts,tnhd->snhd", probs_low, up_heads).astype(jnp.bfloat16)
    prob_grad = jnp.einsum("tnhd,snhd->nhts", up_heads, value_f)
    score_grad = (
        probs * (prob_grad - jnp.sum(prob_grad * probs, axis=-1, keepdims=True)) * scale_factor
    ).astype(jnp.bfloat16)
    score_f = score_grad.astype(jnp.float32)
    query_grad = jnp.einsum("nhts,snhd->tnhd", score_f, key_f).astype(jnp.bfloat16)
    key_grad = jnp.einsum("nhts,tnhd->snhd", score_f, query_f).astype(jnp.bfloat16)
    query_flat = query_grad.reshape(steps_all * nodes_here, width)
    key_flat = key_grad.reshape(steps_all * nodes_here, width)
    value_flat = value_grad.reshape(steps_all * nodes_here, width)

    def weight_grad(grad_rows):
        return lax.dot_general(
            flat, grad_rows, (((0,), (0,)), ((), ())), preferred_element_type=jnp.float32
        )

    def input_grad(grad_rows, weight):
        return lax.dot_general(
            grad_rows, weight, (((1,), (1,)), ((), ())), preferred_element_type=jnp.float32
        )

    back = upstream.reshape(steps_all * nodes_here, width).astype(jnp.float32)
    back = (
        back
        + input_grad(query_flat, w_query)
        + input_grad(key_flat, w_key)
        + input_grad(value_flat, w_value)
    )
    back = back.astype(jnp.bfloat16).reshape(steps_all, nodes_here, width)
    return ((weight_grad(query_flat), weight_grad(key_flat), weight_grad(value_flat)), back)


def attend_blocked(states, upstream, w_query, w_key, w_value):
    steps_all, nodes_here, width = states.shape
    head_dim = width // HEADS
    scale_factor = head_dim ** (-0.5)
    per_group = max(1, 128 // steps_all)
    if nodes_here % per_group:
        per_group = 1
    groups = nodes_here // per_group
    block = per_group * steps_all
    flat = jnp.swapaxes(states, 0, 1).reshape(nodes_here * steps_all, width)
    up_flat = jnp.swapaxes(upstream, 0, 1).reshape(nodes_here * steps_all, width)

    def project(weight):
        return jnp.dot(flat, weight, preferred_element_type=jnp.float32).astype(jnp.bfloat16)

    def blocks(matrix):
        return matrix.reshape(groups, block, HEADS, head_dim)

    queries = blocks(project(w_query))
    key_rows = blocks(project(w_key))
    value_rows = blocks(project(w_value))
    up_heads = blocks(up_flat)
    position = jnp.arange(block)
    same = (position[:, None] // steps_all) == (position[None, :] // steps_all)
    causal = jnp.logical_and(same, (position[:, None] % steps_all) >= (position[None, :] % steps_all))

    def contract(spec, left, right):
        return jnp.einsum(spec, left, right, preferred_element_type=jnp.float32)

    scores = contract("gihd,gjhd->ghij", queries, key_rows) * scale_factor
    scores = jnp.where(causal, scores, -jnp.inf)
    highest = jnp.max(scores, axis=-1, keepdims=True)
    exponent = jnp.exp(scores - highest)
    probs = exponent / jnp.sum(exponent, axis=-1, keepdims=True)
    probs_low = probs.astype(jnp.bfloat16)
    value_grad = contract("ghij,gihd->gjhd", probs_low, up_heads).astype(jnp.bfloat16)
    prob_grad = contract("gihd,gjhd->ghij", up_heads, value_rows)
    score_grad = (
        probs * (prob_grad - jnp.sum(prob_grad * probs, axis=-1, keepdims=True)) * scale_factor
    ).astype(jnp.bfloat16)
    score_grad = lax.optimization_barrier(score_grad)
    query_grad = contract("ghij,gjhd->gihd", score_grad, key_rows).astype(jnp.bfloat16)
    key_grad = contract("ghij,gihd->gjhd", score_grad, queries).astype(jnp.bfloat16)
    query_flat = query_grad.reshape(-1, width)
    key_flat = key_grad.reshape(-1, width)
    value_flat = value_grad.reshape(-1, width)

    def weight_grad(grad_rows):
        return lax.dot_general(
            flat, grad_rows, (((0,), (0,)), ((), ())), preferred_element_type=jnp.float32
        )

    def input_grad(grad_rows, weight):
        return lax.dot_general(
            grad_rows, weight, (((1,), (1,)), ((), ())), preferred_element_type=jnp.float32
        )

    back = (
        up_flat.astype(jnp.float32)
        + input_grad(query_flat, w_query)
        + input_grad(key_flat, w_key)
        + input_grad(value_flat, w_value)
    )
    back = jnp.swapaxes(back.astype(jnp.bfloat16).reshape(nodes_here, steps_all, width), 0, 1)
    return ((weight_grad(query_flat), weight_grad(key_flat), weight_grad(value_flat)), back)


def local(
    node_states,
    edge_source,
    edge_target,
    halo_rows,
    halo_count,
    w_message,
    w_query,
    w_key,
    w_value,
    cotangent,
):
    days_local, node_local, width = node_states.shape
    halo_slots = halo_rows.shape[1]
    live = jnp.arange(halo_slots)[None, :] < halo_count
    rows = jnp.arange(node_local, dtype=jnp.int32)
    slot_hot = jnp.logical_and(
        halo_rows[:, :, None] == rows[None, None, :], live[:, :, None]
    ).astype(jnp.bfloat16)
    sent = jnp.einsum(
        "dsn,dnh->dsh", slot_hot, node_states, preferred_element_type=jnp.float32
    ).astype(jnp.bfloat16)
    received = from_behind(sent, "dom", 1)

    target_hot = (edge_target[:, :, None] == rows[None, None, :]).astype(jnp.bfloat16)
    local_hot = (edge_source[:, :, None] == rows[None, None, :]).astype(jnp.bfloat16)
    halo_ids = node_local + jnp.arange(halo_slots, dtype=jnp.int32)
    halo_hot = (edge_source[:, :, None] == halo_ids[None, None, :]).astype(jnp.bfloat16)
    adjacent_local = jnp.einsum(
        "der,des->drs", target_hot, local_hot, preferred_element_type=jnp.float32
    ).astype(jnp.bfloat16)
    adjacent_halo = jnp.einsum(
        "der,des->drs", target_hot, halo_hot, preferred_element_type=jnp.float32
    ).astype(jnp.bfloat16)
    counted = jnp.sum(target_hot.astype(jnp.float32), axis=1)
    inverse = 1.0 / (counted + 1.0)

    states_f = node_states.astype(jnp.float32)
    neighbours = jnp.einsum(
        "drs,dsh->drh", adjacent_local, node_states, preferred_element_type=jnp.float32
    ) + jnp.einsum("drs,dsh->drh", adjacent_halo, received, preferred_element_type=jnp.float32)
    aggregate = ((states_f + neighbours) * inverse[:, :, None]).astype(jnp.bfloat16)
    preact = jnp.einsum("drh,hk->drk", aggregate, w_message, preferred_element_type=jnp.float32)
    hidden = (states_f + jax.nn.silu(preact)).astype(jnp.bfloat16)

    node_major = exchange(hidden, "day", 1, 0)
    upstream = cotangent.reshape(cotangent.shape[0], -1, width)
    attn_grads, back = attend_blocked(node_major, upstream, w_query, w_key, w_value)
    back_days = exchange(back, "day", 0, 1)

    sigmoid_val = jax.nn.sigmoid(preact)
    pre_grad = (
        back_days.astype(jnp.float32) * sigmoid_val * (1.0 + preact * (1.0 - sigmoid_val))
    ).astype(jnp.bfloat16)
    grad_message = lax.dot_general(
        aggregate.reshape(-1, width),
        pre_grad.reshape(-1, width),
        (((0,), (0,)), ((), ())),
        preferred_element_type=jnp.float32,
    )
    agg_grad = jnp.einsum("drk,hk->drh", pre_grad, w_message, preferred_element_type=jnp.float32)
    term_grad = agg_grad * inverse[:, :, None]
    halo_grad = jnp.einsum(
        "drs,drh->dsh",
        adjacent_halo.astype(jnp.float32),
        term_grad,
        precision=lax.Precision.HIGHEST,
        preferred_element_type=jnp.float32,
    ).astype(jnp.bfloat16)
    returned = from_behind(halo_grad, "dom", -1)
    own_grad = jnp.einsum(
        "drs,drh->dsh",
        adjacent_local.astype(jnp.float32),
        term_grad,
        precision=lax.Precision.HIGHEST,
        preferred_element_type=jnp.float32,
    )
    scattered = jnp.einsum("dsn,dsh->dnh", slot_hot, returned, preferred_element_type=jnp.float32)
    state_grad = back_days.astype(jnp.float32) + term_grad + own_grad + scattered
    (grad_message, grad_query, grad_key, grad_value), state_grad = tree_sum(
        (grad_message, attn_grads[0], attn_grads[1], attn_grads[2]), ("dom", "day"), state_grad
    )
    return (state_grad, grad_message, grad_query, grad_key, grad_value)


def solution(mesh):
    return jax.shard_map(
        local,
        mesh=mesh,
        in_specs=(
            P("day", "dom", None),
            P("day", "dom"),
            P("day", "dom"),
            P("day", "dom"),
            P("day", "dom"),
            P(),
            P(),
            P(),
            P(),
            P(None, "dom", "day", None, None),
        ),
        out_specs=(P("day", "dom", None), P(), P(), P(), P()),
        check_vma=False,
    )
```

```python
import jax
import jax.numpy as jnp
from jax import lax
from jax.sharding import PartitionSpec as P

HEADS = 4


def from_behind(value, axis, steps):
    count = lax.axis_size(axis)
    pairs = [(source, (source + steps) % count) for source in range(count)]
    return lax.ppermute(value, axis, pairs)


def _power_of_two(count):
    return count > 0 and count & (count - 1) == 0


def _group_pairs(axis, stride, group, shift):
    pairs = []
    for source in range(lax.axis_size(axis)):
        digit = (source // stride) % group
        pairs.append((source, source + ((digit + shift) % group - digit) * stride))
    return pairs


def _scatter_step(flat, axis, stride, group):
    digit = (lax.axis_index(axis) // stride) % group
    chunks = flat.reshape(group, -1)
    total = lax.dynamic_index_in_dim(chunks, digit, 0, keepdims=False)
    for shift in range(1, group):
        send = lax.dynamic_index_in_dim(chunks, (digit + shift) % group, 0, keepdims=False)
        total = total + lax.ppermute(send, axis, _group_pairs(axis, stride, group, shift))
    return total


def _by_source(got, digit):
    count = len(got)
    ordered = []
    for source in range(count):
        place = (digit - source) % count
        chosen = got[count - 1]
        for shift in range(count - 2, -1, -1):
            chosen = jnp.where(place == shift, got[shift], chosen)
        ordered.append(chosen)
    return ordered


def _gather_step(flat, axis, stride, group):
    digit = (lax.axis_index(axis) // stride) % group
    got = [flat] + [
        lax.ppermute(flat, axis, _group_pairs(axis, stride, group, shift)) for shift in range(1, group)
    ]
    return jnp.concatenate(_by_source(got, digit))


def _factors(size):
    if size <= 4:
        return [size]
    return [2] + _factors(size // 2)


def tree_sum(values, axes, companion=None):
    sizes = [lax.axis_size(axis) for axis in axes]
    flat = jnp.concatenate([value.reshape(-1) for value in values])
    total = 1
    for size in sizes:
        total *= size
    if not all(_power_of_two(size) for size in sizes) or flat.shape[0] % total:
        return lax.psum(tuple(values), axes), companion
    steps = []
    for axis, size in zip(axes, sizes):
        stride = 1
        for group in _factors(size):
            if group > 1:
                steps.append((axis, stride, group))
            stride *= group
    for axis, stride, group in steps:
        flat = _scatter_step(flat, axis, stride, group)
    flat, companion = lax.optimization_barrier((flat, companion))
    for axis, stride, group in reversed(steps):
        flat = _gather_step(flat, axis, stride, group)
    results, start = [], 0
    for value in values:
        results.append(flat[start : start + value.size].reshape(value.shape))
        start += value.size
    return tuple(results), companion


def exchange(value, axis, split_axis, concat_axis):
    count = lax.axis_size(axis)
    mine = lax.axis_index(axis)
    pieces = jnp.stack(jnp.split(value, count, axis=split_axis))
    got = []
    for shift in range(count):
        send = lax.dynamic_index_in_dim(pieces, (mine + shift) % count, 0, keepdims=False)
        if shift:
            send = lax.ppermute(send, axis, [(i, (i + shift) % count) for i in range(count)])
        got.append(send)
    return jnp.concatenate(_by_source(got, mine), axis=concat_axis)


def adjacency(sources, targets, count_rows, total_rows):
    target_hot = (targets[:, None] == jnp.arange(count_rows, dtype=jnp.int32)[None, :]).astype(
        jnp.bfloat16
    )
    source_hot = (sources[:, None] == jnp.arange(total_rows, dtype=jnp.int32)[None, :]).astype(
        jnp.bfloat16
    )
    counts = lax.dot_general(
        target_hot, source_hot, (((0,), (0,)), ((), ())), preferred_element_type=jnp.float32
    )
    return counts.astype(jnp.bfloat16)


def gnn_forward(states, received, adjacent, w_message):
    extended = jnp.concatenate([states, received], axis=0)
    neighbours = jnp.dot(adjacent, extended, preferred_element_type=jnp.float32)
    counted = jnp.sum(adjacent.astype(jnp.float32), axis=1)
    inverse = 1.0 / (counted + 1.0)
    aggregate = ((states.astype(jnp.float32) + neighbours) * inverse[:, None]).astype(jnp.bfloat16)
    preact = jnp.dot(aggregate, w_message, preferred_element_type=jnp.float32)
    hidden = (states.astype(jnp.float32) + jax.nn.silu(preact)).astype(jnp.bfloat16)
    return (aggregate, preact, inverse, hidden)


def gnn_backward(upstream, aggregate, preact, inverse, adjacent, w_message):
    count_rows = aggregate.shape[0]
    up_float = upstream.astype(jnp.float32)
    sigmoid_val = jax.nn.sigmoid(preact)
    pre_grad = (up_float * sigmoid_val * (1.0 + preact * (1.0 - sigmoid_val))).astype(jnp.bfloat16)
    message_part = lax.dot_general(
        aggregate, pre_grad, (((0,), (0,)), ((), ())), preferred_element_type=jnp.float32
    )
    agg_grad = lax.dot_general(
        pre_grad, w_message, (((1,), (1,)), ((), ())), preferred_element_type=jnp.float32
    )
    term_grad = agg_grad * inverse[:, None]
    ext_grad = lax.dot_general(
        adjacent.astype(jnp.float32),
        term_grad,
        (((0,), (0,)), ((), ())),
        precision=lax.Precision.HIGHEST,
        preferred_element_type=jnp.float32,
    )
    local_grad = up_float + term_grad + ext_grad[:count_rows]
    halo_grad = ext_grad[count_rows:].astype(jnp.bfloat16)
    return (message_part, local_grad, halo_grad)


def attend(states, upstream, w_query, w_key, w_value):
    steps_all, nodes_here, width = states.shape
    head_dim = width // HEADS
    scale_factor = head_dim ** (-0.5)
    flat = states.reshape(steps_all * nodes_here, width)

    def project(weight):
        return jnp.dot(flat, weight, preferred_element_type=jnp.float32).astype(jnp.bfloat16)

    def splitter(matrix):
        return matrix.reshape(steps_all, nodes_here, HEADS, head_dim).astype(jnp.float32)

    queries = project(w_query)
    key_rows = project(w_key)
    value_rows = project(w_value)
    query_f = splitter(queries)
    key_f = splitter(key_rows)
    value_f = splitter(value_rows)
    scores = jnp.einsum("tnhd,snhd->nhts", query_f, key_f) * scale_factor
    causal = jnp.arange(steps_all)[:, None] >= jnp.arange(steps_all)[None, :]
    scores = jnp.where(causal, scores, -jnp.inf)
    highest = jnp.max(scores, axis=-1, keepdims=True)
    exponent = jnp.exp(scores - highest)
    probs = exponent / jnp.sum(exponent, axis=-1, keepdims=True)
    probs_low = probs.astype(jnp.bfloat16).astype(jnp.float32)
    up_heads = splitter(upstream)
    value_grad = jnp.einsum("nhts,tnhd->snhd", probs_low, up_heads).astype(jnp.bfloat16)
    prob_grad = jnp.einsum("tnhd,snhd->nhts", up_heads, value_f)
    score_grad = (
        probs * (prob_grad - jnp.sum(prob_grad * probs, axis=-1, keepdims=True)) * scale_factor
    ).astype(jnp.bfloat16)
    score_f = score_grad.astype(jnp.float32)
    query_grad = jnp.einsum("nhts,snhd->tnhd", score_f, key_f).astype(jnp.bfloat16)
    key_grad = jnp.einsum("nhts,tnhd->snhd", score_f, query_f).astype(jnp.bfloat16)
    query_flat = query_grad.reshape(steps_all * nodes_here, width)
    key_flat = key_grad.reshape(steps_all * nodes_here, width)
    value_flat = value_grad.reshape(steps_all * nodes_here, width)

    def weight_grad(grad_rows):
        return lax.dot_general(
            flat, grad_rows, (((0,), (0,)), ((), ())), preferred_element_type=jnp.float32
        )

    def input_grad(grad_rows, weight):
        return lax.dot_general(
            grad_rows, weight, (((1,), (1,)), ((), ())), preferred_element_type=jnp.float32
        )

    back = upstream.reshape(steps_all * nodes_here, width).astype(jnp.float32)
    back = (
        back
        + input_grad(query_flat, w_query)
        + input_grad(key_flat, w_key)
        + input_grad(value_flat, w_value)
    )
    back = back.astype(jnp.bfloat16).reshape(steps_all, nodes_here, width)
    return ((weight_grad(query_flat), weight_grad(key_flat), weight_grad(value_flat)), back)


def attend_blocked(states, upstream, w_query, w_key, w_value):
    steps_all, nodes_here, width = states.shape
    head_dim = width // HEADS
    scale_factor = head_dim ** (-0.5)
    per_group = max(1, 128 // steps_all)
    if nodes_here % per_group:
        per_group = 1
    groups = nodes_here // per_group
    block = per_group * steps_all
    flat = jnp.swapaxes(states, 0, 1).reshape(nodes_here * steps_all, width)
    up_flat = jnp.swapaxes(upstream, 0, 1).reshape(nodes_here * steps_all, width)

    def project(weight):
        return jnp.dot(flat, weight, preferred_element_type=jnp.float32).astype(jnp.bfloat16)

    def blocks(matrix):
        return matrix.reshape(groups, block, HEADS, head_dim)

    queries = blocks(project(w_query))
    key_rows = blocks(project(w_key))
    value_rows = blocks(project(w_value))
    up_heads = blocks(up_flat)
    position = jnp.arange(block)
    same = (position[:, None] // steps_all) == (position[None, :] // steps_all)
    causal = jnp.logical_and(same, (position[:, None] % steps_all) >= (position[None, :] % steps_all))

    def contract(spec, left, right):
        return jnp.einsum(spec, left, right, preferred_element_type=jnp.float32)

    scores = contract("gihd,gjhd->ghij", queries, key_rows) * scale_factor
    scores = jnp.where(causal, scores, -jnp.inf)
    highest = jnp.max(scores, axis=-1, keepdims=True)
    exponent = jnp.exp(scores - highest)
    probs = exponent / jnp.sum(exponent, axis=-1, keepdims=True)
    probs_low = probs.astype(jnp.bfloat16)
    value_grad = contract("ghij,gihd->gjhd", probs_low, up_heads).astype(jnp.bfloat16)
    prob_grad = contract("gihd,gjhd->ghij", up_heads, value_rows)
    score_grad = (
        probs * (prob_grad - jnp.sum(prob_grad * probs, axis=-1, keepdims=True)) * scale_factor
    ).astype(jnp.bfloat16)
    score_grad = lax.optimization_barrier(score_grad)
    query_grad = contract("ghij,gjhd->gihd", score_grad, key_rows).astype(jnp.bfloat16)
    key_grad = contract("ghij,gihd->gjhd", score_grad, queries).astype(jnp.bfloat16)
    query_flat = query_grad.reshape(-1, width)
    key_flat = key_grad.reshape(-1, width)
    value_flat = value_grad.reshape(-1, width)

    def weight_grad(grad_rows):
        return lax.dot_general(
            flat, grad_rows, (((0,), (0,)), ((), ())), preferred_element_type=jnp.float32
        )

    def input_grad(grad_rows, weight):
        return lax.dot_general(
            grad_rows, weight, (((1,), (1,)), ((), ())), preferred_element_type=jnp.float32
        )

    back = (
        up_flat.astype(jnp.float32)
        + input_grad(query_flat, w_query)
        + input_grad(key_flat, w_key)
        + input_grad(value_flat, w_value)
    )
    back = jnp.swapaxes(back.astype(jnp.bfloat16).reshape(nodes_here, steps_all, width), 0, 1)
    return ((weight_grad(query_flat), weight_grad(key_flat), weight_grad(value_flat)), back)


def local(
    node_states,
    edge_source,
    edge_target,
    halo_rows,
    halo_count,
    w_message,
    w_query,
    w_key,
    w_value,
    cotangent,
):
    days_local, node_local, width = node_states.shape
    halo_slots = halo_rows.shape[1]
    live = jnp.arange(halo_slots)[None, :] < halo_count
    rows = jnp.arange(node_local, dtype=jnp.int32)
    slot_hot = jnp.logical_and(
        halo_rows[:, :, None] == rows[None, None, :], live[:, :, None]
    ).astype(jnp.bfloat16)
    sent = jnp.einsum(
        "dsn,dnh->dsh", slot_hot, node_states, preferred_element_type=jnp.float32
    ).astype(jnp.bfloat16)
    received = from_behind(sent, "dom", 1)

    target_hot = (edge_target[:, :, None] == rows[None, None, :]).astype(jnp.bfloat16)
    local_hot = (edge_source[:, :, None] == rows[None, None, :]).astype(jnp.bfloat16)
    halo_ids = node_local + jnp.arange(halo_slots, dtype=jnp.int32)
    halo_hot = (edge_source[:, :, None] == halo_ids[None, None, :]).astype(jnp.bfloat16)
    adjacent_local = jnp.einsum(
        "der,des->drs", target_hot, local_hot, preferred_element_type=jnp.float32
    ).astype(jnp.bfloat16)
    adjacent_halo = jnp.einsum(
        "der,des->drs", target_hot, halo_hot, preferred_element_type=jnp.float32
    ).astype(jnp.bfloat16)
    counted = jnp.sum(target_hot.astype(jnp.float32), axis=1)
    inverse = 1.0 / (counted + 1.0)

    states_f = node_states.astype(jnp.float32)
    neighbours = jnp.einsum(
        "drs,dsh->drh", adjacent_local, node_states, preferred_element_type=jnp.float32
    ) + jnp.einsum("drs,dsh->drh", adjacent_halo, received, preferred_element_type=jnp.float32)
    aggregate = ((states_f + neighbours) * inverse[:, :, None]).astype(jnp.bfloat16)
    preact = jnp.einsum("drh,hk->drk", aggregate, w_message, preferred_element_type=jnp.float32)
    hidden = (states_f + jax.nn.silu(preact)).astype(jnp.bfloat16)

    node_major = exchange(hidden, "day", 1, 0)
    upstream = cotangent.reshape(cotangent.shape[0], -1, width)
    attn_grads, back = attend_blocked(node_major, upstream, w_query, w_key, w_value)
    back_days = exchange(back, "day", 0, 1)

    sigmoid_val = jax.nn.sigmoid(preact)
    pre_grad = (
        back_days.astype(jnp.float32) * sigmoid_val * (1.0 + preact * (1.0 - sigmoid_val))
    ).astype(jnp.bfloat16)
    grad_message = lax.dot_general(
        aggregate.reshape(-1, width),
        pre_grad.reshape(-1, width),
        (((0,), (0,)), ((), ())),
        preferred_element_type=jnp.float32,
    )
    agg_grad = jnp.einsum("drk,hk->drh", pre_grad, w_message, preferred_element_type=jnp.float32)
    term_grad = agg_grad * inverse[:, :, None]
    halo_grad = jnp.einsum(
        "drs,drh->dsh",
        adjacent_halo.astype(jnp.float32),
        term_grad,
        precision=lax.Precision.HIGHEST,
        preferred_element_type=jnp.float32,
    ).astype(jnp.bfloat16)
    returned = from_behind(halo_grad, "dom", -1)
    own_grad = jnp.einsum(
        "drs,drh->dsh",
        adjacent_local.astype(jnp.float32),
        term_grad,
        precision=lax.Precision.HIGHEST,
        preferred_element_type=jnp.float32,
    )
    scattered = jnp.einsum("dsn,dsh->dnh", slot_hot, returned, preferred_element_type=jnp.float32)
    state_grad = back_days.astype(jnp.float32) + term_grad + own_grad + scattered
    (grad_message, grad_query, grad_key, grad_value), state_grad = tree_sum(
        (grad_message, attn_grads[0], attn_grads[1], attn_grads[2]), ("dom", "day"), state_grad
    )
    return (state_grad, grad_message, grad_query, grad_key, grad_value)


def solution(mesh):
    return jax.shard_map(
        local,
        mesh=mesh,
        in_specs=(
            P("day", "dom", None),
            P("day", "dom"),
            P("day", "dom"),
            P("day", "dom"),
            P("day", "dom"),
            P(),
            P(),
            P(),
            P(),
            P(None, "dom", "day", None, None),
        ),
        out_specs=(P("day", "dom", None), P(), P(), P(), P()),
        check_vma=False,
    )
```

```python
import jax
import jax.numpy as jnp
from jax import lax
from jax.sharding import PartitionSpec as P

HEADS = 4


def from_behind(value, axis, steps):
    count = lax.axis_size(axis)
    pairs = [(source, (source + steps) % count) for source in range(count)]
    return lax.ppermute(value, axis, pairs)


def _power_of_two(count):
    return count > 0 and count & (count - 1) == 0


def _group_pairs(axis, stride, group, shift):
    pairs = []
    for source in range(lax.axis_size(axis)):
        digit = (source // stride) % group
        pairs.append((source, source + ((digit + shift) % group - digit) * stride))
    return pairs


def _scatter_step(flat, axis, stride, group):
    digit = (lax.axis_index(axis) // stride) % group
    chunks = flat.reshape(group, -1)
    total = lax.dynamic_index_in_dim(chunks, digit, 0, keepdims=False)
    for shift in range(1, group):
        send = lax.dynamic_index_in_dim(chunks, (digit + shift) % group, 0, keepdims=False)
        total = total + lax.ppermute(send, axis, _group_pairs(axis, stride, group, shift))
    return total


def _gather_step(flat, axis, stride, group):
    digit = (lax.axis_index(axis) // stride) % group
    got = [flat] + [
        lax.ppermute(flat, axis, _group_pairs(axis, stride, group, shift)) for shift in range(1, group)
    ]
    stacked = jnp.stack(got)
    order = (digit - jnp.arange(group)) % group
    return jnp.take(stacked, order, axis=0).reshape(-1)


def _factors(size):
    if size <= 4:
        return [size]
    return [2] + _factors(size // 2)


def tree_sum(values, axes, companion=None):
    sizes = [lax.axis_size(axis) for axis in axes]
    flat = jnp.concatenate([value.reshape(-1) for value in values])
    total = 1
    for size in sizes:
        total *= size
    if not all(_power_of_two(size) for size in sizes) or flat.shape[0] % total:
        return lax.psum(tuple(values), axes), companion
    steps = []
    for axis, size in zip(axes, sizes):
        stride = 1
        for group in _factors(size):
            if group > 1:
                steps.append((axis, stride, group))
            stride *= group
    for axis, stride, group in steps:
        flat = _scatter_step(flat, axis, stride, group)
    flat, companion = lax.optimization_barrier((flat, companion))
    for axis, stride, group in reversed(steps):
        flat = _gather_step(flat, axis, stride, group)
    results, start = [], 0
    for value in values:
        results.append(flat[start : start + value.size].reshape(value.shape))
        start += value.size
    return tuple(results), companion


def exchange(value, axis, split_axis, concat_axis):
    count = lax.axis_size(axis)
    mine = lax.axis_index(axis)
    pieces = jnp.stack(jnp.split(value, count, axis=split_axis))
    got = []
    for shift in range(count):
        send = lax.dynamic_index_in_dim(pieces, (mine + shift) % count, 0, keepdims=False)
        if shift:
            send = lax.ppermute(send, axis, [(i, (i + shift) % count) for i in range(count)])
        got.append(send)
    stacked = jnp.take(jnp.stack(got), (mine - jnp.arange(count)) % count, axis=0)
    return jnp.concatenate([stacked[k] for k in range(count)], axis=concat_axis)


def adjacency(sources, targets, count_rows, total_rows):
    target_hot = (targets[:, None] == jnp.arange(count_rows, dtype=jnp.int32)[None, :]).astype(
        jnp.bfloat16
    )
    source_hot = (sources[:, None] == jnp.arange(total_rows, dtype=jnp.int32)[None, :]).astype(
        jnp.bfloat16
    )
    counts = lax.dot_general(
        target_hot, source_hot, (((0,), (0,)), ((), ())), preferred_element_type=jnp.float32
    )
    return counts.astype(jnp.bfloat16)


def gnn_forward(states, received, adjacent, w_message):
    extended = jnp.concatenate([states, received], axis=0)
    neighbours = jnp.dot(adjacent, extended, preferred_element_type=jnp.float32)
    counted = jnp.sum(adjacent.astype(jnp.float32), axis=1)
    inverse = 1.0 / (counted + 1.0)
    aggregate = ((states.astype(jnp.float32) + neighbours) * inverse[:, None]).astype(jnp.bfloat16)
    preact = jnp.dot(aggregate, w_message, preferred_element_type=jnp.float32)
    hidden = (states.astype(jnp.float32) + jax.nn.silu(preact)).astype(jnp.bfloat16)
    return (aggregate, preact, inverse, hidden)


def gnn_backward(upstream, aggregate, preact, inverse, adjacent, w_message):
    count_rows = aggregate.shape[0]
    up_float = upstream.astype(jnp.float32)
    sigmoid_val = jax.nn.sigmoid(preact)
    pre_grad = (up_float * sigmoid_val * (1.0 + preact * (1.0 - sigmoid_val))).astype(jnp.bfloat16)
    message_part = lax.dot_general(
        aggregate, pre_grad, (((0,), (0,)), ((), ())), preferred_element_type=jnp.float32
    )
    agg_grad = lax.dot_general(
        pre_grad, w_message, (((1,), (1,)), ((), ())), preferred_element_type=jnp.float32
    )
    term_grad = agg_grad * inverse[:, None]
    ext_grad = lax.dot_general(
        adjacent.astype(jnp.float32),
        term_grad,
        (((0,), (0,)), ((), ())),
        precision=lax.Precision.HIGHEST,
        preferred_element_type=jnp.float32,
    )
    local_grad = up_float + term_grad + ext_grad[:count_rows]
    halo_grad = ext_grad[count_rows:].astype(jnp.bfloat16)
    return (message_part, local_grad, halo_grad)


def attend(states, upstream, w_query, w_key, w_value):
    steps_all, nodes_here, width = states.shape
    head_dim = width // HEADS
    scale_factor = head_dim ** (-0.5)
    flat = states.reshape(steps_all * nodes_here, width)

    def project(weight):
        return jnp.dot(flat, weight, preferred_element_type=jnp.float32).astype(jnp.bfloat16)

    def splitter(matrix):
        return matrix.reshape(steps_all, nodes_here, HEADS, head_dim).astype(jnp.float32)

    queries = project(w_query)
    key_rows = project(w_key)
    value_rows = project(w_value)
    query_f = splitter(queries)
    key_f = splitter(key_rows)
    value_f = splitter(value_rows)
    scores = jnp.einsum("tnhd,snhd->nhts", query_f, key_f) * scale_factor
    causal = jnp.arange(steps_all)[:, None] >= jnp.arange(steps_all)[None, :]
    scores = jnp.where(causal, scores, -jnp.inf)
    highest = jnp.max(scores, axis=-1, keepdims=True)
    exponent = jnp.exp(scores - highest)
    probs = exponent / jnp.sum(exponent, axis=-1, keepdims=True)
    probs_low = probs.astype(jnp.bfloat16).astype(jnp.float32)
    up_heads = splitter(upstream)
    value_grad = jnp.einsum("nhts,tnhd->snhd", probs_low, up_heads).astype(jnp.bfloat16)
    prob_grad = jnp.einsum("tnhd,snhd->nhts", up_heads, value_f)
    score_grad = (
        probs * (prob_grad - jnp.sum(prob_grad * probs, axis=-1, keepdims=True)) * scale_factor
    ).astype(jnp.bfloat16)
    score_f = score_grad.astype(jnp.float32)
    query_grad = jnp.einsum("nhts,snhd->tnhd", score_f, key_f).astype(jnp.bfloat16)
    key_grad = jnp.einsum("nhts,tnhd->snhd", score_f, query_f).astype(jnp.bfloat16)
    query_flat = query_grad.reshape(steps_all * nodes_here, width)
    key_flat = key_grad.reshape(steps_all * nodes_here, width)
    value_flat = value_grad.reshape(steps_all * nodes_here, width)

    def weight_grad(grad_rows):
        return lax.dot_general(
            flat, grad_rows, (((0,), (0,)), ((), ())), preferred_element_type=jnp.float32
        )

    def input_grad(grad_rows, weight):
        return lax.dot_general(
            grad_rows, weight, (((1,), (1,)), ((), ())), preferred_element_type=jnp.float32
        )

    back = upstream.reshape(steps_all * nodes_here, width).astype(jnp.float32)
    back = (
        back
        + input_grad(query_flat, w_query)
        + input_grad(key_flat, w_key)
        + input_grad(value_flat, w_value)
    )
    back = back.astype(jnp.bfloat16).reshape(steps_all, nodes_here, width)
    return ((weight_grad(query_flat), weight_grad(key_flat), weight_grad(value_flat)), back)


def attend_blocked(states, upstream, w_query, w_key, w_value):
    steps_all, nodes_here, width = states.shape
    head_dim = width // HEADS
    scale_factor = head_dim ** (-0.5)
    per_group = max(1, 128 // steps_all)
    if nodes_here % per_group:
        per_group = 1
    groups = nodes_here // per_group
    block = per_group * steps_all
    flat = jnp.swapaxes(states, 0, 1).reshape(nodes_here * steps_all, width)
    up_flat = jnp.swapaxes(upstream, 0, 1).reshape(nodes_here * steps_all, width)

    def project(weight):
        return jnp.dot(flat, weight, preferred_element_type=jnp.float32).astype(jnp.bfloat16)

    def blocks(matrix):
        return matrix.reshape(groups, block, HEADS, head_dim)

    queries = blocks(project(w_query))
    key_rows = blocks(project(w_key))
    value_rows = blocks(project(w_value))
    up_heads = blocks(up_flat)
    position = jnp.arange(block)
    same = (position[:, None] // steps_all) == (position[None, :] // steps_all)
    causal = jnp.logical_and(same, (position[:, None] % steps_all) >= (position[None, :] % steps_all))

    def contract(spec, left, right):
        return jnp.einsum(spec, left, right, preferred_element_type=jnp.float32)

    scores = contract("gihd,gjhd->ghij", queries, key_rows) * scale_factor
    scores = jnp.where(causal, scores, -jnp.inf)
    highest = jnp.max(scores, axis=-1, keepdims=True)
    exponent = jnp.exp(scores - highest)
    probs = exponent / jnp.sum(exponent, axis=-1, keepdims=True)
    probs_low = probs.astype(jnp.bfloat16)
    value_grad = contract("ghij,gihd->gjhd", probs_low, up_heads).astype(jnp.bfloat16)
    prob_grad = contract("gihd,gjhd->ghij", up_heads, value_rows)
    score_grad = (
        probs * (prob_grad - jnp.sum(prob_grad * probs, axis=-1, keepdims=True)) * scale_factor
    ).astype(jnp.bfloat16)
    score_grad = lax.optimization_barrier(score_grad)
    query_grad = contract("ghij,gjhd->gihd", score_grad, key_rows).astype(jnp.bfloat16)
    key_grad = contract("ghij,gihd->gjhd", score_grad, queries).astype(jnp.bfloat16)
    query_flat = query_grad.reshape(-1, width)
    key_flat = key_grad.reshape(-1, width)
    value_flat = value_grad.reshape(-1, width)

    def weight_grad(grad_rows):
        return lax.dot_general(
            flat, grad_rows, (((0,), (0,)), ((), ())), preferred_element_type=jnp.float32
        )

    def input_grad(grad_rows, weight):
        return lax.dot_general(
            grad_rows, weight, (((1,), (1,)), ((), ())), preferred_element_type=jnp.float32
        )

    back = (
        up_flat.astype(jnp.float32)
        + input_grad(query_flat, w_query)
        + input_grad(key_flat, w_key)
        + input_grad(value_flat, w_value)
    )
    back = jnp.swapaxes(back.astype(jnp.bfloat16).reshape(nodes_here, steps_all, width), 0, 1)
    return ((weight_grad(query_flat), weight_grad(key_flat), weight_grad(value_flat)), back)


def local(
    node_states,
    edge_source,
    edge_target,
    halo_rows,
    halo_count,
    w_message,
    w_query,
    w_key,
    w_value,
    cotangent,
):
    days_local, node_local, width = node_states.shape
    halo_slots = halo_rows.shape[1]
    live = jnp.arange(halo_slots)[None, :] < halo_count
    rows = jnp.arange(node_local, dtype=jnp.int32)
    slot_hot = jnp.logical_and(
        halo_rows[:, :, None] == rows[None, None, :], live[:, :, None]
    ).astype(jnp.bfloat16)
    sent = jnp.einsum(
        "dsn,dnh->dsh", slot_hot, node_states, preferred_element_type=jnp.float32
    ).astype(jnp.bfloat16)
    received = from_behind(sent, "dom", 1)

    target_hot = (edge_target[:, :, None] == rows[None, None, :]).astype(jnp.bfloat16)
    local_hot = (edge_source[:, :, None] == rows[None, None, :]).astype(jnp.bfloat16)
    halo_ids = node_local + jnp.arange(halo_slots, dtype=jnp.int32)
    halo_hot = (edge_source[:, :, None] == halo_ids[None, None, :]).astype(jnp.bfloat16)
    adjacent_local = jnp.einsum(
        "der,des->drs", target_hot, local_hot, preferred_element_type=jnp.float32
    ).astype(jnp.bfloat16)
    adjacent_halo = jnp.einsum(
        "der,des->drs", target_hot, halo_hot, preferred_element_type=jnp.float32
    ).astype(jnp.bfloat16)
    counted = jnp.sum(target_hot.astype(jnp.float32), axis=1)
    inverse = 1.0 / (counted + 1.0)

    states_f = node_states.astype(jnp.float32)
    neighbours = jnp.einsum(
        "drs,dsh->drh", adjacent_local, node_states, preferred_element_type=jnp.float32
    ) + jnp.einsum("drs,dsh->drh", adjacent_halo, received, preferred_element_type=jnp.float32)
    aggregate = ((states_f + neighbours) * inverse[:, :, None]).astype(jnp.bfloat16)
    preact = jnp.einsum("drh,hk->drk", aggregate, w_message, preferred_element_type=jnp.float32)
    hidden = (states_f + jax.nn.silu(preact)).astype(jnp.bfloat16)

    day_count = lax.axis_size("day")
    upstream = cotangent.reshape(cotangent.shape[0], -1, width)
    piece = node_local // day_count
    halves = 2 if piece % 2 == 0 and (piece // 2) % max(1, 128 // upstream.shape[0]) == 0 else 1
    part = piece // halves
    split_hidden = hidden.reshape(days_local, day_count, halves, part, width)
    attn_grads, backs = None, []
    for half in range(halves):
        node_major = exchange(
            split_hidden[:, :, half].reshape(days_local, day_count * part, width), "day", 1, 0
        )
        grads, back = attend_blocked(
            node_major, upstream[:, half * part : (half + 1) * part], w_query, w_key, w_value
        )
        attn_grads = grads if attn_grads is None else tuple(a + b for a, b in zip(attn_grads, grads))
        backs.append(exchange(back, "day", 0, 1).reshape(days_local, day_count, part, width))
    back_days = jnp.stack(backs, axis=2).reshape(days_local, node_local, width)

    sigmoid_val = jax.nn.sigmoid(preact)
    pre_grad = (
        back_days.astype(jnp.float32) * sigmoid_val * (1.0 + preact * (1.0 - sigmoid_val))
    ).astype(jnp.bfloat16)
    grad_message = lax.dot_general(
        aggregate.reshape(-1, width),
        pre_grad.reshape(-1, width),
        (((0,), (0,)), ((), ())),
        preferred_element_type=jnp.float32,
    )
    agg_grad = jnp.einsum("drk,hk->drh", pre_grad, w_message, preferred_element_type=jnp.float32)
    term_grad = agg_grad * inverse[:, :, None]
    halo_grad = jnp.einsum(
        "drs,drh->dsh",
        adjacent_halo.astype(jnp.float32),
        term_grad,
        precision=lax.Precision.HIGHEST,
        preferred_element_type=jnp.float32,
    ).astype(jnp.bfloat16)
    returned = from_behind(halo_grad, "dom", -1)
    own_grad = jnp.einsum(
        "drs,drh->dsh",
        adjacent_local.astype(jnp.float32),
        term_grad,
        precision=lax.Precision.HIGHEST,
        preferred_element_type=jnp.float32,
    )
    scattered = jnp.einsum("dsn,dsh->dnh", slot_hot, returned, preferred_element_type=jnp.float32)
    state_grad = back_days.astype(jnp.float32) + term_grad + own_grad + scattered
    (grad_message, grad_query, grad_key, grad_value), state_grad = tree_sum(
        (grad_message, attn_grads[0], attn_grads[1], attn_grads[2]), ("dom", "day"), state_grad
    )
    return (state_grad, grad_message, grad_query, grad_key, grad_value)


def solution(mesh):
    return jax.shard_map(
        local,
        mesh=mesh,
        in_specs=(
            P("day", "dom", None),
            P("day", "dom"),
            P("day", "dom"),
            P("day", "dom"),
            P("day", "dom"),
            P(),
            P(),
            P(),
            P(),
            P(None, "dom", "day", None, None),
        ),
        out_specs=(P("day", "dom", None), P(), P(), P(), P()),
        check_vma=False,
    )
```

```python
import jax
import jax.numpy as jnp
from jax import lax
from jax.sharding import PartitionSpec as P

HEADS = 4


def from_behind(value, axis, steps):
    count = lax.axis_size(axis)
    pairs = [(source, (source + steps) % count) for source in range(count)]
    return lax.ppermute(value, axis, pairs)


def _power_of_two(count):
    return count > 0 and count & (count - 1) == 0


def _group_pairs(axis, stride, group, shift):
    pairs = []
    for source in range(lax.axis_size(axis)):
        digit = (source // stride) % group
        pairs.append((source, source + ((digit + shift) % group - digit) * stride))
    return pairs


def _scatter_step(flat, axis, stride, group):
    digit = (lax.axis_index(axis) // stride) % group
    chunks = flat.reshape(group, -1)
    total = lax.dynamic_index_in_dim(chunks, digit, 0, keepdims=False)
    for shift in range(1, group):
        send = lax.dynamic_index_in_dim(chunks, (digit + shift) % group, 0, keepdims=False)
        total = total + lax.ppermute(send, axis, _group_pairs(axis, stride, group, shift))
    return total


def _gather_step(flat, axis, stride, group):
    digit = (lax.axis_index(axis) // stride) % group
    if group == 2:
        other = lax.ppermute(flat, axis, _group_pairs(axis, stride, group, 1))
        return jnp.where(
            digit == 0, jnp.concatenate([flat, other]), jnp.concatenate([other, flat])
        )
    got = [flat] + [
        lax.ppermute(flat, axis, _group_pairs(axis, stride, group, shift)) for shift in range(1, group)
    ]
    stacked = jnp.stack(got)
    order = (digit - jnp.arange(group)) % group
    return jnp.take(stacked, order, axis=0).reshape(-1)


def _factors(size):
    if size <= 4:
        return [size]
    return [2] + _factors(size // 2)


def tree_sum(values, axes, companion=None):
    sizes = [lax.axis_size(axis) for axis in axes]
    flat = jnp.concatenate([value.reshape(-1) for value in values])
    total = 1
    for size in sizes:
        total *= size
    if not all(_power_of_two(size) for size in sizes) or flat.shape[0] % total:
        return lax.psum(tuple(values), axes), companion
    steps = []
    for axis, size in zip(axes, sizes):
        stride = 1
        for group in _factors(size):
            if group > 1:
                steps.append((axis, stride, group))
            stride *= group
    for axis, stride, group in steps:
        flat = _scatter_step(flat, axis, stride, group)
    flat, companion = lax.optimization_barrier((flat, companion))
    for axis, stride, group in reversed(steps):
        flat = _gather_step(flat, axis, stride, group)
    results, start = [], 0
    for value in values:
        results.append(flat[start : start + value.size].reshape(value.shape))
        start += value.size
    return tuple(results), companion


def exchange(value, axis, split_axis, concat_axis):
    count = lax.axis_size(axis)
    mine = lax.axis_index(axis)
    pieces = jnp.stack(jnp.split(value, count, axis=split_axis))
    got = []
    for shift in range(count):
        send = lax.dynamic_index_in_dim(pieces, (mine + shift) % count, 0, keepdims=False)
        if shift:
            send = lax.ppermute(send, axis, [(i, (i + shift) % count) for i in range(count)])
        got.append(send)
    stacked = jnp.take(jnp.stack(got), (mine - jnp.arange(count)) % count, axis=0)
    return jnp.concatenate([stacked[k] for k in range(count)], axis=concat_axis)


def adjacency(sources, targets, count_rows, total_rows):
    target_hot = (targets[:, None] == jnp.arange(count_rows, dtype=jnp.int32)[None, :]).astype(
        jnp.bfloat16
    )
    source_hot = (sources[:, None] == jnp.arange(total_rows, dtype=jnp.int32)[None, :]).astype(
        jnp.bfloat16
    )
    counts = lax.dot_general(
        target_hot, source_hot, (((0,), (0,)), ((), ())), preferred_element_type=jnp.float32
    )
    return counts.astype(jnp.bfloat16)


def gnn_forward(states, received, adjacent, w_message):
    extended = jnp.concatenate([states, received], axis=0)
    neighbours = jnp.dot(adjacent, extended, preferred_element_type=jnp.float32)
    counted = jnp.sum(adjacent.astype(jnp.float32), axis=1)
    inverse = 1.0 / (counted + 1.0)
    aggregate = ((states.astype(jnp.float32) + neighbours) * inverse[:, None]).astype(jnp.bfloat16)
    preact = jnp.dot(aggregate, w_message, preferred_element_type=jnp.float32)
    hidden = (states.astype(jnp.float32) + jax.nn.silu(preact)).astype(jnp.bfloat16)
    return (aggregate, preact, inverse, hidden)


def gnn_backward(upstream, aggregate, preact, inverse, adjacent, w_message):
    count_rows = aggregate.shape[0]
    up_float = upstream.astype(jnp.float32)
    sigmoid_val = jax.nn.sigmoid(preact)
    pre_grad = (up_float * sigmoid_val * (1.0 + preact * (1.0 - sigmoid_val))).astype(jnp.bfloat16)
    message_part = lax.dot_general(
        aggregate, pre_grad, (((0,), (0,)), ((), ())), preferred_element_type=jnp.float32
    )
    agg_grad = lax.dot_general(
        pre_grad, w_message, (((1,), (1,)), ((), ())), preferred_element_type=jnp.float32
    )
    term_grad = agg_grad * inverse[:, None]
    ext_grad = lax.dot_general(
        adjacent.astype(jnp.float32),
        term_grad,
        (((0,), (0,)), ((), ())),
        precision=lax.Precision.HIGHEST,
        preferred_element_type=jnp.float32,
    )
    local_grad = up_float + term_grad + ext_grad[:count_rows]
    halo_grad = ext_grad[count_rows:].astype(jnp.bfloat16)
    return (message_part, local_grad, halo_grad)


def attend(states, upstream, w_query, w_key, w_value):
    steps_all, nodes_here, width = states.shape
    head_dim = width // HEADS
    scale_factor = head_dim ** (-0.5)
    flat = states.reshape(steps_all * nodes_here, width)

    def project(weight):
        return jnp.dot(flat, weight, preferred_element_type=jnp.float32).astype(jnp.bfloat16)

    def splitter(matrix):
        return matrix.reshape(steps_all, nodes_here, HEADS, head_dim).astype(jnp.float32)

    queries = project(w_query)
    key_rows = project(w_key)
    value_rows = project(w_value)
    query_f = splitter(queries)
    key_f = splitter(key_rows)
    value_f = splitter(value_rows)
    scores = jnp.einsum("tnhd,snhd->nhts", query_f, key_f) * scale_factor
    causal = jnp.arange(steps_all)[:, None] >= jnp.arange(steps_all)[None, :]
    scores = jnp.where(causal, scores, -jnp.inf)
    highest = jnp.max(scores, axis=-1, keepdims=True)
    exponent = jnp.exp(scores - highest)
    probs = exponent / jnp.sum(exponent, axis=-1, keepdims=True)
    probs_low = probs.astype(jnp.bfloat16).astype(jnp.float32)
    up_heads = splitter(upstream)
    value_grad = jnp.einsum("nhts,tnhd->snhd", probs_low, up_heads).astype(jnp.bfloat16)
    prob_grad = jnp.einsum("tnhd,snhd->nhts", up_heads, value_f)
    score_grad = (
        probs * (prob_grad - jnp.sum(prob_grad * probs, axis=-1, keepdims=True)) * scale_factor
    ).astype(jnp.bfloat16)
    score_f = score_grad.astype(jnp.float32)
    query_grad = jnp.einsum("nhts,snhd->tnhd", score_f, key_f).astype(jnp.bfloat16)
    key_grad = jnp.einsum("nhts,tnhd->snhd", score_f, query_f).astype(jnp.bfloat16)
    query_flat = query_grad.reshape(steps_all * nodes_here, width)
    key_flat = key_grad.reshape(steps_all * nodes_here, width)
    value_flat = value_grad.reshape(steps_all * nodes_here, width)

    def weight_grad(grad_rows):
        return lax.dot_general(
            flat, grad_rows, (((0,), (0,)), ((), ())), preferred_element_type=jnp.float32
        )

    def input_grad(grad_rows, weight):
        return lax.dot_general(
            grad_rows, weight, (((1,), (1,)), ((), ())), preferred_element_type=jnp.float32
        )

    back = upstream.reshape(steps_all * nodes_here, width).astype(jnp.float32)
    back = (
        back
        + input_grad(query_flat, w_query)
        + input_grad(key_flat, w_key)
        + input_grad(value_flat, w_value)
    )
    back = back.astype(jnp.bfloat16).reshape(steps_all, nodes_here, width)
    return ((weight_grad(query_flat), weight_grad(key_flat), weight_grad(value_flat)), back)


def attend_blocked(states, upstream, w_query, w_key, w_value):
    steps_all, nodes_here, width = states.shape
    head_dim = width // HEADS
    scale_factor = head_dim ** (-0.5)
    per_group = max(1, 128 // steps_all)
    if nodes_here % per_group:
        per_group = 1
    groups = nodes_here // per_group
    block = per_group * steps_all
    flat = jnp.swapaxes(states, 0, 1).reshape(nodes_here * steps_all, width)
    up_flat = jnp.swapaxes(upstream, 0, 1).reshape(nodes_here * steps_all, width)

    def project(weight):
        return jnp.dot(flat, weight, preferred_element_type=jnp.float32).astype(jnp.bfloat16)

    def blocks(matrix):
        return matrix.reshape(groups, block, HEADS, head_dim)

    queries = blocks(project(w_query))
    key_rows = blocks(project(w_key))
    value_rows = blocks(project(w_value))
    up_heads = blocks(up_flat)
    position = jnp.arange(block)
    same = (position[:, None] // steps_all) == (position[None, :] // steps_all)
    causal = jnp.logical_and(same, (position[:, None] % steps_all) >= (position[None, :] % steps_all))

    def contract(spec, left, right):
        return jnp.einsum(spec, left, right, preferred_element_type=jnp.float32)

    scores = contract("gihd,gjhd->ghij", queries, key_rows) * scale_factor
    scores = jnp.where(causal, scores, -jnp.inf)
    highest = jnp.max(scores, axis=-1, keepdims=True)
    exponent = jnp.exp(scores - highest)
    probs = exponent / jnp.sum(exponent, axis=-1, keepdims=True)
    probs_low = probs.astype(jnp.bfloat16)
    value_grad = contract("ghij,gihd->gjhd", probs_low, up_heads).astype(jnp.bfloat16)
    prob_grad = contract("gihd,gjhd->ghij", up_heads, value_rows)
    score_grad = (
        probs * (prob_grad - jnp.sum(prob_grad * probs, axis=-1, keepdims=True)) * scale_factor
    ).astype(jnp.bfloat16)
    score_grad = lax.optimization_barrier(score_grad)
    query_grad = contract("ghij,gjhd->gihd", score_grad, key_rows).astype(jnp.bfloat16)
    key_grad = contract("ghij,gihd->gjhd", score_grad, queries).astype(jnp.bfloat16)
    query_flat = query_grad.reshape(-1, width)
    key_flat = key_grad.reshape(-1, width)
    value_flat = value_grad.reshape(-1, width)

    def weight_grad(grad_rows):
        return lax.dot_general(
            flat, grad_rows, (((0,), (0,)), ((), ())), preferred_element_type=jnp.float32
        )

    def input_grad(grad_rows, weight):
        return lax.dot_general(
            grad_rows, weight, (((1,), (1,)), ((), ())), preferred_element_type=jnp.float32
        )

    back = (
        up_flat.astype(jnp.float32)
        + input_grad(query_flat, w_query)
        + input_grad(key_flat, w_key)
        + input_grad(value_flat, w_value)
    )
    back = jnp.swapaxes(back.astype(jnp.bfloat16).reshape(nodes_here, steps_all, width), 0, 1)
    return ((weight_grad(query_flat), weight_grad(key_flat), weight_grad(value_flat)), back)


def local(
    node_states,
    edge_source,
    edge_target,
    halo_rows,
    halo_count,
    w_message,
    w_query,
    w_key,
    w_value,
    cotangent,
):
    days_local, node_local, width = node_states.shape
    halo_slots = halo_rows.shape[1]
    live = jnp.arange(halo_slots)[None, :] < halo_count
    rows = jnp.arange(node_local, dtype=jnp.int32)
    slot_hot = jnp.logical_and(
        halo_rows[:, :, None] == rows[None, None, :], live[:, :, None]
    ).astype(jnp.bfloat16)
    sent = jnp.einsum(
        "dsn,dnh->dsh", slot_hot, node_states, preferred_element_type=jnp.float32
    ).astype(jnp.bfloat16)
    received = from_behind(sent, "dom", 1)

    target_hot = (edge_target[:, :, None] == rows[None, None, :]).astype(jnp.bfloat16)
    local_hot = (edge_source[:, :, None] == rows[None, None, :]).astype(jnp.bfloat16)
    halo_ids = node_local + jnp.arange(halo_slots, dtype=jnp.int32)
    halo_hot = (edge_source[:, :, None] == halo_ids[None, None, :]).astype(jnp.bfloat16)
    adjacent_local = jnp.einsum(
        "der,des->drs", target_hot, local_hot, preferred_element_type=jnp.float32
    ).astype(jnp.bfloat16)
    adjacent_halo = jnp.einsum(
        "der,des->drs", target_hot, halo_hot, preferred_element_type=jnp.float32
    ).astype(jnp.bfloat16)
    counted = jnp.sum(target_hot.astype(jnp.float32), axis=1)
    inverse = 1.0 / (counted + 1.0)

    states_f = node_states.astype(jnp.float32)
    neighbours = jnp.einsum(
        "drs,dsh->drh", adjacent_local, node_states, preferred_element_type=jnp.float32
    ) + jnp.einsum("drs,dsh->drh", adjacent_halo, received, preferred_element_type=jnp.float32)
    aggregate = ((states_f + neighbours) * inverse[:, :, None]).astype(jnp.bfloat16)
    preact = jnp.einsum("drh,hk->drk", aggregate, w_message, preferred_element_type=jnp.float32)
    hidden = (states_f + jax.nn.silu(preact)).astype(jnp.bfloat16)

    node_major = exchange(hidden, "day", 1, 0)
    upstream = cotangent.reshape(cotangent.shape[0], -1, width)
    attn_grads, back = attend_blocked(node_major, upstream, w_query, w_key, w_value)
    back_days = exchange(back, "day", 0, 1)

    sigmoid_val = jax.nn.sigmoid(preact)
    pre_grad = (
        back_days.astype(jnp.float32) * sigmoid_val * (1.0 + preact * (1.0 - sigmoid_val))
    ).astype(jnp.bfloat16)
    grad_message = lax.dot_general(
        aggregate.reshape(-1, width),
        pre_grad.reshape(-1, width),
        (((0,), (0,)), ((), ())),
        preferred_element_type=jnp.float32,
    )
    agg_grad = jnp.einsum("drk,hk->drh", pre_grad, w_message, preferred_element_type=jnp.float32)
    term_grad = agg_grad * inverse[:, :, None]
    halo_grad = jnp.einsum(
        "drs,drh->dsh",
        adjacent_halo.astype(jnp.float32),
        term_grad,
        precision=lax.Precision.HIGHEST,
        preferred_element_type=jnp.float32,
    ).astype(jnp.bfloat16)
    returned = from_behind(halo_grad, "dom", -1)
    own_grad = jnp.einsum(
        "drs,drh->dsh",
        adjacent_local.astype(jnp.float32),
        term_grad,
        precision=lax.Precision.HIGHEST,
        preferred_element_type=jnp.float32,
    )
    scattered = jnp.einsum("dsn,dsh->dnh", slot_hot, returned, preferred_element_type=jnp.float32)
    state_grad = back_days.astype(jnp.float32) + term_grad + own_grad + scattered
    (grad_message, grad_query, grad_key, grad_value), state_grad = tree_sum(
        (grad_message, attn_grads[0], attn_grads[1], attn_grads[2]), ("dom", "day"), state_grad
    )
    return (state_grad, grad_message, grad_query, grad_key, grad_value)


def solution(mesh):
    return jax.shard_map(
        local,
        mesh=mesh,
        in_specs=(
            P("day", "dom", None),
            P("day", "dom"),
            P("day", "dom"),
            P("day", "dom"),
            P("day", "dom"),
            P(),
            P(),
            P(),
            P(),
            P(None, "dom", "day", None, None),
        ),
        out_specs=(P("day", "dom", None), P(), P(), P(), P()),
        check_vma=False,
    )
```

```python
import jax
import jax.numpy as jnp
from jax import lax
from jax.sharding import PartitionSpec as P

HEADS = 4


def from_behind(value, axis, steps):
    count = lax.axis_size(axis)
    pairs = [(source, (source + steps) % count) for source in range(count)]
    return lax.ppermute(value, axis, pairs)


def _power_of_two(count):
    return count > 0 and count & (count - 1) == 0


def _group_pairs(axis, stride, group, shift):
    pairs = []
    for source in range(lax.axis_size(axis)):
        digit = (source // stride) % group
        pairs.append((source, source + ((digit + shift) % group - digit) * stride))
    return pairs


def _scatter_step(flat, axis, stride, group):
    digit = (lax.axis_index(axis) // stride) % group
    chunks = flat.reshape(group, -1)
    if group == 2:
        keep = jnp.where(digit == 0, chunks[0], chunks[1])
        send = jnp.where(digit == 0, chunks[1], chunks[0])
        return keep + lax.ppermute(send, axis, _group_pairs(axis, stride, group, 1))
    total = lax.dynamic_index_in_dim(chunks, digit, 0, keepdims=False)
    for shift in range(1, group):
        send = lax.dynamic_index_in_dim(chunks, (digit + shift) % group, 0, keepdims=False)
        total = total + lax.ppermute(send, axis, _group_pairs(axis, stride, group, shift))
    return total


def _gather_step(flat, axis, stride, group):
    digit = (lax.axis_index(axis) // stride) % group
    if group == 2:
        other = lax.ppermute(flat, axis, _group_pairs(axis, stride, group, 1))
        return jnp.where(
            digit == 0, jnp.concatenate([flat, other]), jnp.concatenate([other, flat])
        )
    got = [flat] + [
        lax.ppermute(flat, axis, _group_pairs(axis, stride, group, shift)) for shift in range(1, group)
    ]
    stacked = jnp.stack(got)
    order = (digit - jnp.arange(group)) % group
    return jnp.take(stacked, order, axis=0).reshape(-1)


def _factors(size):
    if size <= 4:
        return [size]
    return [2] + _factors(size // 2)


def tree_sum(values, axes, companion=None):
    sizes = [lax.axis_size(axis) for axis in axes]
    flat = jnp.concatenate([value.reshape(-1) for value in values])
    total = 1
    for size in sizes:
        total *= size
    if not all(_power_of_two(size) for size in sizes) or flat.shape[0] % total:
        return lax.psum(tuple(values), axes), companion
    steps = []
    for axis, size in zip(axes, sizes):
        stride = 1
        for group in _factors(size):
            if group > 1:
                steps.append((axis, stride, group))
            stride *= group
    for axis, stride, group in steps:
        flat = _scatter_step(flat, axis, stride, group)
    flat, companion = lax.optimization_barrier((flat, companion))
    for axis, stride, group in reversed(steps):
        flat = _gather_step(flat, axis, stride, group)
    results, start = [], 0
    for value in values:
        results.append(flat[start : start + value.size].reshape(value.shape))
        start += value.size
    return tuple(results), companion


def exchange(value, axis, split_axis, concat_axis):
    count = lax.axis_size(axis)
    mine = lax.axis_index(axis)
    size = value.shape[split_axis] // count
    got = []
    for shift in range(count):
        send = lax.dynamic_slice_in_dim(value, ((mine + shift) % count) * size, size, axis=split_axis)
        if shift:
            send = lax.ppermute(send, axis, [(i, (i + shift) % count) for i in range(count)])
        got.append(send)
    stacked = jnp.take(jnp.stack(got), (mine - jnp.arange(count)) % count, axis=0)
    return jnp.concatenate([stacked[k] for k in range(count)], axis=concat_axis)


def adjacency(sources, targets, count_rows, total_rows):
    target_hot = (targets[:, None] == jnp.arange(count_rows, dtype=jnp.int32)[None, :]).astype(
        jnp.bfloat16
    )
    source_hot = (sources[:, None] == jnp.arange(total_rows, dtype=jnp.int32)[None, :]).astype(
        jnp.bfloat16
    )
    counts = lax.dot_general(
        target_hot, source_hot, (((0,), (0,)), ((), ())), preferred_element_type=jnp.float32
    )
    return counts.astype(jnp.bfloat16)


def gnn_forward(states, received, adjacent, w_message):
    extended = jnp.concatenate([states, received], axis=0)
    neighbours = jnp.dot(adjacent, extended, preferred_element_type=jnp.float32)
    counted = jnp.sum(adjacent.astype(jnp.float32), axis=1)
    inverse = 1.0 / (counted + 1.0)
    aggregate = ((states.astype(jnp.float32) + neighbours) * inverse[:, None]).astype(jnp.bfloat16)
    preact = jnp.dot(aggregate, w_message, preferred_element_type=jnp.float32)
    hidden = (states.astype(jnp.float32) + jax.nn.silu(preact)).astype(jnp.bfloat16)
    return (aggregate, preact, inverse, hidden)


def gnn_backward(upstream, aggregate, preact, inverse, adjacent, w_message):
    count_rows = aggregate.shape[0]
    up_float = upstream.astype(jnp.float32)
    sigmoid_val = jax.nn.sigmoid(preact)
    pre_grad = (up_float * sigmoid_val * (1.0 + preact * (1.0 - sigmoid_val))).astype(jnp.bfloat16)
    message_part = lax.dot_general(
        aggregate, pre_grad, (((0,), (0,)), ((), ())), preferred_element_type=jnp.float32
    )
    agg_grad = lax.dot_general(
        pre_grad, w_message, (((1,), (1,)), ((), ())), preferred_element_type=jnp.float32
    )
    term_grad = agg_grad * inverse[:, None]
    ext_grad = lax.dot_general(
        adjacent.astype(jnp.float32),
        term_grad,
        (((0,), (0,)), ((), ())),
        precision=lax.Precision.HIGHEST,
        preferred_element_type=jnp.float32,
    )
    local_grad = up_float + term_grad + ext_grad[:count_rows]
    halo_grad = ext_grad[count_rows:].astype(jnp.bfloat16)
    return (message_part, local_grad, halo_grad)


def attend(states, upstream, w_query, w_key, w_value):
    steps_all, nodes_here, width = states.shape
    head_dim = width // HEADS
    scale_factor = head_dim ** (-0.5)
    flat = states.reshape(steps_all * nodes_here, width)

    def project(weight):
        return jnp.dot(flat, weight, preferred_element_type=jnp.float32).astype(jnp.bfloat16)

    def splitter(matrix):
        return matrix.reshape(steps_all, nodes_here, HEADS, head_dim).astype(jnp.float32)

    queries = project(w_query)
    key_rows = project(w_key)
    value_rows = project(w_value)
    query_f = splitter(queries)
    key_f = splitter(key_rows)
    value_f = splitter(value_rows)
    scores = jnp.einsum("tnhd,snhd->nhts", query_f, key_f) * scale_factor
    causal = jnp.arange(steps_all)[:, None] >= jnp.arange(steps_all)[None, :]
    scores = jnp.where(causal, scores, -jnp.inf)
    highest = jnp.max(scores, axis=-1, keepdims=True)
    exponent = jnp.exp(scores - highest)
    probs = exponent / jnp.sum(exponent, axis=-1, keepdims=True)
    probs_low = probs.astype(jnp.bfloat16).astype(jnp.float32)
    up_heads = splitter(upstream)
    value_grad = jnp.einsum("nhts,tnhd->snhd", probs_low, up_heads).astype(jnp.bfloat16)
    prob_grad = jnp.einsum("tnhd,snhd->nhts", up_heads, value_f)
    score_grad = (
        probs * (prob_grad - jnp.sum(prob_grad * probs, axis=-1, keepdims=True)) * scale_factor
    ).astype(jnp.bfloat16)
    score_f = score_grad.astype(jnp.float32)
    query_grad = jnp.einsum("nhts,snhd->tnhd", score_f, key_f).astype(jnp.bfloat16)
    key_grad = jnp.einsum("nhts,tnhd->snhd", score_f, query_f).astype(jnp.bfloat16)
    query_flat = query_grad.reshape(steps_all * nodes_here, width)
    key_flat = key_grad.reshape(steps_all * nodes_here, width)
    value_flat = value_grad.reshape(steps_all * nodes_here, width)

    def weight_grad(grad_rows):
        return lax.dot_general(
            flat, grad_rows, (((0,), (0,)), ((), ())), preferred_element_type=jnp.float32
        )

    def input_grad(grad_rows, weight):
        return lax.dot_general(
            grad_rows, weight, (((1,), (1,)), ((), ())), preferred_element_type=jnp.float32
        )

    back = upstream.reshape(steps_all * nodes_here, width).astype(jnp.float32)
    back = (
        back
        + input_grad(query_flat, w_query)
        + input_grad(key_flat, w_key)
        + input_grad(value_flat, w_value)
    )
    back = back.astype(jnp.bfloat16).reshape(steps_all, nodes_here, width)
    return ((weight_grad(query_flat), weight_grad(key_flat), weight_grad(value_flat)), back)


def attend_blocked(states, upstream, w_query, w_key, w_value):
    steps_all, nodes_here, width = states.shape
    head_dim = width // HEADS
    scale_factor = head_dim ** (-0.5)
    per_group = max(1, 128 // steps_all)
    if nodes_here % per_group:
        per_group = 1
    groups = nodes_here // per_group
    block = per_group * steps_all
    flat = jnp.swapaxes(states, 0, 1).reshape(nodes_here * steps_all, width)
    up_flat = jnp.swapaxes(upstream, 0, 1).reshape(nodes_here * steps_all, width)

    def project(weight):
        return jnp.dot(flat, weight, preferred_element_type=jnp.float32).astype(jnp.bfloat16)

    def blocks(matrix):
        return matrix.reshape(groups, block, HEADS, head_dim)

    queries = blocks(project(w_query))
    key_rows = blocks(project(w_key))
    value_rows = blocks(project(w_value))
    up_heads = blocks(up_flat)
    position = jnp.arange(block)
    same = (position[:, None] // steps_all) == (position[None, :] // steps_all)
    causal = jnp.logical_and(same, (position[:, None] % steps_all) >= (position[None, :] % steps_all))

    def contract(spec, left, right):
        return jnp.einsum(spec, left, right, preferred_element_type=jnp.float32)

    scores = contract("gihd,gjhd->ghij", queries, key_rows) * scale_factor
    scores = jnp.where(causal, scores, -jnp.inf)
    highest = jnp.max(scores, axis=-1, keepdims=True)
    exponent = jnp.exp(scores - highest)
    probs = exponent / jnp.sum(exponent, axis=-1, keepdims=True)
    probs_low = probs.astype(jnp.bfloat16)
    value_grad = contract("ghij,gihd->gjhd", probs_low, up_heads).astype(jnp.bfloat16)
    prob_grad = contract("gihd,gjhd->ghij", up_heads, value_rows)
    score_grad = (
        probs * (prob_grad - jnp.sum(prob_grad * probs, axis=-1, keepdims=True)) * scale_factor
    ).astype(jnp.bfloat16)
    score_grad = lax.optimization_barrier(score_grad)
    query_grad = contract("ghij,gjhd->gihd", score_grad, key_rows).astype(jnp.bfloat16)
    key_grad = contract("ghij,gihd->gjhd", score_grad, queries).astype(jnp.bfloat16)
    query_flat = query_grad.reshape(-1, width)
    key_flat = key_grad.reshape(-1, width)
    value_flat = value_grad.reshape(-1, width)

    def weight_grad(grad_rows):
        return lax.dot_general(
            flat, grad_rows, (((0,), (0,)), ((), ())), preferred_element_type=jnp.float32
        )

    def input_grad(grad_rows, weight):
        return lax.dot_general(
            grad_rows, weight, (((1,), (1,)), ((), ())), preferred_element_type=jnp.float32
        )

    back = (
        up_flat.astype(jnp.float32)
        + input_grad(query_flat, w_query)
        + input_grad(key_flat, w_key)
        + input_grad(value_flat, w_value)
    )
    back = jnp.swapaxes(back.astype(jnp.bfloat16).reshape(nodes_here, steps_all, width), 0, 1)
    return ((weight_grad(query_flat), weight_grad(key_flat), weight_grad(value_flat)), back)


def local(
    node_states,
    edge_source,
    edge_target,
    halo_rows,
    halo_count,
    w_message,
    w_query,
    w_key,
    w_value,
    cotangent,
):
    days_local, node_local, width = node_states.shape
    halo_slots = halo_rows.shape[1]
    live = jnp.arange(halo_slots)[None, :] < halo_count
    rows = jnp.arange(node_local, dtype=jnp.int32)
    slot_hot = jnp.logical_and(
        halo_rows[:, :, None] == rows[None, None, :], live[:, :, None]
    ).astype(jnp.bfloat16)
    sent = jnp.einsum(
        "dsn,dnh->dsh", slot_hot, node_states, preferred_element_type=jnp.float32
    ).astype(jnp.bfloat16)
    received = from_behind(sent, "dom", 1)

    target_hot = (edge_target[:, :, None] == rows[None, None, :]).astype(jnp.bfloat16)
    local_hot = (edge_source[:, :, None] == rows[None, None, :]).astype(jnp.bfloat16)
    halo_ids = node_local + jnp.arange(halo_slots, dtype=jnp.int32)
    halo_hot = (edge_source[:, :, None] == halo_ids[None, None, :]).astype(jnp.bfloat16)
    adjacent_local = jnp.einsum(
        "der,des->drs", target_hot, local_hot, preferred_element_type=jnp.float32
    ).astype(jnp.bfloat16)
    adjacent_halo = jnp.einsum(
        "der,des->drs", target_hot, halo_hot, preferred_element_type=jnp.float32
    ).astype(jnp.bfloat16)
    counted = jnp.sum(target_hot.astype(jnp.float32), axis=1)
    inverse = 1.0 / (counted + 1.0)

    states_f = node_states.astype(jnp.float32)
    neighbours = jnp.einsum(
        "drs,dsh->drh", adjacent_local, node_states, preferred_element_type=jnp.float32
    ) + jnp.einsum("drs,dsh->drh", adjacent_halo, received, preferred_element_type=jnp.float32)
    aggregate = ((states_f + neighbours) * inverse[:, :, None]).astype(jnp.bfloat16)
    preact = jnp.einsum("drh,hk->drk", aggregate, w_message, preferred_element_type=jnp.float32)
    hidden = (states_f + jax.nn.silu(preact)).astype(jnp.bfloat16)

    node_major = exchange(hidden, "day", 1, 0)
    upstream = cotangent.reshape(cotangent.shape[0], -1, width)
    attn_grads, back = attend_blocked(node_major, upstream, w_query, w_key, w_value)
    back_days = exchange(back, "day", 0, 1)

    sigmoid_val = jax.nn.sigmoid(preact)
    pre_grad = (
        back_days.astype(jnp.float32) * sigmoid_val * (1.0 + preact * (1.0 - sigmoid_val))
    ).astype(jnp.bfloat16)
    grad_message = lax.dot_general(
        aggregate.reshape(-1, width),
        pre_grad.reshape(-1, width),
        (((0,), (0,)), ((), ())),
        preferred_element_type=jnp.float32,
    )
    agg_grad = jnp.einsum("drk,hk->drh", pre_grad, w_message, preferred_element_type=jnp.float32)
    term_grad = agg_grad * inverse[:, :, None]
    halo_grad = jnp.einsum(
        "drs,drh->dsh",
        adjacent_halo.astype(jnp.float32),
        term_grad,
        precision=lax.Precision.HIGHEST,
        preferred_element_type=jnp.float32,
    ).astype(jnp.bfloat16)
    returned = from_behind(halo_grad, "dom", -1)
    own_grad = jnp.einsum(
        "drs,drh->dsh",
        adjacent_local.astype(jnp.float32),
        term_grad,
        precision=lax.Precision.HIGHEST,
        preferred_element_type=jnp.float32,
    )
    scattered = jnp.einsum("dsn,dsh->dnh", slot_hot, returned, preferred_element_type=jnp.float32)
    state_grad = back_days.astype(jnp.float32) + term_grad + own_grad + scattered
    (grad_message, grad_query, grad_key, grad_value), state_grad = tree_sum(
        (grad_message, attn_grads[0], attn_grads[1], attn_grads[2]), ("dom", "day"), state_grad
    )
    return (state_grad, grad_message, grad_query, grad_key, grad_value)


def solution(mesh):
    return jax.shard_map(
        local,
        mesh=mesh,
        in_specs=(
            P("day", "dom", None),
            P("day", "dom"),
            P("day", "dom"),
            P("day", "dom"),
            P("day", "dom"),
            P(),
            P(),
            P(),
            P(),
            P(None, "dom", "day", None, None),
        ),
        out_specs=(P("day", "dom", None), P(), P(), P(), P()),
        check_vma=False,
    )
```

```python
import jax
import jax.numpy as jnp
from jax import lax
from jax.sharding import PartitionSpec as P

HEADS = 4


def from_behind(value, axis, steps):
    count = lax.axis_size(axis)
    pairs = [(source, (source + steps) % count) for source in range(count)]
    return lax.ppermute(value, axis, pairs)


def _power_of_two(count):
    return count > 0 and count & (count - 1) == 0


def _group_pairs(axis, stride, group, shift):
    pairs = []
    for source in range(lax.axis_size(axis)):
        digit = (source // stride) % group
        pairs.append((source, source + ((digit + shift) % group - digit) * stride))
    return pairs


def _scatter_step(flat, axis, stride, group):
    digit = (lax.axis_index(axis) // stride) % group
    chunks = flat.reshape(group, -1)
    if group == 2:
        keep = jnp.where(digit == 0, chunks[0], chunks[1])
        send = jnp.where(digit == 0, chunks[1], chunks[0])
        return keep + lax.ppermute(send, axis, _group_pairs(axis, stride, group, 1))
    total = lax.dynamic_index_in_dim(chunks, digit, 0, keepdims=False)
    for shift in range(1, group):
        send = lax.dynamic_index_in_dim(chunks, (digit + shift) % group, 0, keepdims=False)
        total = total + lax.ppermute(send, axis, _group_pairs(axis, stride, group, shift))
    return total


def _gather_step(flat, axis, stride, group):
    digit = (lax.axis_index(axis) // stride) % group
    if group == 2:
        other = lax.ppermute(flat, axis, _group_pairs(axis, stride, group, 1))
        return jnp.where(
            digit == 0, jnp.concatenate([flat, other]), jnp.concatenate([other, flat])
        )
    got = [flat] + [
        lax.ppermute(flat, axis, _group_pairs(axis, stride, group, shift)) for shift in range(1, group)
    ]
    stacked = jnp.stack(got)
    order = (digit - jnp.arange(group)) % group
    return jnp.take(stacked, order, axis=0).reshape(-1)


def _factors(size):
    if size <= 4:
        return [size]
    return [2] + _factors(size // 2)


def tree_sum(values, axes, companion=None):
    sizes = [lax.axis_size(axis) for axis in axes]
    flat = jnp.concatenate([value.reshape(-1) for value in values])
    total = 1
    for size in sizes:
        total *= size
    if not all(_power_of_two(size) for size in sizes) or flat.shape[0] % total:
        return lax.psum(tuple(values), axes), companion
    steps = []
    for axis, size in zip(axes, sizes):
        stride = 1
        for group in _factors(size):
            if group > 1:
                steps.append((axis, stride, group))
            stride *= group
    for axis, stride, group in steps:
        flat = _scatter_step(flat, axis, stride, group)
    flat, companion = lax.optimization_barrier((flat, companion))
    for axis, stride, group in reversed(steps):
        flat = _gather_step(flat, axis, stride, group)
    results, start = [], 0
    for value in values:
        results.append(flat[start : start + value.size].reshape(value.shape))
        start += value.size
    return tuple(results), companion


def exchange(value, axis, split_axis, concat_axis):
    count = lax.axis_size(axis)
    mine = lax.axis_index(axis)
    size = value.shape[split_axis] // count
    got = []
    for shift in range(count):
        send = lax.dynamic_slice_in_dim(value, ((mine + shift) % count) * size, size, axis=split_axis)
        if shift:
            send = lax.ppermute(send, axis, [(i, (i + shift) % count) for i in range(count)])
        got.append(send)
    stacked = jnp.take(jnp.stack(got), (mine - jnp.arange(count)) % count, axis=0)
    return jnp.concatenate([stacked[k] for k in range(count)], axis=concat_axis)


def adjacency(sources, targets, count_rows, total_rows):
    target_hot = (targets[:, None] == jnp.arange(count_rows, dtype=jnp.int32)[None, :]).astype(
        jnp.bfloat16
    )
    source_hot = (sources[:, None] == jnp.arange(total_rows, dtype=jnp.int32)[None, :]).astype(
        jnp.bfloat16
    )
    counts = lax.dot_general(
        target_hot, source_hot, (((0,), (0,)), ((), ())), preferred_element_type=jnp.float32
    )
    return counts.astype(jnp.bfloat16)


def gnn_forward(states, received, adjacent, w_message):
    extended = jnp.concatenate([states, received], axis=0)
    neighbours = jnp.dot(adjacent, extended, preferred_element_type=jnp.float32)
    counted = jnp.sum(adjacent.astype(jnp.float32), axis=1)
    inverse = 1.0 / (counted + 1.0)
    aggregate = ((states.astype(jnp.float32) + neighbours) * inverse[:, None]).astype(jnp.bfloat16)
    preact = jnp.dot(aggregate, w_message, preferred_element_type=jnp.float32)
    hidden = (states.astype(jnp.float32) + jax.nn.silu(preact)).astype(jnp.bfloat16)
    return (aggregate, preact, inverse, hidden)


def gnn_backward(upstream, aggregate, preact, inverse, adjacent, w_message):
    count_rows = aggregate.shape[0]
    up_float = upstream.astype(jnp.float32)
    sigmoid_val = jax.nn.sigmoid(preact)
    pre_grad = (up_float * sigmoid_val * (1.0 + preact * (1.0 - sigmoid_val))).astype(jnp.bfloat16)
    message_part = lax.dot_general(
        aggregate, pre_grad, (((0,), (0,)), ((), ())), preferred_element_type=jnp.float32
    )
    agg_grad = lax.dot_general(
        pre_grad, w_message, (((1,), (1,)), ((), ())), preferred_element_type=jnp.float32
    )
    term_grad = agg_grad * inverse[:, None]
    ext_grad = lax.dot_general(
        adjacent.astype(jnp.float32),
        term_grad,
        (((0,), (0,)), ((), ())),
        precision=lax.Precision.HIGHEST,
        preferred_element_type=jnp.float32,
    )
    local_grad = up_float + term_grad + ext_grad[:count_rows]
    halo_grad = ext_grad[count_rows:].astype(jnp.bfloat16)
    return (message_part, local_grad, halo_grad)


def attend(states, upstream, w_query, w_key, w_value):
    steps_all, nodes_here, width = states.shape
    head_dim = width // HEADS
    scale_factor = head_dim ** (-0.5)
    flat = states.reshape(steps_all * nodes_here, width)

    def project(weight):
        return jnp.dot(flat, weight, preferred_element_type=jnp.float32).astype(jnp.bfloat16)

    def splitter(matrix):
        return matrix.reshape(steps_all, nodes_here, HEADS, head_dim).astype(jnp.float32)

    queries = project(w_query)
    key_rows = project(w_key)
    value_rows = project(w_value)
    query_f = splitter(queries)
    key_f = splitter(key_rows)
    value_f = splitter(value_rows)
    scores = jnp.einsum("tnhd,snhd->nhts", query_f, key_f) * scale_factor
    causal = jnp.arange(steps_all)[:, None] >= jnp.arange(steps_all)[None, :]
    scores = jnp.where(causal, scores, -jnp.inf)
    highest = jnp.max(scores, axis=-1, keepdims=True)
    exponent = jnp.exp(scores - highest)
    probs = exponent / jnp.sum(exponent, axis=-1, keepdims=True)
    probs_low = probs.astype(jnp.bfloat16).astype(jnp.float32)
    up_heads = splitter(upstream)
    value_grad = jnp.einsum("nhts,tnhd->snhd", probs_low, up_heads).astype(jnp.bfloat16)
    prob_grad = jnp.einsum("tnhd,snhd->nhts", up_heads, value_f)
    score_grad = (
        probs * (prob_grad - jnp.sum(prob_grad * probs, axis=-1, keepdims=True)) * scale_factor
    ).astype(jnp.bfloat16)
    score_f = score_grad.astype(jnp.float32)
    query_grad = jnp.einsum("nhts,snhd->tnhd", score_f, key_f).astype(jnp.bfloat16)
    key_grad = jnp.einsum("nhts,tnhd->snhd", score_f, query_f).astype(jnp.bfloat16)
    query_flat = query_grad.reshape(steps_all * nodes_here, width)
    key_flat = key_grad.reshape(steps_all * nodes_here, width)
    value_flat = value_grad.reshape(steps_all * nodes_here, width)

    def weight_grad(grad_rows):
        return lax.dot_general(
            flat, grad_rows, (((0,), (0,)), ((), ())), preferred_element_type=jnp.float32
        )

    def input_grad(grad_rows, weight):
        return lax.dot_general(
            grad_rows, weight, (((1,), (1,)), ((), ())), preferred_element_type=jnp.float32
        )

    back = upstream.reshape(steps_all * nodes_here, width).astype(jnp.float32)
    back = (
        back
        + input_grad(query_flat, w_query)
        + input_grad(key_flat, w_key)
        + input_grad(value_flat, w_value)
    )
    back = back.astype(jnp.bfloat16).reshape(steps_all, nodes_here, width)
    return ((weight_grad(query_flat), weight_grad(key_flat), weight_grad(value_flat)), back)


def attend_blocked(states, upstream, w_query, w_key, w_value):
    steps_all, nodes_here, width = states.shape
    head_dim = width // HEADS
    scale_factor = head_dim ** (-0.5)
    per_group = max(1, 128 // steps_all)
    if nodes_here % per_group:
        per_group = 1
    groups = nodes_here // per_group
    block = per_group * steps_all
    flat = jnp.swapaxes(states, 0, 1).reshape(groups, block, width)
    up_flat = jnp.swapaxes(upstream, 0, 1).reshape(groups, block, width)
    heads_of = {
        name: weight.reshape(width, HEADS, head_dim)
        for name, weight in (("q", w_query), ("k", w_key), ("v", w_value))
    }

    def contract(spec, left, right):
        return jnp.einsum(spec, left, right, preferred_element_type=jnp.float32)

    queries = contract("gic,chd->ghid", flat, heads_of["q"]).astype(jnp.bfloat16)
    key_rows = contract("gic,chd->ghid", flat, heads_of["k"]).astype(jnp.bfloat16)
    value_rows = contract("gic,chd->ghid", flat, heads_of["v"]).astype(jnp.bfloat16)
    up_heads = up_flat.reshape(groups, block, HEADS, head_dim)
    position = jnp.arange(block)
    same = (position[:, None] // steps_all) == (position[None, :] // steps_all)
    causal = jnp.logical_and(same, (position[:, None] % steps_all) >= (position[None, :] % steps_all))

    scores = contract("ghid,ghjd->ghij", queries, key_rows) * scale_factor
    scores = jnp.where(causal, scores, -jnp.inf)
    highest = jnp.max(scores, axis=-1, keepdims=True)
    exponent = jnp.exp(scores - highest)
    probs = exponent / jnp.sum(exponent, axis=-1, keepdims=True)
    probs_low = probs.astype(jnp.bfloat16)
    value_grad = contract("ghij,gihd->ghjd", probs_low, up_heads).astype(jnp.bfloat16)
    prob_grad = contract("gihd,ghjd->ghij", up_heads, value_rows)
    score_grad = (
        probs * (prob_grad - jnp.sum(prob_grad * probs, axis=-1, keepdims=True)) * scale_factor
    ).astype(jnp.bfloat16)
    score_grad = lax.optimization_barrier(score_grad)
    query_grad = contract("ghij,ghjd->ghid", score_grad, key_rows).astype(jnp.bfloat16)
    key_grad = contract("ghij,ghid->ghjd", score_grad, queries).astype(jnp.bfloat16)

    def weight_grad(grad_rows):
        return contract("gic,ghid->chd", flat, grad_rows).reshape(width, width)

    def input_grad(grad_rows, name):
        return contract("ghid,chd->gic", grad_rows, heads_of[name])

    back = (
        up_flat.astype(jnp.float32)
        + input_grad(query_grad, "q")
        + input_grad(key_grad, "k")
        + input_grad(value_grad, "v")
    )
    back = jnp.swapaxes(back.astype(jnp.bfloat16).reshape(nodes_here, steps_all, width), 0, 1)
    return ((weight_grad(query_grad), weight_grad(key_grad), weight_grad(value_grad)), back)


def local(
    node_states,
    edge_source,
    edge_target,
    halo_rows,
    halo_count,
    w_message,
    w_query,
    w_key,
    w_value,
    cotangent,
):
    days_local, node_local, width = node_states.shape
    halo_slots = halo_rows.shape[1]
    live = jnp.arange(halo_slots)[None, :] < halo_count
    rows = jnp.arange(node_local, dtype=jnp.int32)
    slot_hot = jnp.logical_and(
        halo_rows[:, :, None] == rows[None, None, :], live[:, :, None]
    ).astype(jnp.bfloat16)
    sent = jnp.einsum(
        "dsn,dnh->dsh", slot_hot, node_states, preferred_element_type=jnp.float32
    ).astype(jnp.bfloat16)
    received = from_behind(sent, "dom", 1)

    target_hot = (edge_target[:, :, None] == rows[None, None, :]).astype(jnp.bfloat16)
    local_hot = (edge_source[:, :, None] == rows[None, None, :]).astype(jnp.bfloat16)
    halo_ids = node_local + jnp.arange(halo_slots, dtype=jnp.int32)
    halo_hot = (edge_source[:, :, None] == halo_ids[None, None, :]).astype(jnp.bfloat16)
    adjacent_local = jnp.einsum(
        "der,des->drs", target_hot, local_hot, preferred_element_type=jnp.float32
    ).astype(jnp.bfloat16)
    adjacent_halo = jnp.einsum(
        "der,des->drs", target_hot, halo_hot, preferred_element_type=jnp.float32
    ).astype(jnp.bfloat16)
    counted = jnp.sum(target_hot.astype(jnp.float32), axis=1)
    inverse = 1.0 / (counted + 1.0)

    states_f = node_states.astype(jnp.float32)
    neighbours = jnp.einsum(
        "drs,dsh->drh", adjacent_local, node_states, preferred_element_type=jnp.float32
    ) + jnp.einsum("drs,dsh->drh", adjacent_halo, received, preferred_element_type=jnp.float32)
    aggregate = ((states_f + neighbours) * inverse[:, :, None]).astype(jnp.bfloat16)
    preact = jnp.einsum("drh,hk->drk", aggregate, w_message, preferred_element_type=jnp.float32)
    hidden = (states_f + jax.nn.silu(preact)).astype(jnp.bfloat16)

    node_major = exchange(hidden, "day", 1, 0)
    upstream = cotangent.reshape(cotangent.shape[0], -1, width)
    attn_grads, back = attend_blocked(node_major, upstream, w_query, w_key, w_value)
    back_days = exchange(back, "day", 0, 1)

    sigmoid_val = jax.nn.sigmoid(preact)
    pre_grad = (
        back_days.astype(jnp.float32) * sigmoid_val * (1.0 + preact * (1.0 - sigmoid_val))
    ).astype(jnp.bfloat16)
    grad_message = lax.dot_general(
        aggregate.reshape(-1, width),
        pre_grad.reshape(-1, width),
        (((0,), (0,)), ((), ())),
        preferred_element_type=jnp.float32,
    )
    agg_grad = jnp.einsum("drk,hk->drh", pre_grad, w_message, preferred_element_type=jnp.float32)
    term_grad = agg_grad * inverse[:, :, None]
    halo_grad = jnp.einsum(
        "drs,drh->dsh",
        adjacent_halo.astype(jnp.float32),
        term_grad,
        precision=lax.Precision.HIGHEST,
        preferred_element_type=jnp.float32,
    ).astype(jnp.bfloat16)
    returned = from_behind(halo_grad, "dom", -1)
    own_grad = jnp.einsum(
        "drs,drh->dsh",
        adjacent_local.astype(jnp.float32),
        term_grad,
        precision=lax.Precision.HIGHEST,
        preferred_element_type=jnp.float32,
    )
    scattered = jnp.einsum("dsn,dsh->dnh", slot_hot, returned, preferred_element_type=jnp.float32)
    state_grad = back_days.astype(jnp.float32) + term_grad + own_grad + scattered
    (grad_message, grad_query, grad_key, grad_value), state_grad = tree_sum(
        (grad_message, attn_grads[0], attn_grads[1], attn_grads[2]), ("dom", "day"), state_grad
    )
    return (state_grad, grad_message, grad_query, grad_key, grad_value)


def solution(mesh):
    return jax.shard_map(
        local,
        mesh=mesh,
        in_specs=(
            P("day", "dom", None),
            P("day", "dom"),
            P("day", "dom"),
            P("day", "dom"),
            P("day", "dom"),
            P(),
            P(),
            P(),
            P(),
            P(None, "dom", "day", None, None),
        ),
        out_specs=(P("day", "dom", None), P(), P(), P(), P()),
        check_vma=False,
    )
```

```python
import jax
import jax.numpy as jnp
from jax import lax
from jax.sharding import PartitionSpec as P

HEADS = 4


def from_behind(value, axis, steps):
    count = lax.axis_size(axis)
    pairs = [(source, (source + steps) % count) for source in range(count)]
    return lax.ppermute(value, axis, pairs)


def _power_of_two(count):
    return count > 0 and count & (count - 1) == 0


def _group_pairs(axis, stride, group, shift):
    pairs = []
    for source in range(lax.axis_size(axis)):
        digit = (source // stride) % group
        pairs.append((source, source + ((digit + shift) % group - digit) * stride))
    return pairs


def _scatter_step(flat, axis, stride, group):
    digit = (lax.axis_index(axis) // stride) % group
    chunks = flat.reshape(group, -1)
    if group == 2:
        keep = jnp.where(digit == 0, chunks[0], chunks[1])
        send = jnp.where(digit == 0, chunks[1], chunks[0])
        return keep + lax.ppermute(send, axis, _group_pairs(axis, stride, group, 1))
    total = lax.dynamic_index_in_dim(chunks, digit, 0, keepdims=False)
    for shift in range(1, group):
        send = lax.dynamic_index_in_dim(chunks, (digit + shift) % group, 0, keepdims=False)
        total = total + lax.ppermute(send, axis, _group_pairs(axis, stride, group, shift))
    return total


def _gather_step(flat, axis, stride, group):
    digit = (lax.axis_index(axis) // stride) % group
    if group == 2:
        other = lax.ppermute(flat, axis, _group_pairs(axis, stride, group, 1))
        return jnp.where(
            digit == 0, jnp.concatenate([flat, other]), jnp.concatenate([other, flat])
        )
    got = [flat] + [
        lax.ppermute(flat, axis, _group_pairs(axis, stride, group, shift)) for shift in range(1, group)
    ]
    stacked = jnp.stack(got)
    order = (digit - jnp.arange(group)) % group
    return jnp.take(stacked, order, axis=0).reshape(-1)


def _factors(size):
    if size <= 4:
        return [size]
    return [2] + _factors(size // 2)


def tree_sum(values, axes, companion=None):
    sizes = [lax.axis_size(axis) for axis in axes]
    flat = jnp.concatenate([value.reshape(-1) for value in values])
    total = 1
    for size in sizes:
        total *= size
    if not all(_power_of_two(size) for size in sizes) or flat.shape[0] % total:
        return lax.psum(tuple(values), axes), companion
    steps = []
    for axis, size in zip(axes, sizes):
        stride = 1
        for group in _factors(size):
            if group > 1:
                steps.append((axis, stride, group))
            stride *= group
    for axis, stride, group in steps:
        flat = _scatter_step(flat, axis, stride, group)
    flat, companion = lax.optimization_barrier((flat, companion))
    for axis, stride, group in reversed(steps):
        flat = _gather_step(flat, axis, stride, group)
    results, start = [], 0
    for value in values:
        results.append(flat[start : start + value.size].reshape(value.shape))
        start += value.size
    return tuple(results), companion


def early_late_sum(early, late_fn, axes, companion_fn):
    sizes = [lax.axis_size(axis) for axis in axes]
    total = 1
    for size in sizes:
        total *= size
    head = jnp.concatenate([value.reshape(-1) for value in early])
    usable = all(_power_of_two(size) for size in sizes) and sizes[0] > 1
    if not usable or head.shape[0] % (2 * total):
        late = late_fn()
        companion = companion_fn()
        results, companion = tree_sum(tuple(late) + tuple(early), axes, companion)
        return results, companion
    head = _scatter_step(head, axes[0], 1, 2)
    late = late_fn()
    tail = jnp.concatenate([value.reshape(-1) for value in late])
    tail = _scatter_step(tail, axes[0], 1, 2)
    companion = companion_fn()
    flat = jnp.concatenate([tail, head])
    steps = []
    for axis, size in zip(axes, sizes):
        stride = 2 if axis == axes[0] else 1
        rest = size // 2 if axis == axes[0] else size
        for group in _factors(rest) if rest > 1 else []:
            if group > 1:
                steps.append((axis, stride, group))
            stride *= group
    for axis, stride, group in steps:
        flat = _scatter_step(flat, axis, stride, group)
    flat, companion = lax.optimization_barrier((flat, companion))
    for axis, stride, group in reversed(steps):
        flat = _gather_step(flat, axis, stride, group)
    whole = _gather_step(flat, axes[0], 1, 2)
    half = flat.shape[0]
    cut = tail.shape[0]
    tail_all = jnp.concatenate([whole[:cut], whole[half : half + cut]])
    head_all = jnp.concatenate([whole[cut:half], whole[half + cut :]])
    results = []
    for values, joined in ((late, tail_all), (early, head_all)):
        start = 0
        for value in values:
            results.append(joined[start : start + value.size].reshape(value.shape))
            start += value.size
    return tuple(results), companion


def exchange(value, axis, split_axis, concat_axis):
    count = lax.axis_size(axis)
    mine = lax.axis_index(axis)
    size = value.shape[split_axis] // count
    got = []
    for shift in range(count):
        send = lax.dynamic_slice_in_dim(value, ((mine + shift) % count) * size, size, axis=split_axis)
        if shift:
            send = lax.ppermute(send, axis, [(i, (i + shift) % count) for i in range(count)])
        got.append(send)
    stacked = jnp.take(jnp.stack(got), (mine - jnp.arange(count)) % count, axis=0)
    return jnp.concatenate([stacked[k] for k in range(count)], axis=concat_axis)


def adjacency(sources, targets, count_rows, total_rows):
    target_hot = (targets[:, None] == jnp.arange(count_rows, dtype=jnp.int32)[None, :]).astype(
        jnp.bfloat16
    )
    source_hot = (sources[:, None] == jnp.arange(total_rows, dtype=jnp.int32)[None, :]).astype(
        jnp.bfloat16
    )
    counts = lax.dot_general(
        target_hot, source_hot, (((0,), (0,)), ((), ())), preferred_element_type=jnp.float32
    )
    return counts.astype(jnp.bfloat16)


def gnn_forward(states, received, adjacent, w_message):
    extended = jnp.concatenate([states, received], axis=0)
    neighbours = jnp.dot(adjacent, extended, preferred_element_type=jnp.float32)
    counted = jnp.sum(adjacent.astype(jnp.float32), axis=1)
    inverse = 1.0 / (counted + 1.0)
    aggregate = ((states.astype(jnp.float32) + neighbours) * inverse[:, None]).astype(jnp.bfloat16)
    preact = jnp.dot(aggregate, w_message, preferred_element_type=jnp.float32)
    hidden = (states.astype(jnp.float32) + jax.nn.silu(preact)).astype(jnp.bfloat16)
    return (aggregate, preact, inverse, hidden)


def gnn_backward(upstream, aggregate, preact, inverse, adjacent, w_message):
    count_rows = aggregate.shape[0]
    up_float = upstream.astype(jnp.float32)
    sigmoid_val = jax.nn.sigmoid(preact)
    pre_grad = (up_float * sigmoid_val * (1.0 + preact * (1.0 - sigmoid_val))).astype(jnp.bfloat16)
    message_part = lax.dot_general(
        aggregate, pre_grad, (((0,), (0,)), ((), ())), preferred_element_type=jnp.float32
    )
    agg_grad = lax.dot_general(
        pre_grad, w_message, (((1,), (1,)), ((), ())), preferred_element_type=jnp.float32
    )
    term_grad = agg_grad * inverse[:, None]
    ext_grad = lax.dot_general(
        adjacent.astype(jnp.float32),
        term_grad,
        (((0,), (0,)), ((), ())),
        precision=lax.Precision.HIGHEST,
        preferred_element_type=jnp.float32,
    )
    local_grad = up_float + term_grad + ext_grad[:count_rows]
    halo_grad = ext_grad[count_rows:].astype(jnp.bfloat16)
    return (message_part, local_grad, halo_grad)


def attend(states, upstream, w_query, w_key, w_value):
    steps_all, nodes_here, width = states.shape
    head_dim = width // HEADS
    scale_factor = head_dim ** (-0.5)
    flat = states.reshape(steps_all * nodes_here, width)

    def project(weight):
        return jnp.dot(flat, weight, preferred_element_type=jnp.float32).astype(jnp.bfloat16)

    def splitter(matrix):
        return matrix.reshape(steps_all, nodes_here, HEADS, head_dim).astype(jnp.float32)

    queries = project(w_query)
    key_rows = project(w_key)
    value_rows = project(w_value)
    query_f = splitter(queries)
    key_f = splitter(key_rows)
    value_f = splitter(value_rows)
    scores = jnp.einsum("tnhd,snhd->nhts", query_f, key_f) * scale_factor
    causal = jnp.arange(steps_all)[:, None] >= jnp.arange(steps_all)[None, :]
    scores = jnp.where(causal, scores, -jnp.inf)
    highest = jnp.max(scores, axis=-1, keepdims=True)
    exponent = jnp.exp(scores - highest)
    probs = exponent / jnp.sum(exponent, axis=-1, keepdims=True)
    probs_low = probs.astype(jnp.bfloat16).astype(jnp.float32)
    up_heads = splitter(upstream)
    value_grad = jnp.einsum("nhts,tnhd->snhd", probs_low, up_heads).astype(jnp.bfloat16)
    prob_grad = jnp.einsum("tnhd,snhd->nhts", up_heads, value_f)
    score_grad = (
        probs * (prob_grad - jnp.sum(prob_grad * probs, axis=-1, keepdims=True)) * scale_factor
    ).astype(jnp.bfloat16)
    score_f = score_grad.astype(jnp.float32)
    query_grad = jnp.einsum("nhts,snhd->tnhd", score_f, key_f).astype(jnp.bfloat16)
    key_grad = jnp.einsum("nhts,tnhd->snhd", score_f, query_f).astype(jnp.bfloat16)
    query_flat = query_grad.reshape(steps_all * nodes_here, width)
    key_flat = key_grad.reshape(steps_all * nodes_here, width)
    value_flat = value_grad.reshape(steps_all * nodes_here, width)

    def weight_grad(grad_rows):
        return lax.dot_general(
            flat, grad_rows, (((0,), (0,)), ((), ())), preferred_element_type=jnp.float32
        )

    def input_grad(grad_rows, weight):
        return lax.dot_general(
            grad_rows, weight, (((1,), (1,)), ((), ())), preferred_element_type=jnp.float32
        )

    back = upstream.reshape(steps_all * nodes_here, width).astype(jnp.float32)
    back = (
        back
        + input_grad(query_flat, w_query)
        + input_grad(key_flat, w_key)
        + input_grad(value_flat, w_value)
    )
    back = back.astype(jnp.bfloat16).reshape(steps_all, nodes_here, width)
    return ((weight_grad(query_flat), weight_grad(key_flat), weight_grad(value_flat)), back)


def attend_blocked(states, upstream, w_query, w_key, w_value):
    steps_all, nodes_here, width = states.shape
    head_dim = width // HEADS
    scale_factor = head_dim ** (-0.5)
    per_group = max(1, 128 // steps_all)
    if nodes_here % per_group:
        per_group = 1
    groups = nodes_here // per_group
    block = per_group * steps_all
    flat = jnp.swapaxes(states, 0, 1).reshape(groups, block, width)
    up_flat = jnp.swapaxes(upstream, 0, 1).reshape(groups, block, width)
    heads_of = {
        name: weight.reshape(width, HEADS, head_dim)
        for name, weight in (("q", w_query), ("k", w_key), ("v", w_value))
    }

    def contract(spec, left, right):
        return jnp.einsum(spec, left, right, preferred_element_type=jnp.float32)

    queries = contract("gic,chd->ghid", flat, heads_of["q"]).astype(jnp.bfloat16)
    key_rows = contract("gic,chd->ghid", flat, heads_of["k"]).astype(jnp.bfloat16)
    value_rows = contract("gic,chd->ghid", flat, heads_of["v"]).astype(jnp.bfloat16)
    up_heads = up_flat.reshape(groups, block, HEADS, head_dim)
    position = jnp.arange(block)
    same = (position[:, None] // steps_all) == (position[None, :] // steps_all)
    causal = jnp.logical_and(same, (position[:, None] % steps_all) >= (position[None, :] % steps_all))

    scores = contract("ghid,ghjd->ghij", queries, key_rows) * scale_factor
    scores = jnp.where(causal, scores, -jnp.inf)
    highest = jnp.max(scores, axis=-1, keepdims=True)
    exponent = jnp.exp(scores - highest)
    probs = exponent / jnp.sum(exponent, axis=-1, keepdims=True)
    probs_low = probs.astype(jnp.bfloat16)
    value_grad = contract("ghij,gihd->ghjd", probs_low, up_heads).astype(jnp.bfloat16)
    prob_grad = contract("gihd,ghjd->ghij", up_heads, value_rows)
    score_grad = (
        probs * (prob_grad - jnp.sum(prob_grad * probs, axis=-1, keepdims=True)) * scale_factor
    ).astype(jnp.bfloat16)
    score_grad = lax.optimization_barrier(score_grad)
    query_grad = contract("ghij,ghjd->ghid", score_grad, key_rows).astype(jnp.bfloat16)
    key_grad = contract("ghij,ghid->ghjd", score_grad, queries).astype(jnp.bfloat16)

    def weight_grad(grad_rows):
        return contract("gic,ghid->chd", flat, grad_rows).reshape(width, width)

    def input_grad(grad_rows, name):
        return contract("ghid,chd->gic", grad_rows, heads_of[name])

    back = (
        up_flat.astype(jnp.float32)
        + input_grad(query_grad, "q")
        + input_grad(key_grad, "k")
        + input_grad(value_grad, "v")
    )
    back = jnp.swapaxes(back.astype(jnp.bfloat16).reshape(nodes_here, steps_all, width), 0, 1)
    return ((weight_grad(query_grad), weight_grad(key_grad), weight_grad(value_grad)), back)


def local(
    node_states,
    edge_source,
    edge_target,
    halo_rows,
    halo_count,
    w_message,
    w_query,
    w_key,
    w_value,
    cotangent,
):
    days_local, node_local, width = node_states.shape
    halo_slots = halo_rows.shape[1]
    live = jnp.arange(halo_slots)[None, :] < halo_count
    rows = jnp.arange(node_local, dtype=jnp.int32)
    slot_hot = jnp.logical_and(
        halo_rows[:, :, None] == rows[None, None, :], live[:, :, None]
    ).astype(jnp.bfloat16)
    sent = jnp.einsum(
        "dsn,dnh->dsh", slot_hot, node_states, preferred_element_type=jnp.float32
    ).astype(jnp.bfloat16)
    received = from_behind(sent, "dom", 1)

    target_hot = (edge_target[:, :, None] == rows[None, None, :]).astype(jnp.bfloat16)
    local_hot = (edge_source[:, :, None] == rows[None, None, :]).astype(jnp.bfloat16)
    halo_ids = node_local + jnp.arange(halo_slots, dtype=jnp.int32)
    halo_hot = (edge_source[:, :, None] == halo_ids[None, None, :]).astype(jnp.bfloat16)
    adjacent_local = jnp.einsum(
        "der,des->drs", target_hot, local_hot, preferred_element_type=jnp.float32
    ).astype(jnp.bfloat16)
    adjacent_halo = jnp.einsum(
        "der,des->drs", target_hot, halo_hot, preferred_element_type=jnp.float32
    ).astype(jnp.bfloat16)
    counted = jnp.sum(target_hot.astype(jnp.float32), axis=1)
    inverse = 1.0 / (counted + 1.0)

    states_f = node_states.astype(jnp.float32)
    neighbours = jnp.einsum(
        "drs,dsh->drh", adjacent_local, node_states, preferred_element_type=jnp.float32
    ) + jnp.einsum("drs,dsh->drh", adjacent_halo, received, preferred_element_type=jnp.float32)
    aggregate = ((states_f + neighbours) * inverse[:, :, None]).astype(jnp.bfloat16)
    preact = jnp.einsum("drh,hk->drk", aggregate, w_message, preferred_element_type=jnp.float32)
    hidden = (states_f + jax.nn.silu(preact)).astype(jnp.bfloat16)

    node_major = exchange(hidden, "day", 1, 0)
    upstream = cotangent.reshape(cotangent.shape[0], -1, width)
    attn_grads, back = attend_blocked(node_major, upstream, w_query, w_key, w_value)
    back_days = exchange(back, "day", 0, 1)

    sigmoid_val = jax.nn.sigmoid(preact)
    pre_grad = (
        back_days.astype(jnp.float32) * sigmoid_val * (1.0 + preact * (1.0 - sigmoid_val))
    ).astype(jnp.bfloat16)

    def message_grad():
        return (
            lax.dot_general(
                aggregate.reshape(-1, width),
                pre_grad.reshape(-1, width),
                (((0,), (0,)), ((), ())),
                preferred_element_type=jnp.float32,
            ),
        )

    def state_part():
        agg_grad = jnp.einsum(
            "drk,hk->drh", pre_grad, w_message, preferred_element_type=jnp.float32
        )
        term_grad = agg_grad * inverse[:, :, None]
        halo_grad = jnp.einsum(
            "drs,drh->dsh",
            adjacent_halo.astype(jnp.float32),
            term_grad,
            precision=lax.Precision.HIGHEST,
            preferred_element_type=jnp.float32,
        ).astype(jnp.bfloat16)
        returned = from_behind(halo_grad, "dom", -1)
        own_grad = jnp.einsum(
            "drs,drh->dsh",
            adjacent_local.astype(jnp.float32),
            term_grad,
            precision=lax.Precision.HIGHEST,
            preferred_element_type=jnp.float32,
        )
        scattered = jnp.einsum(
            "dsn,dsh->dnh", slot_hot, returned, preferred_element_type=jnp.float32
        )
        return back_days.astype(jnp.float32) + term_grad + own_grad + scattered

    (grad_message, grad_query, grad_key, grad_value), state_grad = early_late_sum(
        attn_grads, message_grad, ("dom", "day"), state_part
    )
    return (state_grad, grad_message, grad_query, grad_key, grad_value)


def solution(mesh):
    return jax.shard_map(
        local,
        mesh=mesh,
        in_specs=(
            P("day", "dom", None),
            P("day", "dom"),
            P("day", "dom"),
            P("day", "dom"),
            P("day", "dom"),
            P(),
            P(),
            P(),
            P(),
            P(None, "dom", "day", None, None),
        ),
        out_specs=(P("day", "dom", None), P(), P(), P(), P()),
        check_vma=False,
    )
```

```python
import jax
import jax.numpy as jnp
from jax import lax
from jax.sharding import PartitionSpec as P

HEADS = 4


def from_behind(value, axis, steps):
    count = lax.axis_size(axis)
    pairs = [(source, (source + steps) % count) for source in range(count)]
    return lax.ppermute(value, axis, pairs)


def _power_of_two(count):
    return count > 0 and count & (count - 1) == 0


def _group_pairs(axis, stride, group, shift):
    pairs = []
    for source in range(lax.axis_size(axis)):
        digit = (source // stride) % group
        pairs.append((source, source + ((digit + shift) % group - digit) * stride))
    return pairs


def _scatter_step(flat, axis, stride, group):
    digit = (lax.axis_index(axis) // stride) % group
    chunks = flat.reshape(group, -1)
    if group == 2:
        keep = jnp.where(digit == 0, chunks[0], chunks[1])
        send = jnp.where(digit == 0, chunks[1], chunks[0])
        return keep + lax.ppermute(send, axis, _group_pairs(axis, stride, group, 1))
    total = lax.dynamic_index_in_dim(chunks, digit, 0, keepdims=False)
    for shift in range(1, group):
        send = lax.dynamic_index_in_dim(chunks, (digit + shift) % group, 0, keepdims=False)
        total = total + lax.ppermute(send, axis, _group_pairs(axis, stride, group, shift))
    return total


def _gather_step(flat, axis, stride, group):
    digit = (lax.axis_index(axis) // stride) % group
    if group == 2:
        other = lax.ppermute(flat, axis, _group_pairs(axis, stride, group, 1))
        return jnp.where(
            digit == 0, jnp.concatenate([flat, other]), jnp.concatenate([other, flat])
        )
    got = [flat] + [
        lax.ppermute(flat, axis, _group_pairs(axis, stride, group, shift)) for shift in range(1, group)
    ]
    stacked = jnp.stack(got)
    order = (digit - jnp.arange(group)) % group
    return jnp.take(stacked, order, axis=0).reshape(-1)


def _factors(size):
    if size <= 4:
        return [size]
    return [2] + _factors(size // 2)


def tree_sum(values, axes, companion=None):
    sizes = [lax.axis_size(axis) for axis in axes]
    flat = jnp.concatenate([value.reshape(-1) for value in values])
    total = 1
    for size in sizes:
        total *= size
    if not all(_power_of_two(size) for size in sizes) or flat.shape[0] % total:
        return lax.psum(tuple(values), axes), companion
    steps = []
    for axis, size in zip(axes, sizes):
        stride = 1
        for group in _factors(size):
            if group > 1:
                steps.append((axis, stride, group))
            stride *= group
    for axis, stride, group in steps:
        flat = _scatter_step(flat, axis, stride, group)
    flat, companion = lax.optimization_barrier((flat, companion))
    for axis, stride, group in reversed(steps):
        flat = _gather_step(flat, axis, stride, group)
    results, start = [], 0
    for value in values:
        results.append(flat[start : start + value.size].reshape(value.shape))
        start += value.size
    return tuple(results), companion


def exchange(value, axis, split_axis, concat_axis):
    count = lax.axis_size(axis)
    mine = lax.axis_index(axis)
    size = value.shape[split_axis] // count
    got = []
    for shift in range(count):
        send = lax.dynamic_slice_in_dim(value, ((mine + shift) % count) * size, size, axis=split_axis)
        if shift:
            send = lax.ppermute(send, axis, [(i, (i + shift) % count) for i in range(count)])
        got.append(send)
    stacked = jnp.take(jnp.stack(got), (mine - jnp.arange(count)) % count, axis=0)
    return jnp.concatenate([stacked[k] for k in range(count)], axis=concat_axis)


def adjacency(sources, targets, count_rows, total_rows):
    target_hot = (targets[:, None] == jnp.arange(count_rows, dtype=jnp.int32)[None, :]).astype(
        jnp.bfloat16
    )
    source_hot = (sources[:, None] == jnp.arange(total_rows, dtype=jnp.int32)[None, :]).astype(
        jnp.bfloat16
    )
    counts = lax.dot_general(
        target_hot, source_hot, (((0,), (0,)), ((), ())), preferred_element_type=jnp.float32
    )
    return counts.astype(jnp.bfloat16)


def gnn_forward(states, received, adjacent, w_message):
    extended = jnp.concatenate([states, received], axis=0)
    neighbours = jnp.dot(adjacent, extended, preferred_element_type=jnp.float32)
    counted = jnp.sum(adjacent.astype(jnp.float32), axis=1)
    inverse = 1.0 / (counted + 1.0)
    aggregate = ((states.astype(jnp.float32) + neighbours) * inverse[:, None]).astype(jnp.bfloat16)
    preact = jnp.dot(aggregate, w_message, preferred_element_type=jnp.float32)
    hidden = (states.astype(jnp.float32) + jax.nn.silu(preact)).astype(jnp.bfloat16)
    return (aggregate, preact, inverse, hidden)


def gnn_backward(upstream, aggregate, preact, inverse, adjacent, w_message):
    count_rows = aggregate.shape[0]
    up_float = upstream.astype(jnp.float32)
    sigmoid_val = jax.nn.sigmoid(preact)
    pre_grad = (up_float * sigmoid_val * (1.0 + preact * (1.0 - sigmoid_val))).astype(jnp.bfloat16)
    message_part = lax.dot_general(
        aggregate, pre_grad, (((0,), (0,)), ((), ())), preferred_element_type=jnp.float32
    )
    agg_grad = lax.dot_general(
        pre_grad, w_message, (((1,), (1,)), ((), ())), preferred_element_type=jnp.float32
    )
    term_grad = agg_grad * inverse[:, None]
    ext_grad = lax.dot_general(
        adjacent.astype(jnp.float32),
        term_grad,
        (((0,), (0,)), ((), ())),
        precision=lax.Precision.HIGHEST,
        preferred_element_type=jnp.float32,
    )
    local_grad = up_float + term_grad + ext_grad[:count_rows]
    halo_grad = ext_grad[count_rows:].astype(jnp.bfloat16)
    return (message_part, local_grad, halo_grad)


def attend(states, upstream, w_query, w_key, w_value):
    steps_all, nodes_here, width = states.shape
    head_dim = width // HEADS
    scale_factor = head_dim ** (-0.5)
    flat = states.reshape(steps_all * nodes_here, width)

    def project(weight):
        return jnp.dot(flat, weight, preferred_element_type=jnp.float32).astype(jnp.bfloat16)

    def splitter(matrix):
        return matrix.reshape(steps_all, nodes_here, HEADS, head_dim).astype(jnp.float32)

    queries = project(w_query)
    key_rows = project(w_key)
    value_rows = project(w_value)
    query_f = splitter(queries)
    key_f = splitter(key_rows)
    value_f = splitter(value_rows)
    scores = jnp.einsum("tnhd,snhd->nhts", query_f, key_f) * scale_factor
    causal = jnp.arange(steps_all)[:, None] >= jnp.arange(steps_all)[None, :]
    scores = jnp.where(causal, scores, -jnp.inf)
    highest = jnp.max(scores, axis=-1, keepdims=True)
    exponent = jnp.exp(scores - highest)
    probs = exponent / jnp.sum(exponent, axis=-1, keepdims=True)
    probs_low = probs.astype(jnp.bfloat16).astype(jnp.float32)
    up_heads = splitter(upstream)
    value_grad = jnp.einsum("nhts,tnhd->snhd", probs_low, up_heads).astype(jnp.bfloat16)
    prob_grad = jnp.einsum("tnhd,snhd->nhts", up_heads, value_f)
    score_grad = (
        probs * (prob_grad - jnp.sum(prob_grad * probs, axis=-1, keepdims=True)) * scale_factor
    ).astype(jnp.bfloat16)
    score_f = score_grad.astype(jnp.float32)
    query_grad = jnp.einsum("nhts,snhd->tnhd", score_f, key_f).astype(jnp.bfloat16)
    key_grad = jnp.einsum("nhts,tnhd->snhd", score_f, query_f).astype(jnp.bfloat16)
    query_flat = query_grad.reshape(steps_all * nodes_here, width)
    key_flat = key_grad.reshape(steps_all * nodes_here, width)
    value_flat = value_grad.reshape(steps_all * nodes_here, width)

    def weight_grad(grad_rows):
        return lax.dot_general(
            flat, grad_rows, (((0,), (0,)), ((), ())), preferred_element_type=jnp.float32
        )

    def input_grad(grad_rows, weight):
        return lax.dot_general(
            grad_rows, weight, (((1,), (1,)), ((), ())), preferred_element_type=jnp.float32
        )

    back = upstream.reshape(steps_all * nodes_here, width).astype(jnp.float32)
    back = (
        back
        + input_grad(query_flat, w_query)
        + input_grad(key_flat, w_key)
        + input_grad(value_flat, w_value)
    )
    back = back.astype(jnp.bfloat16).reshape(steps_all, nodes_here, width)
    return ((weight_grad(query_flat), weight_grad(key_flat), weight_grad(value_flat)), back)


def attend_blocked(states, upstream, w_query, w_key, w_value):
    steps_all, nodes_here, width = states.shape
    head_dim = width // HEADS
    scale_factor = head_dim ** (-0.5)
    per_group = max(1, 128 // steps_all)
    if nodes_here % per_group:
        per_group = 1
    groups = nodes_here // per_group
    block = per_group * steps_all
    flat = jnp.swapaxes(states, 0, 1).reshape(groups, block, width)
    up_flat = jnp.swapaxes(upstream, 0, 1).reshape(groups, block, width)
    heads_of = {
        name: weight.reshape(width, HEADS, head_dim)
        for name, weight in (("q", w_query), ("k", w_key), ("v", w_value))
    }

    def contract(spec, left, right):
        return jnp.einsum(spec, left, right, preferred_element_type=jnp.float32)

    queries = contract("gic,chd->ghid", flat, heads_of["q"]).astype(jnp.bfloat16)
    key_rows = contract("gic,chd->ghid", flat, heads_of["k"]).astype(jnp.bfloat16)
    value_rows = contract("gic,chd->ghid", flat, heads_of["v"]).astype(jnp.bfloat16)
    up_heads = up_flat.reshape(groups, block, HEADS, head_dim)
    position = jnp.arange(block)
    same = (position[:, None] // steps_all) == (position[None, :] // steps_all)
    causal = jnp.logical_and(same, (position[:, None] % steps_all) >= (position[None, :] % steps_all))

    scores = contract("ghid,ghjd->ghij", queries, key_rows) * scale_factor
    scores = jnp.where(causal, scores, -jnp.inf)
    highest = jnp.max(scores, axis=-1, keepdims=True)
    exponent = jnp.exp(scores - highest)
    probs = exponent / jnp.sum(exponent, axis=-1, keepdims=True)
    probs_low = probs.astype(jnp.bfloat16)
    value_grad = contract("ghij,gihd->ghjd", probs_low, up_heads).astype(jnp.bfloat16)
    prob_grad = contract("gihd,ghjd->ghij", up_heads, value_rows)
    score_grad = (
        probs * (prob_grad - jnp.sum(prob_grad * probs, axis=-1, keepdims=True)) * scale_factor
    ).astype(jnp.bfloat16)
    score_grad = lax.optimization_barrier(score_grad)
    query_grad = contract("ghij,ghjd->ghid", score_grad, key_rows).astype(jnp.bfloat16)
    key_grad = contract("ghij,ghid->ghjd", score_grad, queries).astype(jnp.bfloat16)

    def weight_grad(grad_rows):
        return contract("gic,ghid->chd", flat, grad_rows).reshape(width, width)

    def input_grad(grad_rows, name):
        return contract("ghid,chd->gic", grad_rows, heads_of[name])

    back = (
        up_flat.astype(jnp.float32)
        + input_grad(query_grad, "q")
        + input_grad(key_grad, "k")
        + input_grad(value_grad, "v")
    )
    back = jnp.swapaxes(back.astype(jnp.bfloat16).reshape(nodes_here, steps_all, width), 0, 1)
    return ((weight_grad(query_grad), weight_grad(key_grad), weight_grad(value_grad)), back)


def local(
    node_states,
    edge_source,
    edge_target,
    halo_rows,
    halo_count,
    w_message,
    w_query,
    w_key,
    w_value,
    cotangent,
):
    days_local, node_local, width = node_states.shape
    halo_slots = halo_rows.shape[1]
    live = jnp.arange(halo_slots)[None, :] < halo_count
    rows = jnp.arange(node_local, dtype=jnp.int32)
    slot_hot = jnp.logical_and(
        halo_rows[:, :, None] == rows[None, None, :], live[:, :, None]
    ).astype(jnp.bfloat16)
    sent = jnp.einsum(
        "dsn,dnh->dsh", slot_hot, node_states, preferred_element_type=jnp.float32
    ).astype(jnp.bfloat16)
    received = from_behind(sent, "dom", 1)

    target_hot = (edge_target[:, :, None] == rows[None, None, :]).astype(jnp.bfloat16)
    extended_ids = jnp.arange(node_local + halo_slots, dtype=jnp.int32)
    source_hot = (edge_source[:, :, None] == extended_ids[None, None, :]).astype(jnp.bfloat16)
    adjacent = jnp.einsum(
        "der,des->drs", target_hot, source_hot, preferred_element_type=jnp.float32
    ).astype(jnp.bfloat16)
    counted = jnp.einsum(
        "der,e->dr",
        target_hot,
        jnp.ones(target_hot.shape[1], jnp.bfloat16),
        preferred_element_type=jnp.float32,
    )
    inverse = 1.0 / (counted + 1.0)

    states_f = node_states.astype(jnp.float32)
    extended = jnp.concatenate([node_states, received], axis=1)
    neighbours = jnp.einsum("drs,dsh->drh", adjacent, extended, preferred_element_type=jnp.float32)
    aggregate = ((states_f + neighbours) * inverse[:, :, None]).astype(jnp.bfloat16)
    preact = jnp.einsum("drh,hk->drk", aggregate, w_message, preferred_element_type=jnp.float32)
    hidden = (states_f + jax.nn.silu(preact)).astype(jnp.bfloat16)

    node_major = exchange(hidden, "day", 1, 0)
    upstream = cotangent.reshape(cotangent.shape[0], -1, width)
    attn_grads, back = attend_blocked(node_major, upstream, w_query, w_key, w_value)
    back_days = exchange(back, "day", 0, 1)

    sigmoid_val = jax.nn.sigmoid(preact)
    pre_grad = (
        back_days.astype(jnp.float32) * sigmoid_val * (1.0 + preact * (1.0 - sigmoid_val))
    ).astype(jnp.bfloat16)
    grad_message = lax.dot_general(
        aggregate.reshape(-1, width),
        pre_grad.reshape(-1, width),
        (((0,), (0,)), ((), ())),
        preferred_element_type=jnp.float32,
    )
    agg_grad = jnp.einsum("drk,hk->drh", pre_grad, w_message, preferred_element_type=jnp.float32)
    term_grad = agg_grad * inverse[:, :, None]
    ext_grad = jnp.einsum(
        "drs,drh->dsh",
        adjacent.astype(jnp.float32),
        term_grad,
        precision=lax.Precision.HIGHEST,
        preferred_element_type=jnp.float32,
    )
    halo_grad = ext_grad[:, node_local:].astype(jnp.bfloat16)
    returned = from_behind(halo_grad, "dom", -1)
    own_grad = ext_grad[:, :node_local]
    scattered = jnp.einsum("dsn,dsh->dnh", slot_hot, returned, preferred_element_type=jnp.float32)
    state_grad = back_days.astype(jnp.float32) + term_grad + own_grad + scattered
    (grad_message, grad_query, grad_key, grad_value), state_grad = tree_sum(
        (grad_message, attn_grads[0], attn_grads[1], attn_grads[2]), ("dom", "day"), state_grad
    )
    return (state_grad, grad_message, grad_query, grad_key, grad_value)


def solution(mesh):
    return jax.shard_map(
        local,
        mesh=mesh,
        in_specs=(
            P("day", "dom", None),
            P("day", "dom"),
            P("day", "dom"),
            P("day", "dom"),
            P("day", "dom"),
            P(),
            P(),
            P(),
            P(),
            P(None, "dom", "day", None, None),
        ),
        out_specs=(P("day", "dom", None), P(), P(), P(), P()),
        check_vma=False,
    )
```

```python
import jax
import jax.numpy as jnp
from jax import lax
from jax.sharding import PartitionSpec as P

HEADS = 4


def from_behind(value, axis, steps):
    count = lax.axis_size(axis)
    pairs = [(source, (source + steps) % count) for source in range(count)]
    return lax.ppermute(value, axis, pairs)


def _power_of_two(count):
    return count > 0 and count & (count - 1) == 0


def _group_pairs(axis, stride, group, shift):
    pairs = []
    for source in range(lax.axis_size(axis)):
        digit = (source // stride) % group
        pairs.append((source, source + ((digit + shift) % group - digit) * stride))
    return pairs


def _scatter_step(flat, axis, stride, group):
    digit = (lax.axis_index(axis) // stride) % group
    chunks = flat.reshape(group, -1)
    if group == 2:
        keep = jnp.where(digit == 0, chunks[0], chunks[1])
        send = jnp.where(digit == 0, chunks[1], chunks[0])
        return keep + lax.ppermute(send, axis, _group_pairs(axis, stride, group, 1))
    total = lax.dynamic_index_in_dim(chunks, digit, 0, keepdims=False)
    for shift in range(1, group):
        send = lax.dynamic_index_in_dim(chunks, (digit + shift) % group, 0, keepdims=False)
        total = total + lax.ppermute(send, axis, _group_pairs(axis, stride, group, shift))
    return total


def _gather_step(flat, axis, stride, group):
    digit = (lax.axis_index(axis) // stride) % group
    if group == 2:
        other = lax.ppermute(flat, axis, _group_pairs(axis, stride, group, 1))
        return jnp.where(
            digit == 0, jnp.concatenate([flat, other]), jnp.concatenate([other, flat])
        )
    got = [flat] + [
        lax.ppermute(flat, axis, _group_pairs(axis, stride, group, shift)) for shift in range(1, group)
    ]
    stacked = jnp.stack(got)
    order = (digit - jnp.arange(group)) % group
    return jnp.take(stacked, order, axis=0).reshape(-1)


def _factors(size):
    if size <= 4:
        return [size]
    return [2] + _factors(size // 2)


def tree_sum(values, axes, companion=None):
    sizes = [lax.axis_size(axis) for axis in axes]
    flat = jnp.concatenate([value.reshape(-1) for value in values])
    total = 1
    for size in sizes:
        total *= size
    if not all(_power_of_two(size) for size in sizes) or flat.shape[0] % total:
        return lax.psum(tuple(values), axes), companion
    per_axis = []
    for axis, size in zip(axes, sizes):
        stride, own = 1, []
        for group in _factors(size):
            if group > 1:
                own.append((axis, stride, group))
            stride *= group
        per_axis.append(own)
    steps = per_axis[0][:1] + [step for own in per_axis[1:] for step in own] + per_axis[0][1:]
    for axis, stride, group in steps:
        flat = _scatter_step(flat, axis, stride, group)
    flat, companion = lax.optimization_barrier((flat, companion))
    for axis, stride, group in reversed(steps):
        flat = _gather_step(flat, axis, stride, group)
    results, start = [], 0
    for value in values:
        results.append(flat[start : start + value.size].reshape(value.shape))
        start += value.size
    return tuple(results), companion


def exchange(value, axis, split_axis, concat_axis):
    count = lax.axis_size(axis)
    mine = lax.axis_index(axis)
    size = value.shape[split_axis] // count
    got = []
    for shift in range(count):
        send = lax.dynamic_slice_in_dim(value, ((mine + shift) % count) * size, size, axis=split_axis)
        if shift:
            send = lax.ppermute(send, axis, [(i, (i + shift) % count) for i in range(count)])
        got.append(send)
    stacked = jnp.take(jnp.stack(got), (mine - jnp.arange(count)) % count, axis=0)
    return jnp.concatenate([stacked[k] for k in range(count)], axis=concat_axis)


def adjacency(sources, targets, count_rows, total_rows):
    target_hot = (targets[:, None] == jnp.arange(count_rows, dtype=jnp.int32)[None, :]).astype(
        jnp.bfloat16
    )
    source_hot = (sources[:, None] == jnp.arange(total_rows, dtype=jnp.int32)[None, :]).astype(
        jnp.bfloat16
    )
    counts = lax.dot_general(
        target_hot, source_hot, (((0,), (0,)), ((), ())), preferred_element_type=jnp.float32
    )
    return counts.astype(jnp.bfloat16)


def gnn_forward(states, received, adjacent, w_message):
    extended = jnp.concatenate([states, received], axis=0)
    neighbours = jnp.dot(adjacent, extended, preferred_element_type=jnp.float32)
    counted = jnp.sum(adjacent.astype(jnp.float32), axis=1)
    inverse = 1.0 / (counted + 1.0)
    aggregate = ((states.astype(jnp.float32) + neighbours) * inverse[:, None]).astype(jnp.bfloat16)
    preact = jnp.dot(aggregate, w_message, preferred_element_type=jnp.float32)
    hidden = (states.astype(jnp.float32) + jax.nn.silu(preact)).astype(jnp.bfloat16)
    return (aggregate, preact, inverse, hidden)


def gnn_backward(upstream, aggregate, preact, inverse, adjacent, w_message):
    count_rows = aggregate.shape[0]
    up_float = upstream.astype(jnp.float32)
    sigmoid_val = jax.nn.sigmoid(preact)
    pre_grad = (up_float * sigmoid_val * (1.0 + preact * (1.0 - sigmoid_val))).astype(jnp.bfloat16)
    message_part = lax.dot_general(
        aggregate, pre_grad, (((0,), (0,)), ((), ())), preferred_element_type=jnp.float32
    )
    agg_grad = lax.dot_general(
        pre_grad, w_message, (((1,), (1,)), ((), ())), preferred_element_type=jnp.float32
    )
    term_grad = agg_grad * inverse[:, None]
    ext_grad = lax.dot_general(
        adjacent.astype(jnp.float32),
        term_grad,
        (((0,), (0,)), ((), ())),
        precision=lax.Precision.HIGHEST,
        preferred_element_type=jnp.float32,
    )
    local_grad = up_float + term_grad + ext_grad[:count_rows]
    halo_grad = ext_grad[count_rows:].astype(jnp.bfloat16)
    return (message_part, local_grad, halo_grad)


def attend(states, upstream, w_query, w_key, w_value):
    steps_all, nodes_here, width = states.shape
    head_dim = width // HEADS
    scale_factor = head_dim ** (-0.5)
    flat = states.reshape(steps_all * nodes_here, width)

    def project(weight):
        return jnp.dot(flat, weight, preferred_element_type=jnp.float32).astype(jnp.bfloat16)

    def splitter(matrix):
        return matrix.reshape(steps_all, nodes_here, HEADS, head_dim).astype(jnp.float32)

    queries = project(w_query)
    key_rows = project(w_key)
    value_rows = project(w_value)
    query_f = splitter(queries)
    key_f = splitter(key_rows)
    value_f = splitter(value_rows)
    scores = jnp.einsum("tnhd,snhd->nhts", query_f, key_f) * scale_factor
    causal = jnp.arange(steps_all)[:, None] >= jnp.arange(steps_all)[None, :]
    scores = jnp.where(causal, scores, -jnp.inf)
    highest = jnp.max(scores, axis=-1, keepdims=True)
    exponent = jnp.exp(scores - highest)
    probs = exponent / jnp.sum(exponent, axis=-1, keepdims=True)
    probs_low = probs.astype(jnp.bfloat16).astype(jnp.float32)
    up_heads = splitter(upstream)
    value_grad = jnp.einsum("nhts,tnhd->snhd", probs_low, up_heads).astype(jnp.bfloat16)
    prob_grad = jnp.einsum("tnhd,snhd->nhts", up_heads, value_f)
    score_grad = (
        probs * (prob_grad - jnp.sum(prob_grad * probs, axis=-1, keepdims=True)) * scale_factor
    ).astype(jnp.bfloat16)
    score_f = score_grad.astype(jnp.float32)
    query_grad = jnp.einsum("nhts,snhd->tnhd", score_f, key_f).astype(jnp.bfloat16)
    key_grad = jnp.einsum("nhts,tnhd->snhd", score_f, query_f).astype(jnp.bfloat16)
    query_flat = query_grad.reshape(steps_all * nodes_here, width)
    key_flat = key_grad.reshape(steps_all * nodes_here, width)
    value_flat = value_grad.reshape(steps_all * nodes_here, width)

    def weight_grad(grad_rows):
        return lax.dot_general(
            flat, grad_rows, (((0,), (0,)), ((), ())), preferred_element_type=jnp.float32
        )

    def input_grad(grad_rows, weight):
        return lax.dot_general(
            grad_rows, weight, (((1,), (1,)), ((), ())), preferred_element_type=jnp.float32
        )

    back = upstream.reshape(steps_all * nodes_here, width).astype(jnp.float32)
    back = (
        back
        + input_grad(query_flat, w_query)
        + input_grad(key_flat, w_key)
        + input_grad(value_flat, w_value)
    )
    back = back.astype(jnp.bfloat16).reshape(steps_all, nodes_here, width)
    return ((weight_grad(query_flat), weight_grad(key_flat), weight_grad(value_flat)), back)


def attend_blocked(states, upstream, w_query, w_key, w_value):
    steps_all, nodes_here, width = states.shape
    head_dim = width // HEADS
    scale_factor = head_dim ** (-0.5)
    per_group = max(1, 128 // steps_all)
    if nodes_here % per_group:
        per_group = 1
    groups = nodes_here // per_group
    block = per_group * steps_all
    flat = jnp.swapaxes(states, 0, 1).reshape(groups, block, width)
    up_flat = jnp.swapaxes(upstream, 0, 1).reshape(groups, block, width)
    heads_of = {
        name: weight.reshape(width, HEADS, head_dim)
        for name, weight in (("q", w_query), ("k", w_key), ("v", w_value))
    }

    def contract(spec, left, right):
        return jnp.einsum(spec, left, right, preferred_element_type=jnp.float32)

    queries = contract("gic,chd->ghid", flat, heads_of["q"]).astype(jnp.bfloat16)
    key_rows = contract("gic,chd->ghid", flat, heads_of["k"]).astype(jnp.bfloat16)
    value_rows = contract("gic,chd->ghid", flat, heads_of["v"]).astype(jnp.bfloat16)
    up_heads = up_flat.reshape(groups, block, HEADS, head_dim)
    position = jnp.arange(block)
    same = (position[:, None] // steps_all) == (position[None, :] // steps_all)
    causal = jnp.logical_and(same, (position[:, None] % steps_all) >= (position[None, :] % steps_all))

    scores = contract("ghid,ghjd->ghij", queries, key_rows) * scale_factor
    scores = jnp.where(causal, scores, -jnp.inf)
    highest = jnp.max(scores, axis=-1, keepdims=True)
    exponent = jnp.exp(scores - highest)
    probs = exponent / jnp.sum(exponent, axis=-1, keepdims=True)
    probs_low = probs.astype(jnp.bfloat16)
    value_grad = contract("ghij,gihd->ghjd", probs_low, up_heads).astype(jnp.bfloat16)
    prob_grad = contract("gihd,ghjd->ghij", up_heads, value_rows)
    score_grad = (
        probs * (prob_grad - jnp.sum(prob_grad * probs, axis=-1, keepdims=True)) * scale_factor
    ).astype(jnp.bfloat16)
    score_grad = lax.optimization_barrier(score_grad)
    query_grad = contract("ghij,ghjd->ghid", score_grad, key_rows).astype(jnp.bfloat16)
    key_grad = contract("ghij,ghid->ghjd", score_grad, queries).astype(jnp.bfloat16)

    def weight_grad(grad_rows):
        return contract("gic,ghid->chd", flat, grad_rows).reshape(width, width)

    def input_grad(grad_rows, name):
        return contract("ghid,chd->gic", grad_rows, heads_of[name])

    back = (
        up_flat.astype(jnp.float32)
        + input_grad(query_grad, "q")
        + input_grad(key_grad, "k")
        + input_grad(value_grad, "v")
    )
    back = jnp.swapaxes(back.astype(jnp.bfloat16).reshape(nodes_here, steps_all, width), 0, 1)
    return ((weight_grad(query_grad), weight_grad(key_grad), weight_grad(value_grad)), back)


def local(
    node_states,
    edge_source,
    edge_target,
    halo_rows,
    halo_count,
    w_message,
    w_query,
    w_key,
    w_value,
    cotangent,
):
    days_local, node_local, width = node_states.shape
    halo_slots = halo_rows.shape[1]
    live = jnp.arange(halo_slots)[None, :] < halo_count
    rows = jnp.arange(node_local, dtype=jnp.int32)
    slot_hot = jnp.logical_and(
        halo_rows[:, :, None] == rows[None, None, :], live[:, :, None]
    ).astype(jnp.bfloat16)
    sent = jnp.einsum(
        "dsn,dnh->dsh", slot_hot, node_states, preferred_element_type=jnp.float32
    ).astype(jnp.bfloat16)
    received = from_behind(sent, "dom", 1)

    target_hot = (edge_target[:, :, None] == rows[None, None, :]).astype(jnp.bfloat16)
    extended_ids = jnp.arange(node_local + halo_slots, dtype=jnp.int32)
    source_hot = (edge_source[:, :, None] == extended_ids[None, None, :]).astype(jnp.bfloat16)
    adjacent = jnp.einsum(
        "der,des->drs", target_hot, source_hot, preferred_element_type=jnp.float32
    ).astype(jnp.bfloat16)
    counted = jnp.einsum(
        "der,e->dr",
        target_hot,
        jnp.ones(target_hot.shape[1], jnp.bfloat16),
        preferred_element_type=jnp.float32,
    )
    inverse = 1.0 / (counted + 1.0)

    states_f = node_states.astype(jnp.float32)
    extended = jnp.concatenate([node_states, received], axis=1)
    neighbours = jnp.einsum("drs,dsh->drh", adjacent, extended, preferred_element_type=jnp.float32)
    aggregate = ((states_f + neighbours) * inverse[:, :, None]).astype(jnp.bfloat16)
    preact = jnp.einsum("drh,hk->drk", aggregate, w_message, preferred_element_type=jnp.float32)
    hidden = (states_f + jax.nn.silu(preact)).astype(jnp.bfloat16)

    node_major = exchange(hidden, "day", 1, 0)
    upstream = cotangent.reshape(cotangent.shape[0], -1, width)
    attn_grads, back = attend_blocked(node_major, upstream, w_query, w_key, w_value)
    back_days = exchange(back, "day", 0, 1)

    sigmoid_val = jax.nn.sigmoid(preact)
    pre_grad = (
        back_days.astype(jnp.float32) * sigmoid_val * (1.0 + preact * (1.0 - sigmoid_val))
    ).astype(jnp.bfloat16)
    grad_message = lax.dot_general(
        aggregate.reshape(-1, width),
        pre_grad.reshape(-1, width),
        (((0,), (0,)), ((), ())),
        preferred_element_type=jnp.float32,
    )
    agg_grad = jnp.einsum("drk,hk->drh", pre_grad, w_message, preferred_element_type=jnp.float32)
    term_grad = agg_grad * inverse[:, :, None]
    ext_grad = jnp.einsum(
        "drs,drh->dsh",
        adjacent.astype(jnp.float32),
        term_grad,
        precision=lax.Precision.HIGHEST,
        preferred_element_type=jnp.float32,
    )
    halo_grad = ext_grad[:, node_local:].astype(jnp.bfloat16)
    returned = from_behind(halo_grad, "dom", -1)
    own_grad = ext_grad[:, :node_local]
    scattered = jnp.einsum("dsn,dsh->dnh", slot_hot, returned, preferred_element_type=jnp.float32)
    state_grad = back_days.astype(jnp.float32) + term_grad + own_grad + scattered
    (grad_message, grad_query, grad_key, grad_value), state_grad = tree_sum(
        (grad_message, attn_grads[0], attn_grads[1], attn_grads[2]), ("dom", "day"), state_grad
    )
    return (state_grad, grad_message, grad_query, grad_key, grad_value)


def solution(mesh):
    return jax.shard_map(
        local,
        mesh=mesh,
        in_specs=(
            P("day", "dom", None),
            P("day", "dom"),
            P("day", "dom"),
            P("day", "dom"),
            P("day", "dom"),
            P(),
            P(),
            P(),
            P(),
            P(None, "dom", "day", None, None),
        ),
        out_specs=(P("day", "dom", None), P(), P(), P(), P()),
        check_vma=False,
    )
```

```python
import jax
import jax.numpy as jnp
from jax import lax
from jax.sharding import PartitionSpec as P

HEADS = 4


def from_behind(value, axis, steps):
    count = lax.axis_size(axis)
    pairs = [(source, (source + steps) % count) for source in range(count)]
    return lax.ppermute(value, axis, pairs)


def _power_of_two(count):
    return count > 0 and count & (count - 1) == 0


def _group_pairs(axis, stride, group, shift):
    pairs = []
    for source in range(lax.axis_size(axis)):
        digit = (source // stride) % group
        pairs.append((source, source + ((digit + shift) % group - digit) * stride))
    return pairs


def _scatter_step(flat, axis, stride, group):
    digit = (lax.axis_index(axis) // stride) % group
    chunks = flat.reshape(group, -1)
    if group == 2:
        keep = jnp.where(digit == 0, chunks[0], chunks[1])
        send = jnp.where(digit == 0, chunks[1], chunks[0])
        return keep + lax.ppermute(send, axis, _group_pairs(axis, stride, group, 1))
    total = lax.dynamic_index_in_dim(chunks, digit, 0, keepdims=False)
    for shift in range(1, group):
        send = lax.dynamic_index_in_dim(chunks, (digit + shift) % group, 0, keepdims=False)
        total = total + lax.ppermute(send, axis, _group_pairs(axis, stride, group, shift))
    return total


def _gather_step(flat, axis, stride, group):
    digit = (lax.axis_index(axis) // stride) % group
    if group == 2:
        other = lax.ppermute(flat, axis, _group_pairs(axis, stride, group, 1))
        return jnp.where(
            digit == 0, jnp.concatenate([flat, other]), jnp.concatenate([other, flat])
        )
    got = [flat] + [
        lax.ppermute(flat, axis, _group_pairs(axis, stride, group, shift)) for shift in range(1, group)
    ]
    stacked = jnp.stack(got)
    order = (digit - jnp.arange(group)) % group
    return jnp.take(stacked, order, axis=0).reshape(-1)


def _factors(size):
    if size <= 4:
        return [size]
    return [2] + _factors(size // 2)


def tree_sum(values, axes, companion=None):
    sizes = [lax.axis_size(axis) for axis in axes]
    flat = jnp.concatenate([value.reshape(-1) for value in values])
    total = 1
    for size in sizes:
        total *= size
    if not all(_power_of_two(size) for size in sizes) or flat.shape[0] % total:
        return lax.psum(tuple(values), axes), companion
    steps = []
    for axis, size in zip(axes, sizes):
        stride = 1
        for group in _factors(size):
            if group > 1:
                steps.append((axis, stride, group))
            stride *= group
    for axis, stride, group in steps:
        flat = _scatter_step(flat, axis, stride, group)
    flat, companion = lax.optimization_barrier((flat, companion))
    for axis, stride, group in reversed(steps):
        flat = _gather_step(flat, axis, stride, group)
    results, start = [], 0
    for value in values:
        results.append(flat[start : start + value.size].reshape(value.shape))
        start += value.size
    return tuple(results), companion


def exchange(value, axis, split_axis, concat_axis):
    count = lax.axis_size(axis)
    mine = lax.axis_index(axis)
    size = value.shape[split_axis] // count
    got = []
    for shift in range(count):
        send = lax.dynamic_slice_in_dim(value, ((mine + shift) % count) * size, size, axis=split_axis)
        if shift:
            send = lax.ppermute(send, axis, [(i, (i + shift) % count) for i in range(count)])
        got.append(send)
    stacked = jnp.take(jnp.stack(got), (mine - jnp.arange(count)) % count, axis=0)
    return jnp.concatenate([stacked[k] for k in range(count)], axis=concat_axis)


def adjacency(sources, targets, count_rows, total_rows):
    target_hot = (targets[:, None] == jnp.arange(count_rows, dtype=jnp.int32)[None, :]).astype(
        jnp.bfloat16
    )
    source_hot = (sources[:, None] == jnp.arange(total_rows, dtype=jnp.int32)[None, :]).astype(
        jnp.bfloat16
    )
    counts = lax.dot_general(
        target_hot, source_hot, (((0,), (0,)), ((), ())), preferred_element_type=jnp.float32
    )
    return counts.astype(jnp.bfloat16)


def gnn_forward(states, received, adjacent, w_message):
    extended = jnp.concatenate([states, received], axis=0)
    neighbours = jnp.dot(adjacent, extended, preferred_element_type=jnp.float32)
    counted = jnp.sum(adjacent.astype(jnp.float32), axis=1)
    inverse = 1.0 / (counted + 1.0)
    aggregate = ((states.astype(jnp.float32) + neighbours) * inverse[:, None]).astype(jnp.bfloat16)
    preact = jnp.dot(aggregate, w_message, preferred_element_type=jnp.float32)
    hidden = (states.astype(jnp.float32) + jax.nn.silu(preact)).astype(jnp.bfloat16)
    return (aggregate, preact, inverse, hidden)


def gnn_backward(upstream, aggregate, preact, inverse, adjacent, w_message):
    count_rows = aggregate.shape[0]
    up_float = upstream.astype(jnp.float32)
    sigmoid_val = jax.nn.sigmoid(preact)
    pre_grad = (up_float * sigmoid_val * (1.0 + preact * (1.0 - sigmoid_val))).astype(jnp.bfloat16)
    message_part = lax.dot_general(
        aggregate, pre_grad, (((0,), (0,)), ((), ())), preferred_element_type=jnp.float32
    )
    agg_grad = lax.dot_general(
        pre_grad, w_message, (((1,), (1,)), ((), ())), preferred_element_type=jnp.float32
    )
    term_grad = agg_grad * inverse[:, None]
    ext_grad = lax.dot_general(
        adjacent.astype(jnp.float32),
        term_grad,
        (((0,), (0,)), ((), ())),
        precision=lax.Precision.HIGHEST,
        preferred_element_type=jnp.float32,
    )
    local_grad = up_float + term_grad + ext_grad[:count_rows]
    halo_grad = ext_grad[count_rows:].astype(jnp.bfloat16)
    return (message_part, local_grad, halo_grad)


def attend(states, upstream, w_query, w_key, w_value):
    steps_all, nodes_here, width = states.shape
    head_dim = width // HEADS
    scale_factor = head_dim ** (-0.5)
    flat = states.reshape(steps_all * nodes_here, width)

    def project(weight):
        return jnp.dot(flat, weight, preferred_element_type=jnp.float32).astype(jnp.bfloat16)

    def splitter(matrix):
        return matrix.reshape(steps_all, nodes_here, HEADS, head_dim).astype(jnp.float32)

    queries = project(w_query)
    key_rows = project(w_key)
    value_rows = project(w_value)
    query_f = splitter(queries)
    key_f = splitter(key_rows)
    value_f = splitter(value_rows)
    scores = jnp.einsum("tnhd,snhd->nhts", query_f, key_f) * scale_factor
    causal = jnp.arange(steps_all)[:, None] >= jnp.arange(steps_all)[None, :]
    scores = jnp.where(causal, scores, -jnp.inf)
    highest = jnp.max(scores, axis=-1, keepdims=True)
    exponent = jnp.exp(scores - highest)
    probs = exponent / jnp.sum(exponent, axis=-1, keepdims=True)
    probs_low = probs.astype(jnp.bfloat16).astype(jnp.float32)
    up_heads = splitter(upstream)
    value_grad = jnp.einsum("nhts,tnhd->snhd", probs_low, up_heads).astype(jnp.bfloat16)
    prob_grad = jnp.einsum("tnhd,snhd->nhts", up_heads, value_f)
    score_grad = (
        probs * (prob_grad - jnp.sum(prob_grad * probs, axis=-1, keepdims=True)) * scale_factor
    ).astype(jnp.bfloat16)
    score_f = score_grad.astype(jnp.float32)
    query_grad = jnp.einsum("nhts,snhd->tnhd", score_f, key_f).astype(jnp.bfloat16)
    key_grad = jnp.einsum("nhts,tnhd->snhd", score_f, query_f).astype(jnp.bfloat16)
    query_flat = query_grad.reshape(steps_all * nodes_here, width)
    key_flat = key_grad.reshape(steps_all * nodes_here, width)
    value_flat = value_grad.reshape(steps_all * nodes_here, width)

    def weight_grad(grad_rows):
        return lax.dot_general(
            flat, grad_rows, (((0,), (0,)), ((), ())), preferred_element_type=jnp.float32
        )

    def input_grad(grad_rows, weight):
        return lax.dot_general(
            grad_rows, weight, (((1,), (1,)), ((), ())), preferred_element_type=jnp.float32
        )

    back = upstream.reshape(steps_all * nodes_here, width).astype(jnp.float32)
    back = (
        back
        + input_grad(query_flat, w_query)
        + input_grad(key_flat, w_key)
        + input_grad(value_flat, w_value)
    )
    back = back.astype(jnp.bfloat16).reshape(steps_all, nodes_here, width)
    return ((weight_grad(query_flat), weight_grad(key_flat), weight_grad(value_flat)), back)


def attend_blocked(states, upstream, w_query, w_key, w_value):
    steps_all, nodes_here, width = states.shape
    head_dim = width // HEADS
    scale_factor = head_dim ** (-0.5)
    per_group = max(1, 128 // steps_all)
    if nodes_here % per_group:
        per_group = 1
    groups = nodes_here // per_group
    block = per_group * steps_all
    flat = jnp.swapaxes(states, 0, 1).reshape(groups, block, width)
    up_flat = jnp.swapaxes(upstream, 0, 1).reshape(groups, block, width)
    heads_of = {
        name: weight.reshape(width, HEADS, head_dim)
        for name, weight in (("q", w_query), ("k", w_key), ("v", w_value))
    }

    def contract(spec, left, right):
        return jnp.einsum(spec, left, right, preferred_element_type=jnp.float32)

    queries = contract("gic,chd->ghid", flat, heads_of["q"]).astype(jnp.bfloat16)
    key_rows = contract("gic,chd->ghid", flat, heads_of["k"]).astype(jnp.bfloat16)
    value_rows = contract("gic,chd->ghid", flat, heads_of["v"]).astype(jnp.bfloat16)
    up_heads = up_flat.reshape(groups, block, HEADS, head_dim)
    position = jnp.arange(block)
    same = (position[:, None] // steps_all) == (position[None, :] // steps_all)
    causal = jnp.logical_and(same, (position[:, None] % steps_all) >= (position[None, :] % steps_all))

    scores = contract("ghid,ghjd->ghij", queries, key_rows) * scale_factor
    scores = jnp.where(causal, scores, -jnp.inf)
    highest = jnp.max(scores, axis=-1, keepdims=True)
    exponent = jnp.exp(scores - highest)
    probs = exponent / jnp.sum(exponent, axis=-1, keepdims=True)
    probs_low = probs.astype(jnp.bfloat16)
    value_grad = contract("ghij,gihd->ghjd", probs_low, up_heads).astype(jnp.bfloat16)
    prob_grad = contract("gihd,ghjd->ghij", up_heads, value_rows)
    score_grad = (
        probs * (prob_grad - jnp.sum(prob_grad * probs, axis=-1, keepdims=True)) * scale_factor
    ).astype(jnp.bfloat16)
    score_grad = lax.optimization_barrier(score_grad)
    query_grad = contract("ghij,ghjd->ghid", score_grad, key_rows).astype(jnp.bfloat16)
    key_grad = contract("ghij,ghid->ghjd", score_grad, queries).astype(jnp.bfloat16)

    def weight_grad(grad_rows):
        return contract("gic,ghid->chd", flat, grad_rows).reshape(width, width)

    def input_grad(grad_rows, name):
        return contract("ghid,chd->gic", grad_rows, heads_of[name])

    back = (
        up_flat.astype(jnp.float32)
        + input_grad(query_grad, "q")
        + input_grad(key_grad, "k")
        + input_grad(value_grad, "v")
    )
    back = jnp.swapaxes(back.astype(jnp.bfloat16).reshape(nodes_here, steps_all, width), 0, 1)
    return ((weight_grad(query_grad), weight_grad(key_grad), weight_grad(value_grad)), back)


def local(
    node_states,
    edge_source,
    edge_target,
    halo_rows,
    halo_count,
    w_message,
    w_query,
    w_key,
    w_value,
    cotangent,
):
    days_local, node_local, width = node_states.shape
    halo_slots = halo_rows.shape[1]
    live = jnp.arange(halo_slots)[None, :] < halo_count
    rows = jnp.arange(node_local, dtype=jnp.int32)
    slot_hot = jnp.logical_and(
        halo_rows[:, :, None] == rows[None, None, :], live[:, :, None]
    ).astype(jnp.bfloat16)
    sent = jnp.einsum(
        "dsn,dnh->dsh", slot_hot, node_states, preferred_element_type=jnp.float32
    ).astype(jnp.bfloat16)
    received = from_behind(sent, "dom", 1)

    target_hot = (edge_target[:, :, None] == rows[None, None, :]).astype(jnp.bfloat16)
    extended_ids = jnp.arange(node_local + halo_slots, dtype=jnp.int32)
    source_hot = (edge_source[:, :, None] == extended_ids[None, None, :]).astype(jnp.bfloat16)
    adjacent = jnp.einsum(
        "der,des->drs", target_hot, source_hot, preferred_element_type=jnp.float32
    ).astype(jnp.bfloat16)
    counted = jnp.einsum(
        "der,e->dr",
        target_hot,
        jnp.ones(target_hot.shape[1], jnp.bfloat16),
        preferred_element_type=jnp.float32,
    )
    inverse = 1.0 / (counted + 1.0)

    states_f = node_states.astype(jnp.float32)
    neighbours = jnp.einsum(
        "drs,dsh->drh", adjacent[:, :, :node_local], node_states, preferred_element_type=jnp.float32
    ) + jnp.einsum(
        "drs,dsh->drh", adjacent[:, :, node_local:], received, preferred_element_type=jnp.float32
    )
    aggregate = ((states_f + neighbours) * inverse[:, :, None]).astype(jnp.bfloat16)
    preact = jnp.einsum("drh,hk->drk", aggregate, w_message, preferred_element_type=jnp.float32)
    hidden = (states_f + jax.nn.silu(preact)).astype(jnp.bfloat16)

    node_major = exchange(hidden, "day", 1, 0)
    upstream = cotangent.reshape(cotangent.shape[0], -1, width)
    attn_grads, back = attend_blocked(node_major, upstream, w_query, w_key, w_value)
    back_days = exchange(back, "day", 0, 1)

    sigmoid_val = jax.nn.sigmoid(preact)
    pre_grad = (
        back_days.astype(jnp.float32) * sigmoid_val * (1.0 + preact * (1.0 - sigmoid_val))
    ).astype(jnp.bfloat16)
    grad_message = lax.dot_general(
        aggregate.reshape(-1, width),
        pre_grad.reshape(-1, width),
        (((0,), (0,)), ((), ())),
        preferred_element_type=jnp.float32,
    )
    agg_grad = jnp.einsum("drk,hk->drh", pre_grad, w_message, preferred_element_type=jnp.float32)
    term_grad = agg_grad * inverse[:, :, None]
    ext_grad = jnp.einsum(
        "drs,drh->dsh",
        adjacent.astype(jnp.float32),
        term_grad,
        precision=lax.Precision.HIGHEST,
        preferred_element_type=jnp.float32,
    )
    halo_grad = ext_grad[:, node_local:].astype(jnp.bfloat16)
    returned = from_behind(halo_grad, "dom", -1)
    own_grad = ext_grad[:, :node_local]
    scattered = jnp.einsum("dsn,dsh->dnh", slot_hot, returned, preferred_element_type=jnp.float32)
    state_grad = back_days.astype(jnp.float32) + term_grad + own_grad + scattered
    (grad_message, grad_query, grad_key, grad_value), state_grad = tree_sum(
        (grad_message, attn_grads[0], attn_grads[1], attn_grads[2]), ("dom", "day"), state_grad
    )
    return (state_grad, grad_message, grad_query, grad_key, grad_value)


def solution(mesh):
    return jax.shard_map(
        local,
        mesh=mesh,
        in_specs=(
            P("day", "dom", None),
            P("day", "dom"),
            P("day", "dom"),
            P("day", "dom"),
            P("day", "dom"),
            P(),
            P(),
            P(),
            P(),
            P(None, "dom", "day", None, None),
        ),
        out_specs=(P("day", "dom", None), P(), P(), P(), P()),
        check_vma=False,
    )
```

```python
import jax
import jax.numpy as jnp
from jax import lax
from jax.sharding import PartitionSpec as P

HEADS = 4


def from_behind(value, axis, steps):
    count = lax.axis_size(axis)
    pairs = [(source, (source + steps) % count) for source in range(count)]
    return lax.ppermute(value, axis, pairs)


def _power_of_two(count):
    return count > 0 and count & (count - 1) == 0


def _group_pairs(axis, stride, group, shift):
    pairs = []
    for source in range(lax.axis_size(axis)):
        digit = (source // stride) % group
        pairs.append((source, source + ((digit + shift) % group - digit) * stride))
    return pairs


def _scatter_step(flat, axis, stride, group):
    digit = (lax.axis_index(axis) // stride) % group
    chunks = flat.reshape(group, -1)
    if group == 2:
        keep = jnp.where(digit == 0, chunks[0], chunks[1])
        send = jnp.where(digit == 0, chunks[1], chunks[0])
        return keep + lax.ppermute(send, axis, _group_pairs(axis, stride, group, 1))
    total = lax.dynamic_index_in_dim(chunks, digit, 0, keepdims=False)
    for shift in range(1, group):
        send = lax.dynamic_index_in_dim(chunks, (digit + shift) % group, 0, keepdims=False)
        total = total + lax.ppermute(send, axis, _group_pairs(axis, stride, group, shift))
    return total


def _gather_step(flat, axis, stride, group):
    digit = (lax.axis_index(axis) // stride) % group
    if group == 2:
        other = lax.ppermute(flat, axis, _group_pairs(axis, stride, group, 1))
        return jnp.where(
            digit == 0, jnp.concatenate([flat, other]), jnp.concatenate([other, flat])
        )
    got = [flat] + [
        lax.ppermute(flat, axis, _group_pairs(axis, stride, group, shift)) for shift in range(1, group)
    ]
    stacked = jnp.stack(got)
    order = (digit - jnp.arange(group)) % group
    return jnp.take(stacked, order, axis=0).reshape(-1)


def _factors(size):
    if size <= 4:
        return [size]
    return [2] + _factors(size // 2)


def tree_sum(values, axes, companion=None):
    sizes = [lax.axis_size(axis) for axis in axes]
    flat = jnp.concatenate([value.reshape(-1) for value in values])
    total = 1
    for size in sizes:
        total *= size
    if not all(_power_of_two(size) for size in sizes) or flat.shape[0] % total:
        return lax.psum(tuple(values), axes), companion
    steps = []
    for axis, size in zip(axes, sizes):
        stride = 1
        for group in _factors(size):
            if group > 1:
                steps.append((axis, stride, group))
            stride *= group
    for axis, stride, group in steps:
        flat = _scatter_step(flat, axis, stride, group)
    flat, companion = lax.optimization_barrier((flat, companion))
    for axis, stride, group in reversed(steps):
        flat = _gather_step(flat, axis, stride, group)
    results, start = [], 0
    for value in values:
        results.append(flat[start : start + value.size].reshape(value.shape))
        start += value.size
    return tuple(results), companion


def exchange(value, axis, split_axis, concat_axis):
    count = lax.axis_size(axis)
    mine = lax.axis_index(axis)
    size = value.shape[split_axis] // count
    got = []
    for shift in range(count):
        send = lax.dynamic_slice_in_dim(value, ((mine + shift) % count) * size, size, axis=split_axis)
        if shift:
            send = lax.ppermute(send, axis, [(i, (i + shift) % count) for i in range(count)])
        got.append(send)
    stacked = jnp.take(jnp.stack(got), (mine - jnp.arange(count)) % count, axis=0)
    return jnp.concatenate([stacked[k] for k in range(count)], axis=concat_axis)


def adjacency(sources, targets, count_rows, total_rows):
    target_hot = (targets[:, None] == jnp.arange(count_rows, dtype=jnp.int32)[None, :]).astype(
        jnp.bfloat16
    )
    source_hot = (sources[:, None] == jnp.arange(total_rows, dtype=jnp.int32)[None, :]).astype(
        jnp.bfloat16
    )
    counts = lax.dot_general(
        target_hot, source_hot, (((0,), (0,)), ((), ())), preferred_element_type=jnp.float32
    )
    return counts.astype(jnp.bfloat16)


def gnn_forward(states, received, adjacent, w_message):
    extended = jnp.concatenate([states, received], axis=0)
    neighbours = jnp.dot(adjacent, extended, preferred_element_type=jnp.float32)
    counted = jnp.sum(adjacent.astype(jnp.float32), axis=1)
    inverse = 1.0 / (counted + 1.0)
    aggregate = ((states.astype(jnp.float32) + neighbours) * inverse[:, None]).astype(jnp.bfloat16)
    preact = jnp.dot(aggregate, w_message, preferred_element_type=jnp.float32)
    hidden = (states.astype(jnp.float32) + jax.nn.silu(preact)).astype(jnp.bfloat16)
    return (aggregate, preact, inverse, hidden)


def gnn_backward(upstream, aggregate, preact, inverse, adjacent, w_message):
    count_rows = aggregate.shape[0]
    up_float = upstream.astype(jnp.float32)
    sigmoid_val = jax.nn.sigmoid(preact)
    pre_grad = (up_float * sigmoid_val * (1.0 + preact * (1.0 - sigmoid_val))).astype(jnp.bfloat16)
    message_part = lax.dot_general(
        aggregate, pre_grad, (((0,), (0,)), ((), ())), preferred_element_type=jnp.float32
    )
    agg_grad = lax.dot_general(
        pre_grad, w_message, (((1,), (1,)), ((), ())), preferred_element_type=jnp.float32
    )
    term_grad = agg_grad * inverse[:, None]
    ext_grad = lax.dot_general(
        adjacent.astype(jnp.float32),
        term_grad,
        (((0,), (0,)), ((), ())),
        precision=lax.Precision.HIGHEST,
        preferred_element_type=jnp.float32,
    )
    local_grad = up_float + term_grad + ext_grad[:count_rows]
    halo_grad = ext_grad[count_rows:].astype(jnp.bfloat16)
    return (message_part, local_grad, halo_grad)


def attend(states, upstream, w_query, w_key, w_value):
    steps_all, nodes_here, width = states.shape
    head_dim = width // HEADS
    scale_factor = head_dim ** (-0.5)
    flat = states.reshape(steps_all * nodes_here, width)

    def project(weight):
        return jnp.dot(flat, weight, preferred_element_type=jnp.float32).astype(jnp.bfloat16)

    def splitter(matrix):
        return matrix.reshape(steps_all, nodes_here, HEADS, head_dim).astype(jnp.float32)

    queries = project(w_query)
    key_rows = project(w_key)
    value_rows = project(w_value)
    query_f = splitter(queries)
    key_f = splitter(key_rows)
    value_f = splitter(value_rows)
    scores = jnp.einsum("tnhd,snhd->nhts", query_f, key_f) * scale_factor
    causal = jnp.arange(steps_all)[:, None] >= jnp.arange(steps_all)[None, :]
    scores = jnp.where(causal, scores, -jnp.inf)
    highest = jnp.max(scores, axis=-1, keepdims=True)
    exponent = jnp.exp(scores - highest)
    probs = exponent / jnp.sum(exponent, axis=-1, keepdims=True)
    probs_low = probs.astype(jnp.bfloat16).astype(jnp.float32)
    up_heads = splitter(upstream)
    value_grad = jnp.einsum("nhts,tnhd->snhd", probs_low, up_heads).astype(jnp.bfloat16)
    prob_grad = jnp.einsum("tnhd,snhd->nhts", up_heads, value_f)
    score_grad = (
        probs * (prob_grad - jnp.sum(prob_grad * probs, axis=-1, keepdims=True)) * scale_factor
    ).astype(jnp.bfloat16)
    score_f = score_grad.astype(jnp.float32)
    query_grad = jnp.einsum("nhts,snhd->tnhd", score_f, key_f).astype(jnp.bfloat16)
    key_grad = jnp.einsum("nhts,tnhd->snhd", score_f, query_f).astype(jnp.bfloat16)
    query_flat = query_grad.reshape(steps_all * nodes_here, width)
    key_flat = key_grad.reshape(steps_all * nodes_here, width)
    value_flat = value_grad.reshape(steps_all * nodes_here, width)

    def weight_grad(grad_rows):
        return lax.dot_general(
            flat, grad_rows, (((0,), (0,)), ((), ())), preferred_element_type=jnp.float32
        )

    def input_grad(grad_rows, weight):
        return lax.dot_general(
            grad_rows, weight, (((1,), (1,)), ((), ())), preferred_element_type=jnp.float32
        )

    back = upstream.reshape(steps_all * nodes_here, width).astype(jnp.float32)
    back = (
        back
        + input_grad(query_flat, w_query)
        + input_grad(key_flat, w_key)
        + input_grad(value_flat, w_value)
    )
    back = back.astype(jnp.bfloat16).reshape(steps_all, nodes_here, width)
    return ((weight_grad(query_flat), weight_grad(key_flat), weight_grad(value_flat)), back)


def attend_blocked(states, upstream, w_query, w_key, w_value):
    steps_all, nodes_here, width = states.shape
    head_dim = width // HEADS
    scale_factor = head_dim ** (-0.5)
    per_group = max(1, 128 // steps_all)
    if nodes_here % per_group:
        per_group = 1
    groups = nodes_here // per_group
    block = per_group * steps_all
    flat = jnp.swapaxes(states, 0, 1).reshape(groups, block, width)
    up_flat = jnp.swapaxes(upstream, 0, 1).reshape(groups, block, width)
    heads_of = {
        name: weight.reshape(width, HEADS, head_dim)
        for name, weight in (("q", w_query), ("k", w_key), ("v", w_value))
    }

    def contract(spec, left, right):
        return jnp.einsum(spec, left, right, preferred_element_type=jnp.float32)

    queries = contract("gic,chd->ghid", flat, heads_of["q"]).astype(jnp.bfloat16)
    key_rows = contract("gic,chd->ghid", flat, heads_of["k"]).astype(jnp.bfloat16)
    value_rows = contract("gic,chd->ghid", flat, heads_of["v"]).astype(jnp.bfloat16)
    up_heads = up_flat.reshape(groups, block, HEADS, head_dim)
    position = jnp.arange(block)
    same = (position[:, None] // steps_all) == (position[None, :] // steps_all)
    causal = jnp.logical_and(same, (position[:, None] % steps_all) >= (position[None, :] % steps_all))

    scores = contract("ghid,ghjd->ghij", queries, key_rows) * scale_factor
    scores = jnp.where(causal, scores, -jnp.inf)
    highest = jnp.max(scores, axis=-1, keepdims=True)
    exponent = jnp.exp(scores - highest)
    probs = exponent / jnp.sum(exponent, axis=-1, keepdims=True)
    probs_low = probs.astype(jnp.bfloat16)
    value_grad = contract("ghij,gihd->ghjd", probs_low, up_heads).astype(jnp.bfloat16)
    prob_grad = contract("gihd,ghjd->ghij", up_heads, value_rows)
    score_grad = (
        probs * (prob_grad - jnp.sum(prob_grad * probs, axis=-1, keepdims=True)) * scale_factor
    ).astype(jnp.bfloat16)
    score_grad = lax.optimization_barrier(score_grad)
    query_grad = contract("ghij,ghjd->ghid", score_grad, key_rows).astype(jnp.bfloat16)
    key_grad = contract("ghij,ghid->ghjd", score_grad, queries).astype(jnp.bfloat16)

    def weight_grad(grad_rows):
        return contract("gic,ghid->chd", flat, grad_rows).reshape(width, width)

    def input_grad(grad_rows, name):
        return contract("ghid,chd->gic", grad_rows, heads_of[name])

    through = input_grad(query_grad, "q") + input_grad(key_grad, "k") + input_grad(value_grad, "v")
    through = jnp.swapaxes(through.reshape(nodes_here, steps_all, width), 0, 1)
    back = (upstream.astype(jnp.float32) + through).astype(jnp.bfloat16)
    return ((weight_grad(query_grad), weight_grad(key_grad), weight_grad(value_grad)), back)


def local(
    node_states,
    edge_source,
    edge_target,
    halo_rows,
    halo_count,
    w_message,
    w_query,
    w_key,
    w_value,
    cotangent,
):
    days_local, node_local, width = node_states.shape
    halo_slots = halo_rows.shape[1]
    live = jnp.arange(halo_slots)[None, :] < halo_count
    rows = jnp.arange(node_local, dtype=jnp.int32)
    slot_hot = jnp.logical_and(
        halo_rows[:, :, None] == rows[None, None, :], live[:, :, None]
    ).astype(jnp.bfloat16)
    sent = jnp.einsum(
        "dsn,dnh->dsh", slot_hot, node_states, preferred_element_type=jnp.float32
    ).astype(jnp.bfloat16)
    received = from_behind(sent, "dom", 1)

    target_hot = (edge_target[:, :, None] == rows[None, None, :]).astype(jnp.bfloat16)
    extended_ids = jnp.arange(node_local + halo_slots, dtype=jnp.int32)
    source_hot = (edge_source[:, :, None] == extended_ids[None, None, :]).astype(jnp.bfloat16)
    adjacent = jnp.einsum(
        "der,des->drs", target_hot, source_hot, preferred_element_type=jnp.float32
    ).astype(jnp.bfloat16)
    counted = jnp.einsum(
        "der,e->dr",
        target_hot,
        jnp.ones(target_hot.shape[1], jnp.bfloat16),
        preferred_element_type=jnp.float32,
    )
    inverse = 1.0 / (counted + 1.0)

    states_f = node_states.astype(jnp.float32)
    extended = jnp.concatenate([node_states, received], axis=1)
    neighbours = jnp.einsum("drs,dsh->drh", adjacent, extended, preferred_element_type=jnp.float32)
    aggregate = ((states_f + neighbours) * inverse[:, :, None]).astype(jnp.bfloat16)
    preact = jnp.einsum("drh,hk->drk", aggregate, w_message, preferred_element_type=jnp.float32)
    hidden = (states_f + jax.nn.silu(preact)).astype(jnp.bfloat16)

    node_major = exchange(hidden, "day", 1, 0)
    upstream = cotangent.reshape(cotangent.shape[0], -1, width)
    attn_grads, back = attend_blocked(node_major, upstream, w_query, w_key, w_value)
    back_days = exchange(back, "day", 0, 1)

    sigmoid_val = jax.nn.sigmoid(preact)
    pre_grad = (
        back_days.astype(jnp.float32) * sigmoid_val * (1.0 + preact * (1.0 - sigmoid_val))
    ).astype(jnp.bfloat16)
    grad_message = lax.dot_general(
        aggregate.reshape(-1, width),
        pre_grad.reshape(-1, width),
        (((0,), (0,)), ((), ())),
        preferred_element_type=jnp.float32,
    )
    agg_grad = jnp.einsum("drk,hk->drh", pre_grad, w_message, preferred_element_type=jnp.float32)
    term_grad = agg_grad * inverse[:, :, None]
    ext_grad = jnp.einsum(
        "drs,drh->dsh",
        adjacent.astype(jnp.float32),
        term_grad,
        precision=lax.Precision.HIGHEST,
        preferred_element_type=jnp.float32,
    )
    halo_grad = ext_grad[:, node_local:].astype(jnp.bfloat16)
    returned = from_behind(halo_grad, "dom", -1)
    own_grad = ext_grad[:, :node_local]
    scattered = jnp.einsum("dsn,dsh->dnh", slot_hot, returned, preferred_element_type=jnp.float32)
    state_grad = back_days.astype(jnp.float32) + term_grad + own_grad + scattered
    (grad_message, grad_query, grad_key, grad_value), state_grad = tree_sum(
        (grad_message, attn_grads[0], attn_grads[1], attn_grads[2]), ("dom", "day"), state_grad
    )
    return (state_grad, grad_message, grad_query, grad_key, grad_value)


def solution(mesh):
    return jax.shard_map(
        local,
        mesh=mesh,
        in_specs=(
            P("day", "dom", None),
            P("day", "dom"),
            P("day", "dom"),
            P("day", "dom"),
            P("day", "dom"),
            P(),
            P(),
            P(),
            P(),
            P(None, "dom", "day", None, None),
        ),
        out_specs=(P("day", "dom", None), P(), P(), P(), P()),
        check_vma=False,
    )
```

```python
import jax
import jax.numpy as jnp
from jax import lax
from jax.sharding import PartitionSpec as P

HEADS = 4


def from_behind(value, axis, steps):
    count = lax.axis_size(axis)
    pairs = [(source, (source + steps) % count) for source in range(count)]
    return lax.ppermute(value, axis, pairs)


def _power_of_two(count):
    return count > 0 and count & (count - 1) == 0


def _group_pairs(axis, stride, group, shift):
    pairs = []
    for source in range(lax.axis_size(axis)):
        digit = (source // stride) % group
        pairs.append((source, source + ((digit + shift) % group - digit) * stride))
    return pairs


def _scatter_step(flat, axis, stride, group):
    digit = (lax.axis_index(axis) // stride) % group
    chunks = flat.reshape(group, -1)
    if group == 2:
        keep = jnp.where(digit == 0, chunks[0], chunks[1])
        send = jnp.where(digit == 0, chunks[1], chunks[0])
        return keep + lax.ppermute(send, axis, _group_pairs(axis, stride, group, 1))
    total = lax.dynamic_index_in_dim(chunks, digit, 0, keepdims=False)
    for shift in range(1, group):
        send = lax.dynamic_index_in_dim(chunks, (digit + shift) % group, 0, keepdims=False)
        total = total + lax.ppermute(send, axis, _group_pairs(axis, stride, group, shift))
    return total


def _gather_step(flat, axis, stride, group):
    digit = (lax.axis_index(axis) // stride) % group
    if group == 2:
        other = lax.ppermute(flat, axis, _group_pairs(axis, stride, group, 1))
        return jnp.where(
            digit == 0, jnp.concatenate([flat, other]), jnp.concatenate([other, flat])
        )
    got = [flat] + [
        lax.ppermute(flat, axis, _group_pairs(axis, stride, group, shift)) for shift in range(1, group)
    ]
    stacked = jnp.stack(got)
    order = (digit - jnp.arange(group)) % group
    return jnp.take(stacked, order, axis=0).reshape(-1)


def _factors(size):
    if size <= 4:
        return [size]
    return [2] + _factors(size // 2)


def tree_sum(values, axes, companion=None):
    sizes = [lax.axis_size(axis) for axis in axes]
    flat = jnp.concatenate([value.reshape(-1) for value in values])
    total = 1
    for size in sizes:
        total *= size
    if not all(_power_of_two(size) for size in sizes) or flat.shape[0] % total:
        return lax.psum(tuple(values), axes), companion
    steps = []
    for axis, size in zip(axes, sizes):
        stride = 1
        for group in _factors(size):
            if group > 1:
                steps.append((axis, stride, group))
            stride *= group
    for axis, stride, group in steps:
        flat = _scatter_step(flat, axis, stride, group)
    flat, companion = lax.optimization_barrier((flat, companion))
    for axis, stride, group in reversed(steps):
        flat = _gather_step(flat, axis, stride, group)
    results, start = [], 0
    for value in values:
        results.append(flat[start : start + value.size].reshape(value.shape))
        start += value.size
    return tuple(results), companion


def exchange(value, axis, split_axis, concat_axis):
    count = lax.axis_size(axis)
    mine = lax.axis_index(axis)
    size = value.shape[split_axis] // count
    got = []
    for shift in range(count):
        send = lax.dynamic_slice_in_dim(value, ((mine + shift) % count) * size, size, axis=split_axis)
        if shift:
            send = lax.ppermute(send, axis, [(i, (i + shift) % count) for i in range(count)])
        got.append(send)
    stacked = jnp.take(jnp.stack(got), (mine - jnp.arange(count)) % count, axis=0)
    return jnp.concatenate([stacked[k] for k in range(count)], axis=concat_axis)


def adjacency(sources, targets, count_rows, total_rows):
    target_hot = (targets[:, None] == jnp.arange(count_rows, dtype=jnp.int32)[None, :]).astype(
        jnp.bfloat16
    )
    source_hot = (sources[:, None] == jnp.arange(total_rows, dtype=jnp.int32)[None, :]).astype(
        jnp.bfloat16
    )
    counts = lax.dot_general(
        target_hot, source_hot, (((0,), (0,)), ((), ())), preferred_element_type=jnp.float32
    )
    return counts.astype(jnp.bfloat16)


def gnn_forward(states, received, adjacent, w_message):
    extended = jnp.concatenate([states, received], axis=0)
    neighbours = jnp.dot(adjacent, extended, preferred_element_type=jnp.float32)
    counted = jnp.sum(adjacent.astype(jnp.float32), axis=1)
    inverse = 1.0 / (counted + 1.0)
    aggregate = ((states.astype(jnp.float32) + neighbours) * inverse[:, None]).astype(jnp.bfloat16)
    preact = jnp.dot(aggregate, w_message, preferred_element_type=jnp.float32)
    hidden = (states.astype(jnp.float32) + jax.nn.silu(preact)).astype(jnp.bfloat16)
    return (aggregate, preact, inverse, hidden)


def gnn_backward(upstream, aggregate, preact, inverse, adjacent, w_message):
    count_rows = aggregate.shape[0]
    up_float = upstream.astype(jnp.float32)
    sigmoid_val = jax.nn.sigmoid(preact)
    pre_grad = (up_float * sigmoid_val * (1.0 + preact * (1.0 - sigmoid_val))).astype(jnp.bfloat16)
    message_part = lax.dot_general(
        aggregate, pre_grad, (((0,), (0,)), ((), ())), preferred_element_type=jnp.float32
    )
    agg_grad = lax.dot_general(
        pre_grad, w_message, (((1,), (1,)), ((), ())), preferred_element_type=jnp.float32
    )
    term_grad = agg_grad * inverse[:, None]
    ext_grad = lax.dot_general(
        adjacent.astype(jnp.float32),
        term_grad,
        (((0,), (0,)), ((), ())),
        precision=lax.Precision.HIGHEST,
        preferred_element_type=jnp.float32,
    )
    local_grad = up_float + term_grad + ext_grad[:count_rows]
    halo_grad = ext_grad[count_rows:].astype(jnp.bfloat16)
    return (message_part, local_grad, halo_grad)


def attend(states, upstream, w_query, w_key, w_value):
    steps_all, nodes_here, width = states.shape
    head_dim = width // HEADS
    scale_factor = head_dim ** (-0.5)
    flat = states.reshape(steps_all * nodes_here, width)

    def project(weight):
        return jnp.dot(flat, weight, preferred_element_type=jnp.float32).astype(jnp.bfloat16)

    def splitter(matrix):
        return matrix.reshape(steps_all, nodes_here, HEADS, head_dim).astype(jnp.float32)

    queries = project(w_query)
    key_rows = project(w_key)
    value_rows = project(w_value)
    query_f = splitter(queries)
    key_f = splitter(key_rows)
    value_f = splitter(value_rows)
    scores = jnp.einsum("tnhd,snhd->nhts", query_f, key_f) * scale_factor
    causal = jnp.arange(steps_all)[:, None] >= jnp.arange(steps_all)[None, :]
    scores = jnp.where(causal, scores, -jnp.inf)
    highest = jnp.max(scores, axis=-1, keepdims=True)
    exponent = jnp.exp(scores - highest)
    probs = exponent / jnp.sum(exponent, axis=-1, keepdims=True)
    probs_low = probs.astype(jnp.bfloat16).astype(jnp.float32)
    up_heads = splitter(upstream)
    value_grad = jnp.einsum("nhts,tnhd->snhd", probs_low, up_heads).astype(jnp.bfloat16)
    prob_grad = jnp.einsum("tnhd,snhd->nhts", up_heads, value_f)
    score_grad = (
        probs * (prob_grad - jnp.sum(prob_grad * probs, axis=-1, keepdims=True)) * scale_factor
    ).astype(jnp.bfloat16)
    score_f = score_grad.astype(jnp.float32)
    query_grad = jnp.einsum("nhts,snhd->tnhd", score_f, key_f).astype(jnp.bfloat16)
    key_grad = jnp.einsum("nhts,tnhd->snhd", score_f, query_f).astype(jnp.bfloat16)
    query_flat = query_grad.reshape(steps_all * nodes_here, width)
    key_flat = key_grad.reshape(steps_all * nodes_here, width)
    value_flat = value_grad.reshape(steps_all * nodes_here, width)

    def weight_grad(grad_rows):
        return lax.dot_general(
            flat, grad_rows, (((0,), (0,)), ((), ())), preferred_element_type=jnp.float32
        )

    def input_grad(grad_rows, weight):
        return lax.dot_general(
            grad_rows, weight, (((1,), (1,)), ((), ())), preferred_element_type=jnp.float32
        )

    back = upstream.reshape(steps_all * nodes_here, width).astype(jnp.float32)
    back = (
        back
        + input_grad(query_flat, w_query)
        + input_grad(key_flat, w_key)
        + input_grad(value_flat, w_value)
    )
    back = back.astype(jnp.bfloat16).reshape(steps_all, nodes_here, width)
    return ((weight_grad(query_flat), weight_grad(key_flat), weight_grad(value_flat)), back)


def attend_blocked(states, upstream, w_query, w_key, w_value):
    steps_all, nodes_here, width = states.shape
    head_dim = width // HEADS
    scale_factor = head_dim ** (-0.5)
    per_group = max(1, 128 // steps_all)
    if nodes_here % per_group:
        per_group = 1
    groups = nodes_here // per_group
    block = per_group * steps_all
    up_flat = jnp.swapaxes(upstream, 0, 1).reshape(groups, block, width)
    heads_of = {
        name: weight.reshape(width, HEADS, head_dim)
        for name, weight in (("q", w_query), ("k", w_key), ("v", w_value))
    }

    def contract(spec, left, right):
        return jnp.einsum(spec, left, right, preferred_element_type=jnp.float32)

    by_day = states.reshape(steps_all, groups, per_group, width)

    def project(name):
        rows = contract("tgac,chd->ghatd", by_day, heads_of[name]).astype(jnp.bfloat16)
        return rows.reshape(groups, HEADS, block, head_dim)

    queries = project("q")
    key_rows = project("k")
    value_rows = project("v")
    up_heads = up_flat.reshape(groups, block, HEADS, head_dim)
    position = jnp.arange(block)
    same = (position[:, None] // steps_all) == (position[None, :] // steps_all)
    causal = jnp.logical_and(same, (position[:, None] % steps_all) >= (position[None, :] % steps_all))

    scores = contract("ghid,ghjd->ghij", queries, key_rows) * scale_factor
    scores = jnp.where(causal, scores, -jnp.inf)
    highest = jnp.max(scores, axis=-1, keepdims=True)
    exponent = jnp.exp(scores - highest)
    probs = exponent / jnp.sum(exponent, axis=-1, keepdims=True)
    probs_low = probs.astype(jnp.bfloat16)
    value_grad = contract("ghij,gihd->ghjd", probs_low, up_heads).astype(jnp.bfloat16)
    prob_grad = contract("gihd,ghjd->ghij", up_heads, value_rows)
    score_grad = (
        probs * (prob_grad - jnp.sum(prob_grad * probs, axis=-1, keepdims=True)) * scale_factor
    ).astype(jnp.bfloat16)
    score_grad = lax.optimization_barrier(score_grad)
    query_grad = contract("ghij,ghjd->ghid", score_grad, key_rows).astype(jnp.bfloat16)
    key_grad = contract("ghij,ghid->ghjd", score_grad, queries).astype(jnp.bfloat16)

    def weight_grad(grad_rows):
        split_rows = grad_rows.reshape(groups, HEADS, per_group, steps_all, head_dim)
        return contract("tgac,ghatd->chd", by_day, split_rows).reshape(width, width)

    def input_grad(grad_rows, name):
        return contract("ghid,chd->gic", grad_rows, heads_of[name])

    through = input_grad(query_grad, "q") + input_grad(key_grad, "k") + input_grad(value_grad, "v")
    through = jnp.swapaxes(through.reshape(nodes_here, steps_all, width), 0, 1)
    back = (upstream.astype(jnp.float32) + through).astype(jnp.bfloat16)
    return ((weight_grad(query_grad), weight_grad(key_grad), weight_grad(value_grad)), back)


def local(
    node_states,
    edge_source,
    edge_target,
    halo_rows,
    halo_count,
    w_message,
    w_query,
    w_key,
    w_value,
    cotangent,
):
    days_local, node_local, width = node_states.shape
    halo_slots = halo_rows.shape[1]
    live = jnp.arange(halo_slots)[None, :] < halo_count
    rows = jnp.arange(node_local, dtype=jnp.int32)
    slot_hot = jnp.logical_and(
        halo_rows[:, :, None] == rows[None, None, :], live[:, :, None]
    ).astype(jnp.bfloat16)
    sent = jnp.einsum(
        "dsn,dnh->dsh", slot_hot, node_states, preferred_element_type=jnp.float32
    ).astype(jnp.bfloat16)
    received = from_behind(sent, "dom", 1)

    target_hot = (edge_target[:, :, None] == rows[None, None, :]).astype(jnp.bfloat16)
    extended_ids = jnp.arange(node_local + halo_slots, dtype=jnp.int32)
    source_hot = (edge_source[:, :, None] == extended_ids[None, None, :]).astype(jnp.bfloat16)
    adjacent = jnp.einsum(
        "der,des->drs", target_hot, source_hot, preferred_element_type=jnp.float32
    ).astype(jnp.bfloat16)
    counted = jnp.einsum(
        "der,e->dr",
        target_hot,
        jnp.ones(target_hot.shape[1], jnp.bfloat16),
        preferred_element_type=jnp.float32,
    )
    inverse = 1.0 / (counted + 1.0)

    states_f = node_states.astype(jnp.float32)
    extended = jnp.concatenate([node_states, received], axis=1)
    neighbours = jnp.einsum("drs,dsh->drh", adjacent, extended, preferred_element_type=jnp.float32)
    aggregate = ((states_f + neighbours) * inverse[:, :, None]).astype(jnp.bfloat16)
    preact = jnp.einsum("drh,hk->drk", aggregate, w_message, preferred_element_type=jnp.float32)
    hidden = (states_f + jax.nn.silu(preact)).astype(jnp.bfloat16)

    node_major = exchange(hidden, "day", 1, 0)
    upstream = cotangent.reshape(cotangent.shape[0], -1, width)
    attn_grads, back = attend_blocked(node_major, upstream, w_query, w_key, w_value)
    back_days = exchange(back, "day", 0, 1)

    sigmoid_val = jax.nn.sigmoid(preact)
    pre_grad = (
        back_days.astype(jnp.float32) * sigmoid_val * (1.0 + preact * (1.0 - sigmoid_val))
    ).astype(jnp.bfloat16)
    grad_message = lax.dot_general(
        aggregate.reshape(-1, width),
        pre_grad.reshape(-1, width),
        (((0,), (0,)), ((), ())),
        preferred_element_type=jnp.float32,
    )
    agg_grad = jnp.einsum("drk,hk->drh", pre_grad, w_message, preferred_element_type=jnp.float32)
    term_grad = agg_grad * inverse[:, :, None]
    ext_grad = jnp.einsum(
        "drs,drh->dsh",
        adjacent.astype(jnp.float32),
        term_grad,
        precision=lax.Precision.HIGHEST,
        preferred_element_type=jnp.float32,
    )
    halo_grad = ext_grad[:, node_local:].astype(jnp.bfloat16)
    returned = from_behind(halo_grad, "dom", -1)
    own_grad = ext_grad[:, :node_local]
    scattered = jnp.einsum("dsn,dsh->dnh", slot_hot, returned, preferred_element_type=jnp.float32)
    state_grad = back_days.astype(jnp.float32) + term_grad + own_grad + scattered
    (grad_message, grad_query, grad_key, grad_value), state_grad = tree_sum(
        (grad_message, attn_grads[0], attn_grads[1], attn_grads[2]), ("dom", "day"), state_grad
    )
    return (state_grad, grad_message, grad_query, grad_key, grad_value)


def solution(mesh):
    return jax.shard_map(
        local,
        mesh=mesh,
        in_specs=(
            P("day", "dom", None),
            P("day", "dom"),
            P("day", "dom"),
            P("day", "dom"),
            P("day", "dom"),
            P(),
            P(),
            P(),
            P(),
            P(None, "dom", "day", None, None),
        ),
        out_specs=(P("day", "dom", None), P(), P(), P(), P()),
        check_vma=False,
    )
```

```python
import jax
import jax.numpy as jnp
from jax import lax
from jax.sharding import PartitionSpec as P

HEADS = 4


def from_behind(value, axis, steps):
    count = lax.axis_size(axis)
    pairs = [(source, (source + steps) % count) for source in range(count)]
    return lax.ppermute(value, axis, pairs)


def _power_of_two(count):
    return count > 0 and count & (count - 1) == 0


def _group_pairs(axis, stride, group, shift):
    pairs = []
    for source in range(lax.axis_size(axis)):
        digit = (source // stride) % group
        pairs.append((source, source + ((digit + shift) % group - digit) * stride))
    return pairs


def _scatter_step(flat, axis, stride, group):
    digit = (lax.axis_index(axis) // stride) % group
    chunks = flat.reshape(group, -1)
    if group == 2:
        keep = jnp.where(digit == 0, chunks[0], chunks[1])
        send = jnp.where(digit == 0, chunks[1], chunks[0])
        return keep + lax.ppermute(send, axis, _group_pairs(axis, stride, group, 1))
    total = lax.dynamic_index_in_dim(chunks, digit, 0, keepdims=False)
    for shift in range(1, group):
        send = lax.dynamic_index_in_dim(chunks, (digit + shift) % group, 0, keepdims=False)
        total = total + lax.ppermute(send, axis, _group_pairs(axis, stride, group, shift))
    return total


def _gather_step(flat, axis, stride, group):
    digit = (lax.axis_index(axis) // stride) % group
    if group == 2:
        other = lax.ppermute(flat, axis, _group_pairs(axis, stride, group, 1))
        return jnp.where(
            digit == 0, jnp.concatenate([flat, other]), jnp.concatenate([other, flat])
        )
    got = [flat] + [
        lax.ppermute(flat, axis, _group_pairs(axis, stride, group, shift)) for shift in range(1, group)
    ]
    stacked = jnp.stack(got)
    order = (digit - jnp.arange(group)) % group
    return jnp.take(stacked, order, axis=0).reshape(-1)


def _factors(size):
    if size <= 4:
        return [size]
    return [2] + _factors(size // 2)


def tree_sum(values, axes, companion=None):
    sizes = [lax.axis_size(axis) for axis in axes]
    flat = jnp.concatenate([value.reshape(-1) for value in values])
    total = 1
    for size in sizes:
        total *= size
    if not all(_power_of_two(size) for size in sizes) or flat.shape[0] % total:
        return lax.psum(tuple(values), axes), companion
    steps = []
    for axis, size in zip(axes, sizes):
        stride = 1
        for group in _factors(size):
            if group > 1:
                steps.append((axis, stride, group))
            stride *= group
    for axis, stride, group in steps:
        flat = _scatter_step(flat, axis, stride, group)
    flat, companion = lax.optimization_barrier((flat, companion))
    for axis, stride, group in reversed(steps):
        flat = _gather_step(flat, axis, stride, group)
    results, start = [], 0
    for value in values:
        results.append(flat[start : start + value.size].reshape(value.shape))
        start += value.size
    return tuple(results), companion


def exchange(value, axis, split_axis, concat_axis):
    count = lax.axis_size(axis)
    mine = lax.axis_index(axis)
    size = value.shape[split_axis] // count
    got = []
    for shift in range(count):
        send = lax.dynamic_slice_in_dim(value, ((mine + shift) % count) * size, size, axis=split_axis)
        if shift:
            send = lax.ppermute(send, axis, [(i, (i + shift) % count) for i in range(count)])
        got.append(send)
    stacked = jnp.take(jnp.stack(got), (mine - jnp.arange(count)) % count, axis=0)
    return jnp.concatenate([stacked[k] for k in range(count)], axis=concat_axis)


def adjacency(sources, targets, count_rows, total_rows):
    target_hot = (targets[:, None] == jnp.arange(count_rows, dtype=jnp.int32)[None, :]).astype(
        jnp.bfloat16
    )
    source_hot = (sources[:, None] == jnp.arange(total_rows, dtype=jnp.int32)[None, :]).astype(
        jnp.bfloat16
    )
    counts = lax.dot_general(
        target_hot, source_hot, (((0,), (0,)), ((), ())), preferred_element_type=jnp.float32
    )
    return counts.astype(jnp.bfloat16)


def gnn_forward(states, received, adjacent, w_message):
    extended = jnp.concatenate([states, received], axis=0)
    neighbours = jnp.dot(adjacent, extended, preferred_element_type=jnp.float32)
    counted = jnp.sum(adjacent.astype(jnp.float32), axis=1)
    inverse = 1.0 / (counted + 1.0)
    aggregate = ((states.astype(jnp.float32) + neighbours) * inverse[:, None]).astype(jnp.bfloat16)
    preact = jnp.dot(aggregate, w_message, preferred_element_type=jnp.float32)
    hidden = (states.astype(jnp.float32) + jax.nn.silu(preact)).astype(jnp.bfloat16)
    return (aggregate, preact, inverse, hidden)


def gnn_backward(upstream, aggregate, preact, inverse, adjacent, w_message):
    count_rows = aggregate.shape[0]
    up_float = upstream.astype(jnp.float32)
    sigmoid_val = jax.nn.sigmoid(preact)
    pre_grad = (up_float * sigmoid_val * (1.0 + preact * (1.0 - sigmoid_val))).astype(jnp.bfloat16)
    message_part = lax.dot_general(
        aggregate, pre_grad, (((0,), (0,)), ((), ())), preferred_element_type=jnp.float32
    )
    agg_grad = lax.dot_general(
        pre_grad, w_message, (((1,), (1,)), ((), ())), preferred_element_type=jnp.float32
    )
    term_grad = agg_grad * inverse[:, None]
    ext_grad = lax.dot_general(
        adjacent.astype(jnp.float32),
        term_grad,
        (((0,), (0,)), ((), ())),
        precision=lax.Precision.HIGHEST,
        preferred_element_type=jnp.float32,
    )
    local_grad = up_float + term_grad + ext_grad[:count_rows]
    halo_grad = ext_grad[count_rows:].astype(jnp.bfloat16)
    return (message_part, local_grad, halo_grad)


def attend(states, upstream, w_query, w_key, w_value):
    steps_all, nodes_here, width = states.shape
    head_dim = width // HEADS
    scale_factor = head_dim ** (-0.5)
    flat = states.reshape(steps_all * nodes_here, width)

    def project(weight):
        return jnp.dot(flat, weight, preferred_element_type=jnp.float32).astype(jnp.bfloat16)

    def splitter(matrix):
        return matrix.reshape(steps_all, nodes_here, HEADS, head_dim).astype(jnp.float32)

    queries = project(w_query)
    key_rows = project(w_key)
    value_rows = project(w_value)
    query_f = splitter(queries)
    key_f = splitter(key_rows)
    value_f = splitter(value_rows)
    scores = jnp.einsum("tnhd,snhd->nhts", query_f, key_f) * scale_factor
    causal = jnp.arange(steps_all)[:, None] >= jnp.arange(steps_all)[None, :]
    scores = jnp.where(causal, scores, -jnp.inf)
    highest = jnp.max(scores, axis=-1, keepdims=True)
    exponent = jnp.exp(scores - highest)
    probs = exponent / jnp.sum(exponent, axis=-1, keepdims=True)
    probs_low = probs.astype(jnp.bfloat16).astype(jnp.float32)
    up_heads = splitter(upstream)
    value_grad = jnp.einsum("nhts,tnhd->snhd", probs_low, up_heads).astype(jnp.bfloat16)
    prob_grad = jnp.einsum("tnhd,snhd->nhts", up_heads, value_f)
    score_grad = (
        probs * (prob_grad - jnp.sum(prob_grad * probs, axis=-1, keepdims=True)) * scale_factor
    ).astype(jnp.bfloat16)
    score_f = score_grad.astype(jnp.float32)
    query_grad = jnp.einsum("nhts,snhd->tnhd", score_f, key_f).astype(jnp.bfloat16)
    key_grad = jnp.einsum("nhts,tnhd->snhd", score_f, query_f).astype(jnp.bfloat16)
    query_flat = query_grad.reshape(steps_all * nodes_here, width)
    key_flat = key_grad.reshape(steps_all * nodes_here, width)
    value_flat = value_grad.reshape(steps_all * nodes_here, width)

    def weight_grad(grad_rows):
        return lax.dot_general(
            flat, grad_rows, (((0,), (0,)), ((), ())), preferred_element_type=jnp.float32
        )

    def input_grad(grad_rows, weight):
        return lax.dot_general(
            grad_rows, weight, (((1,), (1,)), ((), ())), preferred_element_type=jnp.float32
        )

    back = upstream.reshape(steps_all * nodes_here, width).astype(jnp.float32)
    back = (
        back
        + input_grad(query_flat, w_query)
        + input_grad(key_flat, w_key)
        + input_grad(value_flat, w_value)
    )
    back = back.astype(jnp.bfloat16).reshape(steps_all, nodes_here, width)
    return ((weight_grad(query_flat), weight_grad(key_flat), weight_grad(value_flat)), back)


def attend_blocked(states, upstream, w_query, w_key, w_value):
    steps_all, nodes_here, width = states.shape
    head_dim = width // HEADS
    scale_factor = head_dim ** (-0.5)
    per_group = max(1, 128 // steps_all)
    if nodes_here % per_group:
        per_group = 1
    groups = nodes_here // per_group
    block = per_group * steps_all
    flat = jnp.swapaxes(states, 0, 1).reshape(groups, block, width)
    up_flat = jnp.swapaxes(upstream, 0, 1).reshape(groups, block, width)
    heads_of = {
        name: weight.reshape(width, HEADS, head_dim)
        for name, weight in (("q", w_query), ("k", w_key), ("v", w_value))
    }

    def contract(spec, left, right):
        return jnp.einsum(spec, left, right, preferred_element_type=jnp.float32)

    queries = contract("gic,chd->ghid", flat, heads_of["q"]).astype(jnp.bfloat16)
    key_rows = contract("gic,chd->ghid", flat, heads_of["k"]).astype(jnp.bfloat16)
    value_rows = contract("gic,chd->ghid", flat, heads_of["v"]).astype(jnp.bfloat16)
    up_heads = up_flat.reshape(groups, block, HEADS, head_dim)
    position = jnp.arange(block)
    same = (position[:, None] // steps_all) == (position[None, :] // steps_all)
    causal = jnp.logical_and(same, (position[:, None] % steps_all) >= (position[None, :] % steps_all))

    scores = contract("ghid,ghjd->ghij", queries, key_rows) * scale_factor
    scores = jnp.where(causal, scores, -jnp.inf)
    highest = jnp.max(scores, axis=-1, keepdims=True)
    exponent = jnp.exp(scores - highest)
    probs = exponent / jnp.sum(exponent, axis=-1, keepdims=True)
    probs_low = probs.astype(jnp.bfloat16)
    value_grad = contract("ghij,gihd->ghjd", probs_low, up_heads).astype(jnp.bfloat16)
    prob_grad = contract("gihd,ghjd->ghij", up_heads, value_rows)
    score_grad = (
        probs * (prob_grad - jnp.sum(prob_grad * probs, axis=-1, keepdims=True)) * scale_factor
    ).astype(jnp.bfloat16)
    score_grad = lax.optimization_barrier(score_grad)
    query_grad = contract("ghij,ghjd->ghid", score_grad, key_rows).astype(jnp.bfloat16)
    key_grad = contract("ghij,ghid->ghjd", score_grad, queries).astype(jnp.bfloat16)

    def weight_grad(grad_rows):
        return contract("gic,ghid->chd", flat, grad_rows).reshape(width, width)

    def input_grad(grad_rows, name):
        return contract("ghid,chd->gic", grad_rows, heads_of[name])

    through = input_grad(query_grad, "q") + input_grad(key_grad, "k") + input_grad(value_grad, "v")
    through = jnp.swapaxes(through.reshape(nodes_here, steps_all, width), 0, 1)
    back = (upstream.astype(jnp.float32) + through).astype(jnp.bfloat16)
    return ((weight_grad(query_grad), weight_grad(key_grad), weight_grad(value_grad)), back)


def local(
    node_states,
    edge_source,
    edge_target,
    halo_rows,
    halo_count,
    w_message,
    w_query,
    w_key,
    w_value,
    cotangent,
):
    days_local, node_local, width = node_states.shape
    halo_slots = halo_rows.shape[1]
    live = jnp.arange(halo_slots)[None, :] < halo_count
    rows = jnp.arange(node_local, dtype=jnp.int32)
    slot_hot = jnp.logical_and(
        halo_rows[:, :, None] == rows[None, None, :], live[:, :, None]
    ).astype(jnp.bfloat16)
    sent = jnp.einsum(
        "dsn,dnh->dsh", slot_hot, node_states, preferred_element_type=jnp.float32
    ).astype(jnp.bfloat16)
    received = from_behind(sent, "dom", 1)

    target_hot = (edge_target[:, :, None] == rows[None, None, :]).astype(jnp.bfloat16)
    extended_ids = jnp.arange(node_local + halo_slots, dtype=jnp.int32)
    source_hot = (edge_source[:, :, None] == extended_ids[None, None, :]).astype(jnp.bfloat16)
    adjacent = jnp.einsum(
        "der,des->drs", target_hot, source_hot, preferred_element_type=jnp.float32
    ).astype(jnp.bfloat16)
    counted = jnp.einsum(
        "der,e->dr",
        target_hot,
        jnp.ones(target_hot.shape[1], jnp.bfloat16),
        preferred_element_type=jnp.float32,
    )
    inverse = 1.0 / (counted + 1.0)

    states_f = node_states.astype(jnp.float32)
    extended = jnp.concatenate([node_states, received], axis=1)
    neighbours = jnp.einsum("drs,dsh->drh", adjacent, extended, preferred_element_type=jnp.float32)
    aggregate = ((states_f + neighbours) * inverse[:, :, None]).astype(jnp.bfloat16)
    preact = jnp.einsum("drh,hk->drk", aggregate, w_message, preferred_element_type=jnp.float32)
    hidden = (states_f + jax.nn.silu(preact)).astype(jnp.bfloat16)

    node_major = exchange(hidden, "day", 1, 0)
    upstream = cotangent.reshape(cotangent.shape[0], -1, width)
    attn_grads, back = attend_blocked(node_major, upstream, w_query, w_key, w_value)
    back_days = exchange(back, "day", 0, 1)

    sigmoid_val = jax.nn.sigmoid(preact)
    pre_grad = (
        back_days.astype(jnp.float32) * sigmoid_val * (1.0 + preact * (1.0 - sigmoid_val))
    ).astype(jnp.bfloat16)
    grad_message = lax.dot_general(
        aggregate.reshape(-1, width),
        pre_grad.reshape(-1, width),
        (((0,), (0,)), ((), ())),
        preferred_element_type=jnp.float32,
    )
    agg_grad = jnp.einsum("drk,hk->drh", pre_grad, w_message, preferred_element_type=jnp.float32)
    term_grad = agg_grad * inverse[:, :, None]
    high = term_grad.astype(jnp.bfloat16)
    rest = term_grad - high.astype(jnp.float32)
    middle = rest.astype(jnp.bfloat16)
    low = (rest - middle.astype(jnp.float32)).astype(jnp.bfloat16)
    ext_grad = jnp.einsum(
        "drs,drh->dsh",
        adjacent,
        jnp.concatenate([high, middle, low], axis=2),
        preferred_element_type=jnp.float32,
    )
    ext_grad = ext_grad[:, :, :width] + ext_grad[:, :, width : 2 * width] + ext_grad[:, :, 2 * width :]
    halo_grad = ext_grad[:, node_local:].astype(jnp.bfloat16)
    returned = from_behind(halo_grad, "dom", -1)
    own_grad = ext_grad[:, :node_local]
    scattered = jnp.einsum("dsn,dsh->dnh", slot_hot, returned, preferred_element_type=jnp.float32)
    state_grad = back_days.astype(jnp.float32) + term_grad + own_grad + scattered
    (grad_message, grad_query, grad_key, grad_value), state_grad = tree_sum(
        (grad_message, attn_grads[0], attn_grads[1], attn_grads[2]), ("dom", "day"), state_grad
    )
    return (state_grad, grad_message, grad_query, grad_key, grad_value)


def solution(mesh):
    return jax.shard_map(
        local,
        mesh=mesh,
        in_specs=(
            P("day", "dom", None),
            P("day", "dom"),
            P("day", "dom"),
            P("day", "dom"),
            P("day", "dom"),
            P(),
            P(),
            P(),
            P(),
            P(None, "dom", "day", None, None),
        ),
        out_specs=(P("day", "dom", None), P(), P(), P(), P()),
        check_vma=False,
    )
```

```python
import jax
import jax.numpy as jnp
from jax import lax
from jax.sharding import PartitionSpec as P

HEADS = 4


def from_behind(value, axis, steps):
    count = lax.axis_size(axis)
    pairs = [(source, (source + steps) % count) for source in range(count)]
    return lax.ppermute(value, axis, pairs)


def _power_of_two(count):
    return count > 0 and count & (count - 1) == 0


def _group_pairs(axis, stride, group, shift):
    pairs = []
    for source in range(lax.axis_size(axis)):
        digit = (source // stride) % group
        pairs.append((source, source + ((digit + shift) % group - digit) * stride))
    return pairs


def _scatter_step(flat, axis, stride, group):
    digit = (lax.axis_index(axis) // stride) % group
    chunks = flat.reshape(group, -1)
    if group == 2:
        keep = jnp.where(digit == 0, chunks[0], chunks[1])
        send = jnp.where(digit == 0, chunks[1], chunks[0])
        return keep + lax.ppermute(send, axis, _group_pairs(axis, stride, group, 1))
    total = lax.dynamic_index_in_dim(chunks, digit, 0, keepdims=False)
    for shift in range(1, group):
        send = lax.dynamic_index_in_dim(chunks, (digit + shift) % group, 0, keepdims=False)
        total = total + lax.ppermute(send, axis, _group_pairs(axis, stride, group, shift))
    return total


def _gather_step(flat, axis, stride, group):
    digit = (lax.axis_index(axis) // stride) % group
    if group == 2:
        other = lax.ppermute(flat, axis, _group_pairs(axis, stride, group, 1))
        return jnp.where(
            digit == 0, jnp.concatenate([flat, other]), jnp.concatenate([other, flat])
        )
    got = [flat] + [
        lax.ppermute(flat, axis, _group_pairs(axis, stride, group, shift)) for shift in range(1, group)
    ]
    stacked = jnp.stack(got)
    order = (digit - jnp.arange(group)) % group
    return jnp.take(stacked, order, axis=0).reshape(-1)


def _factors(size):
    if size <= 4:
        return [size]
    return [2] + _factors(size // 2)


def tree_sum(values, axes, companion=None):
    sizes = [lax.axis_size(axis) for axis in axes]
    flat = jnp.concatenate([value.reshape(-1) for value in values])
    total = 1
    for size in sizes:
        total *= size
    if not all(_power_of_two(size) for size in sizes) or flat.shape[0] % total:
        return lax.psum(tuple(values), axes), companion
    steps = []
    for axis, size in zip(axes, sizes):
        stride = 1
        for group in _factors(size):
            if group > 1:
                steps.append((axis, stride, group))
            stride *= group
    for axis, stride, group in steps:
        flat = _scatter_step(flat, axis, stride, group)
    flat, companion = lax.optimization_barrier((flat, companion))
    for axis, stride, group in reversed(steps):
        flat = _gather_step(flat, axis, stride, group)
    results, start = [], 0
    for value in values:
        results.append(flat[start : start + value.size].reshape(value.shape))
        start += value.size
    return tuple(results), companion


def exchange(value, axis, split_axis, concat_axis):
    count = lax.axis_size(axis)
    mine = lax.axis_index(axis)
    size = value.shape[split_axis] // count
    got = []
    for shift in range(count):
        send = lax.dynamic_slice_in_dim(value, ((mine + shift) % count) * size, size, axis=split_axis)
        if shift:
            send = lax.ppermute(send, axis, [(i, (i + shift) % count) for i in range(count)])
        got.append(send)
    stacked = jnp.take(jnp.stack(got), (mine - jnp.arange(count)) % count, axis=0)
    return jnp.concatenate([stacked[k] for k in range(count)], axis=concat_axis)


def adjacency(sources, targets, count_rows, total_rows):
    target_hot = (targets[:, None] == jnp.arange(count_rows, dtype=jnp.int32)[None, :]).astype(
        jnp.bfloat16
    )
    source_hot = (sources[:, None] == jnp.arange(total_rows, dtype=jnp.int32)[None, :]).astype(
        jnp.bfloat16
    )
    counts = lax.dot_general(
        target_hot, source_hot, (((0,), (0,)), ((), ())), preferred_element_type=jnp.float32
    )
    return counts.astype(jnp.bfloat16)


def gnn_forward(states, received, adjacent, w_message):
    extended = jnp.concatenate([states, received], axis=0)
    neighbours = jnp.dot(adjacent, extended, preferred_element_type=jnp.float32)
    counted = jnp.sum(adjacent.astype(jnp.float32), axis=1)
    inverse = 1.0 / (counted + 1.0)
    aggregate = ((states.astype(jnp.float32) + neighbours) * inverse[:, None]).astype(jnp.bfloat16)
    preact = jnp.dot(aggregate, w_message, preferred_element_type=jnp.float32)
    hidden = (states.astype(jnp.float32) + jax.nn.silu(preact)).astype(jnp.bfloat16)
    return (aggregate, preact, inverse, hidden)


def gnn_backward(upstream, aggregate, preact, inverse, adjacent, w_message):
    count_rows = aggregate.shape[0]
    up_float = upstream.astype(jnp.float32)
    sigmoid_val = jax.nn.sigmoid(preact)
    pre_grad = (up_float * sigmoid_val * (1.0 + preact * (1.0 - sigmoid_val))).astype(jnp.bfloat16)
    message_part = lax.dot_general(
        aggregate, pre_grad, (((0,), (0,)), ((), ())), preferred_element_type=jnp.float32
    )
    agg_grad = lax.dot_general(
        pre_grad, w_message, (((1,), (1,)), ((), ())), preferred_element_type=jnp.float32
    )
    term_grad = agg_grad * inverse[:, None]
    ext_grad = lax.dot_general(
        adjacent.astype(jnp.float32),
        term_grad,
        (((0,), (0,)), ((), ())),
        precision=lax.Precision.HIGHEST,
        preferred_element_type=jnp.float32,
    )
    local_grad = up_float + term_grad + ext_grad[:count_rows]
    halo_grad = ext_grad[count_rows:].astype(jnp.bfloat16)
    return (message_part, local_grad, halo_grad)


def attend(states, upstream, w_query, w_key, w_value):
    steps_all, nodes_here, width = states.shape
    head_dim = width // HEADS
    scale_factor = head_dim ** (-0.5)
    flat = states.reshape(steps_all * nodes_here, width)

    def project(weight):
        return jnp.dot(flat, weight, preferred_element_type=jnp.float32).astype(jnp.bfloat16)

    def splitter(matrix):
        return matrix.reshape(steps_all, nodes_here, HEADS, head_dim).astype(jnp.float32)

    queries = project(w_query)
    key_rows = project(w_key)
    value_rows = project(w_value)
    query_f = splitter(queries)
    key_f = splitter(key_rows)
    value_f = splitter(value_rows)
    scores = jnp.einsum("tnhd,snhd->nhts", query_f, key_f) * scale_factor
    causal = jnp.arange(steps_all)[:, None] >= jnp.arange(steps_all)[None, :]
    scores = jnp.where(causal, scores, -jnp.inf)
    highest = jnp.max(scores, axis=-1, keepdims=True)
    exponent = jnp.exp(scores - highest)
    probs = exponent / jnp.sum(exponent, axis=-1, keepdims=True)
    probs_low = probs.astype(jnp.bfloat16).astype(jnp.float32)
    up_heads = splitter(upstream)
    value_grad = jnp.einsum("nhts,tnhd->snhd", probs_low, up_heads).astype(jnp.bfloat16)
    prob_grad = jnp.einsum("tnhd,snhd->nhts", up_heads, value_f)
    score_grad = (
        probs * (prob_grad - jnp.sum(prob_grad * probs, axis=-1, keepdims=True)) * scale_factor
    ).astype(jnp.bfloat16)
    score_f = score_grad.astype(jnp.float32)
    query_grad = jnp.einsum("nhts,snhd->tnhd", score_f, key_f).astype(jnp.bfloat16)
    key_grad = jnp.einsum("nhts,tnhd->snhd", score_f, query_f).astype(jnp.bfloat16)
    query_flat = query_grad.reshape(steps_all * nodes_here, width)
    key_flat = key_grad.reshape(steps_all * nodes_here, width)
    value_flat = value_grad.reshape(steps_all * nodes_here, width)

    def weight_grad(grad_rows):
        return lax.dot_general(
            flat, grad_rows, (((0,), (0,)), ((), ())), preferred_element_type=jnp.float32
        )

    def input_grad(grad_rows, weight):
        return lax.dot_general(
            grad_rows, weight, (((1,), (1,)), ((), ())), preferred_element_type=jnp.float32
        )

    back = upstream.reshape(steps_all * nodes_here, width).astype(jnp.float32)
    back = (
        back
        + input_grad(query_flat, w_query)
        + input_grad(key_flat, w_key)
        + input_grad(value_flat, w_value)
    )
    back = back.astype(jnp.bfloat16).reshape(steps_all, nodes_here, width)
    return ((weight_grad(query_flat), weight_grad(key_flat), weight_grad(value_flat)), back)


def attend_blocked(states, upstream, w_query, w_key, w_value):
    steps_all, nodes_here, width = states.shape
    head_dim = width // HEADS
    scale_factor = head_dim ** (-0.5)
    per_group = max(1, 128 // steps_all)
    if nodes_here % per_group:
        per_group = 1
    groups = nodes_here // per_group
    block = per_group * steps_all
    flat = jnp.swapaxes(states, 0, 1).reshape(groups, block, width)
    up_flat = jnp.swapaxes(upstream, 0, 1).reshape(groups, block, width)
    heads_of = {
        name: weight.reshape(width, HEADS, head_dim)
        for name, weight in (("q", w_query), ("k", w_key), ("v", w_value))
    }

    def contract(spec, left, right):
        return jnp.einsum(spec, left, right, preferred_element_type=jnp.float32)

    queries = contract("gic,chd->ghid", flat, heads_of["q"]).astype(jnp.bfloat16)
    key_rows = contract("gic,chd->ghid", flat, heads_of["k"]).astype(jnp.bfloat16)
    value_rows = contract("gic,chd->ghid", flat, heads_of["v"]).astype(jnp.bfloat16)
    up_heads = up_flat.reshape(groups, block, HEADS, head_dim)
    position = jnp.arange(block)
    same = (position[:, None] // steps_all) == (position[None, :] // steps_all)
    causal = jnp.logical_and(same, (position[:, None] % steps_all) >= (position[None, :] % steps_all))

    scores = contract("ghid,ghjd->ghij", queries, key_rows) * scale_factor
    scores = jnp.where(causal, scores, -jnp.inf)
    highest = jnp.max(scores, axis=-1, keepdims=True)
    exponent = jnp.exp(scores - highest)
    probs = lax.optimization_barrier(exponent / jnp.sum(exponent, axis=-1, keepdims=True))
    probs_low = probs.astype(jnp.bfloat16)
    value_grad = contract("ghij,gihd->ghjd", probs_low, up_heads).astype(jnp.bfloat16)
    prob_grad = contract("gihd,ghjd->ghij", up_heads, value_rows)
    score_grad = (
        probs * (prob_grad - jnp.sum(prob_grad * probs, axis=-1, keepdims=True)) * scale_factor
    ).astype(jnp.bfloat16)
    score_grad = lax.optimization_barrier(score_grad)
    query_grad = contract("ghij,ghjd->ghid", score_grad, key_rows).astype(jnp.bfloat16)
    key_grad = contract("ghij,ghid->ghjd", score_grad, queries).astype(jnp.bfloat16)

    def weight_grad(grad_rows):
        return contract("gic,ghid->chd", flat, grad_rows).reshape(width, width)

    def input_grad(grad_rows, name):
        return contract("ghid,chd->gic", grad_rows, heads_of[name])

    through = input_grad(query_grad, "q") + input_grad(key_grad, "k") + input_grad(value_grad, "v")
    through = jnp.swapaxes(through.reshape(nodes_here, steps_all, width), 0, 1)
    back = (upstream.astype(jnp.float32) + through).astype(jnp.bfloat16)
    return ((weight_grad(query_grad), weight_grad(key_grad), weight_grad(value_grad)), back)


def local(
    node_states,
    edge_source,
    edge_target,
    halo_rows,
    halo_count,
    w_message,
    w_query,
    w_key,
    w_value,
    cotangent,
):
    days_local, node_local, width = node_states.shape
    halo_slots = halo_rows.shape[1]
    live = jnp.arange(halo_slots)[None, :] < halo_count
    rows = jnp.arange(node_local, dtype=jnp.int32)
    slot_hot = jnp.logical_and(
        halo_rows[:, :, None] == rows[None, None, :], live[:, :, None]
    ).astype(jnp.bfloat16)
    sent = jnp.einsum(
        "dsn,dnh->dsh", slot_hot, node_states, preferred_element_type=jnp.float32
    ).astype(jnp.bfloat16)
    received = from_behind(sent, "dom", 1)

    target_hot = (edge_target[:, :, None] == rows[None, None, :]).astype(jnp.bfloat16)
    extended_ids = jnp.arange(node_local + halo_slots, dtype=jnp.int32)
    source_hot = (edge_source[:, :, None] == extended_ids[None, None, :]).astype(jnp.bfloat16)
    adjacent = jnp.einsum(
        "der,des->drs", target_hot, source_hot, preferred_element_type=jnp.float32
    ).astype(jnp.bfloat16)
    counted = jnp.einsum(
        "der,e->dr",
        target_hot,
        jnp.ones(target_hot.shape[1], jnp.bfloat16),
        preferred_element_type=jnp.float32,
    )
    inverse = 1.0 / (counted + 1.0)

    states_f = node_states.astype(jnp.float32)
    extended = jnp.concatenate([node_states, received], axis=1)
    neighbours = jnp.einsum("drs,dsh->drh", adjacent, extended, preferred_element_type=jnp.float32)
    aggregate = ((states_f + neighbours) * inverse[:, :, None]).astype(jnp.bfloat16)
    preact = jnp.einsum("drh,hk->drk", aggregate, w_message, preferred_element_type=jnp.float32)
    hidden = (states_f + jax.nn.silu(preact)).astype(jnp.bfloat16)

    node_major = exchange(hidden, "day", 1, 0)
    upstream = cotangent.reshape(cotangent.shape[0], -1, width)
    attn_grads, back = attend_blocked(node_major, upstream, w_query, w_key, w_value)
    back_days = exchange(back, "day", 0, 1)

    sigmoid_val = jax.nn.sigmoid(preact)
    pre_grad = (
        back_days.astype(jnp.float32) * sigmoid_val * (1.0 + preact * (1.0 - sigmoid_val))
    ).astype(jnp.bfloat16)
    grad_message = lax.dot_general(
        aggregate.reshape(-1, width),
        pre_grad.reshape(-1, width),
        (((0,), (0,)), ((), ())),
        preferred_element_type=jnp.float32,
    )
    agg_grad = jnp.einsum("drk,hk->drh", pre_grad, w_message, preferred_element_type=jnp.float32)
    term_grad = agg_grad * inverse[:, :, None]
    ext_grad = jnp.einsum(
        "drs,drh->dsh",
        adjacent.astype(jnp.float32),
        term_grad,
        precision=lax.Precision.HIGHEST,
        preferred_element_type=jnp.float32,
    )
    halo_grad = ext_grad[:, node_local:].astype(jnp.bfloat16)
    returned = from_behind(halo_grad, "dom", -1)
    own_grad = ext_grad[:, :node_local]
    scattered = jnp.einsum("dsn,dsh->dnh", slot_hot, returned, preferred_element_type=jnp.float32)
    state_grad = back_days.astype(jnp.float32) + term_grad + own_grad + scattered
    (grad_message, grad_query, grad_key, grad_value), state_grad = tree_sum(
        (grad_message, attn_grads[0], attn_grads[1], attn_grads[2]), ("dom", "day"), state_grad
    )
    return (state_grad, grad_message, grad_query, grad_key, grad_value)


def solution(mesh):
    return jax.shard_map(
        local,
        mesh=mesh,
        in_specs=(
            P("day", "dom", None),
            P("day", "dom"),
            P("day", "dom"),
            P("day", "dom"),
            P("day", "dom"),
            P(),
            P(),
            P(),
            P(),
            P(None, "dom", "day", None, None),
        ),
        out_specs=(P("day", "dom", None), P(), P(), P(), P()),
        check_vma=False,
    )
```

```python
import jax
import jax.numpy as jnp
from jax import lax
from jax.sharding import PartitionSpec as P

HEADS = 4


def from_behind(value, axis, steps):
    count = lax.axis_size(axis)
    pairs = [(source, (source + steps) % count) for source in range(count)]
    return lax.ppermute(value, axis, pairs)


def _power_of_two(count):
    return count > 0 and count & (count - 1) == 0


def _group_pairs(axis, stride, group, shift):
    pairs = []
    for source in range(lax.axis_size(axis)):
        digit = (source // stride) % group
        pairs.append((source, source + ((digit + shift) % group - digit) * stride))
    return pairs


def _scatter_step(flat, axis, stride, group):
    digit = (lax.axis_index(axis) // stride) % group
    chunks = flat.reshape(group, -1)
    if group == 2:
        keep = jnp.where(digit == 0, chunks[0], chunks[1])
        send = jnp.where(digit == 0, chunks[1], chunks[0])
        return keep + lax.ppermute(send, axis, _group_pairs(axis, stride, group, 1))
    total = lax.dynamic_index_in_dim(chunks, digit, 0, keepdims=False)
    for shift in range(1, group):
        send = lax.dynamic_index_in_dim(chunks, (digit + shift) % group, 0, keepdims=False)
        total = total + lax.ppermute(send, axis, _group_pairs(axis, stride, group, shift))
    return total


def _gather_step(flat, axis, stride, group):
    digit = (lax.axis_index(axis) // stride) % group
    if group == 2:
        other = lax.ppermute(flat, axis, _group_pairs(axis, stride, group, 1))
        return jnp.where(
            digit == 0, jnp.concatenate([flat, other]), jnp.concatenate([other, flat])
        )
    got = [flat] + [
        lax.ppermute(flat, axis, _group_pairs(axis, stride, group, shift)) for shift in range(1, group)
    ]
    stacked = jnp.stack(got)
    order = (digit - jnp.arange(group)) % group
    return jnp.take(stacked, order, axis=0).reshape(-1)


def _factors(size):
    if size <= 4:
        return [size]
    return [2] + _factors(size // 2)


def tree_sum(values, axes, companion=None):
    sizes = [lax.axis_size(axis) for axis in axes]
    flat = jnp.concatenate([value.reshape(-1) for value in values])
    total = 1
    for size in sizes:
        total *= size
    if not all(_power_of_two(size) for size in sizes) or flat.shape[0] % total:
        return lax.psum(tuple(values), axes), companion
    steps = []
    for axis, size in zip(axes, sizes):
        stride = 1
        for group in _factors(size):
            if group > 1:
                steps.append((axis, stride, group))
            stride *= group
    for axis, stride, group in steps:
        flat = _scatter_step(flat, axis, stride, group)
    flat, companion = lax.optimization_barrier((flat, companion))
    for axis, stride, group in reversed(steps):
        flat = _gather_step(flat, axis, stride, group)
    results, start = [], 0
    for value in values:
        results.append(flat[start : start + value.size].reshape(value.shape))
        start += value.size
    return tuple(results), companion


def exchange(value, axis, split_axis, concat_axis):
    count = lax.axis_size(axis)
    mine = lax.axis_index(axis)
    size = value.shape[split_axis] // count
    got = []
    for shift in range(count):
        send = lax.dynamic_slice_in_dim(value, ((mine + shift) % count) * size, size, axis=split_axis)
        if shift:
            send = lax.ppermute(send, axis, [(i, (i + shift) % count) for i in range(count)])
        got.append(send)
    stacked = jnp.take(jnp.stack(got), (mine - jnp.arange(count)) % count, axis=0)
    return jnp.concatenate([stacked[k] for k in range(count)], axis=concat_axis)


def adjacency(sources, targets, count_rows, total_rows):
    target_hot = (targets[:, None] == jnp.arange(count_rows, dtype=jnp.int32)[None, :]).astype(
        jnp.bfloat16
    )
    source_hot = (sources[:, None] == jnp.arange(total_rows, dtype=jnp.int32)[None, :]).astype(
        jnp.bfloat16
    )
    counts = lax.dot_general(
        target_hot, source_hot, (((0,), (0,)), ((), ())), preferred_element_type=jnp.float32
    )
    return counts.astype(jnp.bfloat16)


def gnn_forward(states, received, adjacent, w_message):
    extended = jnp.concatenate([states, received], axis=0)
    neighbours = jnp.dot(adjacent, extended, preferred_element_type=jnp.float32)
    counted = jnp.sum(adjacent.astype(jnp.float32), axis=1)
    inverse = 1.0 / (counted + 1.0)
    aggregate = ((states.astype(jnp.float32) + neighbours) * inverse[:, None]).astype(jnp.bfloat16)
    preact = jnp.dot(aggregate, w_message, preferred_element_type=jnp.float32)
    hidden = (states.astype(jnp.float32) + jax.nn.silu(preact)).astype(jnp.bfloat16)
    return (aggregate, preact, inverse, hidden)


def gnn_backward(upstream, aggregate, preact, inverse, adjacent, w_message):
    count_rows = aggregate.shape[0]
    up_float = upstream.astype(jnp.float32)
    sigmoid_val = jax.nn.sigmoid(preact)
    pre_grad = (up_float * sigmoid_val * (1.0 + preact * (1.0 - sigmoid_val))).astype(jnp.bfloat16)
    message_part = lax.dot_general(
        aggregate, pre_grad, (((0,), (0,)), ((), ())), preferred_element_type=jnp.float32
    )
    agg_grad = lax.dot_general(
        pre_grad, w_message, (((1,), (1,)), ((), ())), preferred_element_type=jnp.float32
    )
    term_grad = agg_grad * inverse[:, None]
    ext_grad = lax.dot_general(
        adjacent.astype(jnp.float32),
        term_grad,
        (((0,), (0,)), ((), ())),
        precision=lax.Precision.HIGHEST,
        preferred_element_type=jnp.float32,
    )
    local_grad = up_float + term_grad + ext_grad[:count_rows]
    halo_grad = ext_grad[count_rows:].astype(jnp.bfloat16)
    return (message_part, local_grad, halo_grad)


def attend(states, upstream, w_query, w_key, w_value):
    steps_all, nodes_here, width = states.shape
    head_dim = width // HEADS
    scale_factor = head_dim ** (-0.5)
    flat = states.reshape(steps_all * nodes_here, width)

    def project(weight):
        return jnp.dot(flat, weight, preferred_element_type=jnp.float32).astype(jnp.bfloat16)

    def splitter(matrix):
        return matrix.reshape(steps_all, nodes_here, HEADS, head_dim).astype(jnp.float32)

    queries = project(w_query)
    key_rows = project(w_key)
    value_rows = project(w_value)
    query_f = splitter(queries)
    key_f = splitter(key_rows)
    value_f = splitter(value_rows)
    scores = jnp.einsum("tnhd,snhd->nhts", query_f, key_f) * scale_factor
    causal = jnp.arange(steps_all)[:, None] >= jnp.arange(steps_all)[None, :]
    scores = jnp.where(causal, scores, -jnp.inf)
    highest = jnp.max(scores, axis=-1, keepdims=True)
    exponent = jnp.exp(scores - highest)
    probs = exponent / jnp.sum(exponent, axis=-1, keepdims=True)
    probs_low = probs.astype(jnp.bfloat16).astype(jnp.float32)
    up_heads = splitter(upstream)
    value_grad = jnp.einsum("nhts,tnhd->snhd", probs_low, up_heads).astype(jnp.bfloat16)
    prob_grad = jnp.einsum("tnhd,snhd->nhts", up_heads, value_f)
    score_grad = (
        probs * (prob_grad - jnp.sum(prob_grad * probs, axis=-1, keepdims=True)) * scale_factor
    ).astype(jnp.bfloat16)
    score_f = score_grad.astype(jnp.float32)
    query_grad = jnp.einsum("nhts,snhd->tnhd", score_f, key_f).astype(jnp.bfloat16)
    key_grad = jnp.einsum("nhts,tnhd->snhd", score_f, query_f).astype(jnp.bfloat16)
    query_flat = query_grad.reshape(steps_all * nodes_here, width)
    key_flat = key_grad.reshape(steps_all * nodes_here, width)
    value_flat = value_grad.reshape(steps_all * nodes_here, width)

    def weight_grad(grad_rows):
        return lax.dot_general(
            flat, grad_rows, (((0,), (0,)), ((), ())), preferred_element_type=jnp.float32
        )

    def input_grad(grad_rows, weight):
        return lax.dot_general(
            grad_rows, weight, (((1,), (1,)), ((), ())), preferred_element_type=jnp.float32
        )

    back = upstream.reshape(steps_all * nodes_here, width).astype(jnp.float32)
    back = (
        back
        + input_grad(query_flat, w_query)
        + input_grad(key_flat, w_key)
        + input_grad(value_flat, w_value)
    )
    back = back.astype(jnp.bfloat16).reshape(steps_all, nodes_here, width)
    return ((weight_grad(query_flat), weight_grad(key_flat), weight_grad(value_flat)), back)


def attend_blocked(states, upstream, w_query, w_key, w_value):
    steps_all, nodes_here, width = states.shape
    head_dim = width // HEADS
    scale_factor = head_dim ** (-0.5)
    per_group = max(1, 128 // steps_all)
    if nodes_here % per_group:
        per_group = 1
    groups = nodes_here // per_group
    block = per_group * steps_all
    flat = jnp.swapaxes(states, 0, 1).reshape(groups, block, width)
    up_flat = jnp.swapaxes(upstream, 0, 1).reshape(groups, block, width)
    heads_of = {
        name: weight.reshape(width, HEADS, head_dim)
        for name, weight in (("q", w_query), ("k", w_key), ("v", w_value))
    }

    def contract(spec, left, right):
        return jnp.einsum(spec, left, right, preferred_element_type=jnp.float32)

    queries = contract("gic,chd->ghid", flat, heads_of["q"]).astype(jnp.bfloat16)
    key_rows = contract("gic,chd->ghid", flat, heads_of["k"]).astype(jnp.bfloat16)
    value_rows = contract("gic,chd->ghid", flat, heads_of["v"]).astype(jnp.bfloat16)
    up_heads = up_flat.reshape(groups, block, HEADS, head_dim)
    position = jnp.arange(block)
    same = (position[:, None] // steps_all) == (position[None, :] // steps_all)
    causal = jnp.logical_and(same, (position[:, None] % steps_all) >= (position[None, :] % steps_all))

    scores = contract("ghid,ghjd->ghij", queries, key_rows) * scale_factor
    scores = jnp.where(causal, scores, -jnp.inf)
    highest = jnp.max(scores, axis=-1, keepdims=True)
    exponent = jnp.exp(scores - highest)
    probs = exponent / jnp.sum(exponent, axis=-1, keepdims=True)
    probs_low = probs.astype(jnp.bfloat16)
    value_grad = contract("ghij,gihd->ghjd", probs_low, up_heads).astype(jnp.bfloat16)
    prob_grad = contract("gihd,ghjd->ghij", up_heads, value_rows)
    score_grad = (
        probs * (prob_grad - jnp.sum(prob_grad * probs, axis=-1, keepdims=True)) * scale_factor
    ).astype(jnp.bfloat16)
    query_grad = contract("ghij,ghjd->ghid", score_grad, key_rows).astype(jnp.bfloat16)
    key_grad = contract("ghij,ghid->ghjd", score_grad, queries).astype(jnp.bfloat16)

    def weight_grad(grad_rows):
        return contract("gic,ghid->chd", flat, grad_rows).reshape(width, width)

    def input_grad(grad_rows, name):
        return contract("ghid,chd->gic", grad_rows, heads_of[name])

    through = input_grad(query_grad, "q") + input_grad(key_grad, "k") + input_grad(value_grad, "v")
    through = jnp.swapaxes(through.reshape(nodes_here, steps_all, width), 0, 1)
    back = (upstream.astype(jnp.float32) + through).astype(jnp.bfloat16)
    return ((weight_grad(query_grad), weight_grad(key_grad), weight_grad(value_grad)), back)


def local(
    node_states,
    edge_source,
    edge_target,
    halo_rows,
    halo_count,
    w_message,
    w_query,
    w_key,
    w_value,
    cotangent,
):
    days_local, node_local, width = node_states.shape
    halo_slots = halo_rows.shape[1]
    live = jnp.arange(halo_slots)[None, :] < halo_count
    rows = jnp.arange(node_local, dtype=jnp.int32)
    slot_hot = jnp.logical_and(
        halo_rows[:, :, None] == rows[None, None, :], live[:, :, None]
    ).astype(jnp.bfloat16)
    sent = jnp.einsum(
        "dsn,dnh->dsh", slot_hot, node_states, preferred_element_type=jnp.float32
    ).astype(jnp.bfloat16)
    received = from_behind(sent, "dom", 1)

    target_hot = (edge_target[:, :, None] == rows[None, None, :]).astype(jnp.bfloat16)
    extended_ids = jnp.arange(node_local + halo_slots, dtype=jnp.int32)
    source_hot = (edge_source[:, :, None] == extended_ids[None, None, :]).astype(jnp.bfloat16)
    adjacent = jnp.einsum(
        "der,des->drs", target_hot, source_hot, preferred_element_type=jnp.float32
    ).astype(jnp.bfloat16)
    counted = jnp.einsum(
        "der,e->dr",
        target_hot,
        jnp.ones(target_hot.shape[1], jnp.bfloat16),
        preferred_element_type=jnp.float32,
    )
    inverse = 1.0 / (counted + 1.0)

    states_f = node_states.astype(jnp.float32)
    extended = jnp.concatenate([node_states, received], axis=1)
    neighbours = jnp.einsum("drs,dsh->drh", adjacent, extended, preferred_element_type=jnp.float32)
    aggregate = ((states_f + neighbours) * inverse[:, :, None]).astype(jnp.bfloat16)
    preact = jnp.einsum("drh,hk->drk", aggregate, w_message, preferred_element_type=jnp.float32)
    hidden = (states_f + jax.nn.silu(preact)).astype(jnp.bfloat16)

    node_major = exchange(hidden, "day", 1, 0)
    upstream = cotangent.reshape(cotangent.shape[0], -1, width)
    attn_grads, back = attend_blocked(node_major, upstream, w_query, w_key, w_value)
    back_days = exchange(back, "day", 0, 1)

    sigmoid_val = jax.nn.sigmoid(preact)
    pre_grad = (
        back_days.astype(jnp.float32) * sigmoid_val * (1.0 + preact * (1.0 - sigmoid_val))
    ).astype(jnp.bfloat16)
    grad_message = lax.dot_general(
        aggregate.reshape(-1, width),
        pre_grad.reshape(-1, width),
        (((0,), (0,)), ((), ())),
        preferred_element_type=jnp.float32,
    )
    agg_grad = jnp.einsum("drk,hk->drh", pre_grad, w_message, preferred_element_type=jnp.float32)
    term_grad = agg_grad * inverse[:, :, None]
    ext_grad = jnp.einsum(
        "drs,drh->dsh",
        adjacent.astype(jnp.float32),
        term_grad,
        precision=lax.Precision.HIGHEST,
        preferred_element_type=jnp.float32,
    )
    halo_grad = ext_grad[:, node_local:].astype(jnp.bfloat16)
    returned = from_behind(halo_grad, "dom", -1)
    own_grad = ext_grad[:, :node_local]
    scattered = jnp.einsum("dsn,dsh->dnh", slot_hot, returned, preferred_element_type=jnp.float32)
    state_grad = back_days.astype(jnp.float32) + term_grad + own_grad + scattered
    (grad_message, grad_query, grad_key, grad_value), state_grad = tree_sum(
        (grad_message, attn_grads[0], attn_grads[1], attn_grads[2]), ("dom", "day"), state_grad
    )
    return (state_grad, grad_message, grad_query, grad_key, grad_value)


def solution(mesh):
    return jax.shard_map(
        local,
        mesh=mesh,
        in_specs=(
            P("day", "dom", None),
            P("day", "dom"),
            P("day", "dom"),
            P("day", "dom"),
            P("day", "dom"),
            P(),
            P(),
            P(),
            P(),
            P(None, "dom", "day", None, None),
        ),
        out_specs=(P("day", "dom", None), P(), P(), P(), P()),
        check_vma=False,
    )
```
